32 devices in a mesh: groups: 2 (over y), ctx: 4 (over z), fsdp: 2 (over x), sub: 2 (over core).
Axes of the slice: x: 2, y: 2, z: 4, core: 2. Of those that a mesh axis runs over, the one named last changes fastest.
Arguments:
- layer_input: bfloat16 [4, 2048, 2304], P(('groups', 'fsdp'), ('ctx', 'sub')), parts along dimension 0, may hold values from -6 to 6
- query_heads: bfloat16 [4, 2048, 1024], P(('groups', 'fsdp'), ('ctx', 'sub')), parts along dimension 0, may hold values from -11 to 11
- key_heads: bfloat16 [4, 2048, 512], P(('groups', 'fsdp'), ('ctx', 'sub')), parts along dimension 0, may hold values from -11 to 11
- value_heads: bfloat16 [4, 2048, 512], P(('groups', 'fsdp'), ('ctx', 'sub')), parts along dimension 0, may hold values from -6 to 6
- grad_out: bfloat16 [4, 2048, 1024], P(('groups', 'fsdp'), ('ctx', 'sub')), parts along dimension 0, may hold values from -96 to 96
- doc_starts: int32 [4, 12], P(('groups', 'fsdp')), parts along dimension 0, may hold values from 0 to 2047, as said below
Outputs:
- grad_query: bfloat16 [4, 2048, 1024], P(('groups', 'fsdp'), ('ctx', 'sub')), parts along dimension 0
- grad_key: bfloat16 [4, 2048, 512], P(('groups', 'fsdp'), ('ctx', 'sub')), parts along dimension 0
- grad_value: bfloat16 [4, 2048, 512], P(('groups', 'fsdp'), ('ctx', 'sub')), parts along dimension 0
- grad_value_proj: float32 [4608, 512], P(('groups', 'fsdp')), parts along dimension 0
The draws below stay inside these ranges and needn't reach their ends.
There are 2 independent parts, one for each index of `groups`. The reference program is written for one: setup_inputs(seed, part) draws one part's arguments, and reference() takes and returns one part's arrays. A program takes and returns all parts, laid end to end along the dimension named above; each array names one. Nothing has to cross between parts.
Inputs may be any that keep to these rules, and one draw needn't show every extreme that they name: `doc_starts`: each row holds the first positions of the 12 documents of one sequence in increasing order; the first is 0, every document has at least one token, and the longest has exactly 1024 tokens.
All inputs are finite; a program needn't handle non-finite values.
Results may differ from the reference program's by a relative error of at most 0.015.
Values may be sent and summed in bfloat16 or wider, within the bound.
No kernel may reach another device: no remote copies, remote signals or barrier semaphores. Data moves between devices by JAX's collectives and lax.ppermute only.
A program may use at most 64 MiB of HBM per device.

```python
import jax
import jax.numpy as jnp
from jax import lax

D = 2304
HEADS = 4
KV_HEADS = 2
HEAD_DIM = 256
TOK_DEV = 256
DOCS = 12
SEQS = 2
LENGTH = 2048
WINDOW = 768
MOST = 1024


def draw_query_heads(key, part):
    random_part = jnp.clip(jax.random.normal(jax.random.fold_in(key, 11), (SEQS, LENGTH, HEADS * HEAD_DIM), jnp.float32), -6.0, 6.0)
    return random_part.astype(jnp.bfloat16)


def draw_key_heads(key, part):
    random_part = jnp.clip(jax.random.normal(jax.random.fold_in(key, 13), (SEQS, LENGTH, KV_HEADS * HEAD_DIM), jnp.float32), -6.0, 6.0)
    return random_part.astype(jnp.bfloat16)


def draw_doc_starts(key, part):

    def one_row(row_key):
        weights = jax.random.randint(jax.random.fold_in(row_key, 1), (DOCS - 1,), 1, 3)
        spread = LENGTH - MOST - (DOCS - 1)
        shares = spread * weights // jnp.sum(weights)
        leftover = spread - jnp.sum(shares)
        others = 1 + shares + (jnp.arange(DOCS - 1) < leftover).astype(jnp.int32)
        place = jax.random.randint(jax.random.fold_in(row_key, 2), (), 0, DOCS)
        slot_ids = jnp.arange(DOCS)
        below = others[jnp.clip(slot_ids, 0, DOCS - 2)]
        above = others[jnp.clip(slot_ids - 1, 0, DOCS - 2)]
        lengths = jnp.where(slot_ids < place, below, jnp.where(slot_ids == place, MOST, above))
        return (jnp.cumsum(lengths) - lengths).astype(jnp.int32)
    return jax.vmap(one_row)(jax.random.split(key, SEQS)).astype(jnp.int32)


def spiked(entries, key, source, target, shards_of, factor):
    def block_of(axis_at):
        return (jnp.arange(entries.shape[axis_at]) // (entries.shape[axis_at] // shards_of)).reshape((-1,) + (1,) * (entries.ndim - 1 - axis_at))

    one_side = jax.random.permutation(key, shards_of)[block_of(target)]
    other_side = (block_of(target) + shards_of // 2) % shards_of
    return jnp.where((block_of(source) == one_side) | (block_of(source) == other_side), factor * entries, entries)


def block_levels(rng, extent, cuts, low, top_value):
    level = 1.0
    for axis_at, parts in cuts:
        heights = jax.random.uniform(jax.random.fold_in(jax.random.fold_in(rng, 6), axis_at), (parts,), jnp.float32, low / len(cuts), top_value / len(cuts))
        level = level * jnp.repeat(jnp.exp(heights), extent[axis_at] // parts).reshape((-1,) + (1,) * (len(extent) - 1 - axis_at))
    return level


def centred(key, dims, width, most, shards=(), held_as=jnp.bfloat16):
    values = jax.random.normal(key, dims, jnp.float32) * width
    if len(shards) > 0:
        values = block_levels(key, dims, shards, -0.22, 0.18) * values
    return jnp.clip(values, min=-most, max=most).astype(held_as)


def noise_with(stream_key, shape, deviation, reach, cuts, heavy, kind=jnp.bfloat16):
    result = deviation * jax.random.normal(stream_key, shape, jnp.float32)
    if cuts:
        result = result * block_levels(stream_key, shape, cuts, -0.22, 0.18)
    return jnp.clip(spiked(result, jax.random.fold_in(stream_key, 3), *heavy), -reach, reach).astype(kind)


def setup_inputs(seed: int = 0, part: int = 0) -> dict:
    seeds = jax.random.split(jax.random.key(seed), 7)
    part_keys = jax.random.split(jax.random.fold_in(seeds[6], part), 7)
    return {
        "layer_input": noise_with(part_keys[0], (SEQS, LENGTH, D), 1.0, 6.0, ((0, 2), (1, 8)), (1, 2, 8, 2.0)),
        "query_heads": draw_query_heads(jax.random.fold_in(jax.random.fold_in(seeds[6], part), 71), part),
        "key_heads": draw_key_heads(jax.random.fold_in(jax.random.fold_in(seeds[6], part), 71), part),
        "value_heads": centred(part_keys[3], (SEQS, LENGTH, KV_HEADS * HEAD_DIM), 1.0, 6.0, ((0, 2), (1, 8))),
        "grad_out": centred(part_keys[4], (SEQS, LENGTH, HEADS * HEAD_DIM), 16.0, 96.0, ((0, 2), (1, 8))),
        "doc_starts": draw_doc_starts(jax.random.fold_in(jax.random.fold_in(seeds[6], part), 71), part),
    }


def doc_start_of(starts, positions):
    covered = starts[None, :] <= positions[:, None]
    return jnp.max(jnp.where(covered, starts[None, :], 0), axis=1).astype(jnp.int32)


def attend_block(queries, key_block, value_block, grads, query_pos, key_pos, lowest):
    row_count = queries.shape[0]
    key_count = key_block.shape[0]
    groups = key_block.shape[1] // HEAD_DIM
    per_group = queries.shape[1] // key_block.shape[1]
    inv_root = HEAD_DIM ** -0.5
    query_four = queries.astype(jnp.float32).reshape(row_count, groups, per_group, HEAD_DIM)
    grad_four = grads.astype(jnp.float32).reshape(row_count, groups, per_group, HEAD_DIM)
    key_three = key_block.astype(jnp.float32).reshape(key_count, groups, HEAD_DIM)
    value_three = value_block.astype(jnp.float32).reshape(key_count, groups, HEAD_DIM)
    allowed = (key_pos[None, :] >= lowest[:, None]) & (key_pos[None, :] <= query_pos[:, None])

    def one_group(group):
        query_g = lax.dynamic_index_in_dim(query_four, group, 1, keepdims=False)
        grad_g = lax.dynamic_index_in_dim(grad_four, group, 1, keepdims=False)
        key_g = lax.dynamic_index_in_dim(key_three, group, 1, keepdims=False)
        value_g = lax.dynamic_index_in_dim(value_three, group, 1, keepdims=False)
        scores = jnp.einsum("thd,kd->htk", query_g, key_g) * inv_root
        scores = jnp.where(allowed[None], scores, -1e30)
        largest = jnp.max(scores, axis=2, keepdims=True)
        raised = jnp.where(allowed[None], jnp.exp(scores - largest), 0.0)
        attn_probs = raised / jnp.sum(raised, axis=2, keepdims=True)
        grad_probs = jnp.einsum("thd,kd->htk", grad_g, value_g)
        row_dot = jnp.sum(attn_probs * grad_probs, axis=2, keepdims=True)
        scores_low = (attn_probs * (grad_probs - row_dot) * inv_root).astype(jnp.bfloat16)
        grad_scores = lax.optimization_barrier(scores_low).astype(jnp.float32)
        probs_low = lax.optimization_barrier(attn_probs.astype(jnp.bfloat16)).astype(jnp.float32)
        grad_q = jnp.einsum("htk,kd->thd", grad_scores, key_g)
        grad_k = jnp.einsum("htk,thd->kd", grad_scores, query_g)
        grad_v = jnp.einsum("htk,thd->kd", probs_low, grad_g)
        return grad_q, grad_k, grad_v

    grad_q, grad_k, grad_v = lax.map(one_group, jnp.arange(groups, dtype=jnp.int32))
    grad_q = jnp.moveaxis(grad_q, 0, 1).reshape(row_count, -1)
    grad_k = jnp.moveaxis(grad_k, 0, 1).reshape(key_count, -1)
    grad_v = jnp.moveaxis(grad_v, 0, 1).reshape(key_count, -1)
    return grad_q, grad_k, grad_v


def reference(layer_input, query_heads, key_heads, value_heads, grad_out, doc_starts):
    block_rows = TOK_DEV
    reach_blocks = (WINDOW + block_rows - 2) // block_rows
    margin_rows = reach_blocks * block_rows
    key_count = margin_rows + block_rows
    block_total = LENGTH // block_rows
    positions = jnp.arange(LENGTH, dtype=jnp.int32)
    kv_width = key_heads.shape[2]

    def one_sequence(operands):
        inputs_s, queries_s, keys_s, values_s, grads_s, starts_s = operands
        lowest_all = jnp.maximum(doc_start_of(starts_s, positions), positions - WINDOW + 1)
        zero_rows = jnp.zeros((margin_rows, kv_width), keys_s.dtype)
        padded_keys = jnp.concatenate([zero_rows, keys_s], axis=0)
        padded_values = jnp.concatenate([zero_rows, values_s], axis=0)

        def block_step(running, block_id):
            acc_k, acc_v = running
            row_start = (block_id * block_rows).astype(jnp.int32)
            query_b = lax.dynamic_slice_in_dim(queries_s, row_start, block_rows, 0)
            grad_b = lax.dynamic_slice_in_dim(grads_s, row_start, block_rows, 0)
            lowest_b = lax.dynamic_slice_in_dim(lowest_all, row_start, block_rows, 0)
            key_b = lax.dynamic_slice_in_dim(padded_keys, row_start, key_count, 0)
            value_b = lax.dynamic_slice_in_dim(padded_values, row_start, key_count, 0)
            query_pos = row_start + jnp.arange(block_rows, dtype=jnp.int32)
            key_pos = row_start - margin_rows + jnp.arange(key_count, dtype=jnp.int32)
            grad_q, grad_k, grad_v = attend_block(query_b, key_b, value_b, grad_b, query_pos, key_pos, lowest_b)
            acc_k = lax.dynamic_update_slice_in_dim(acc_k, lax.dynamic_slice_in_dim(acc_k, row_start, key_count, 0) + grad_k, row_start, 0)
            acc_v = lax.dynamic_update_slice_in_dim(acc_v, lax.dynamic_slice_in_dim(acc_v, row_start, key_count, 0) + grad_v, row_start, 0)
            return (acc_k, acc_v), grad_q.astype(jnp.bfloat16)

        start_acc = jnp.zeros((margin_rows + LENGTH, kv_width), jnp.float32)
        sums_kv, grad_q = lax.scan(block_step, (start_acc, start_acc), jnp.arange(block_total, dtype=jnp.int32))
        grad_k = sums_kv[0][margin_rows:].astype(jnp.bfloat16)
        grad_v = sums_kv[1][margin_rows:].astype(jnp.bfloat16)

        def weight_step(running, pieces):
            input_b, value_b = pieces
            term_v = jnp.dot(input_b.T, value_b, preferred_element_type=jnp.float32).astype(jnp.bfloat16)
            term_v = lax.optimization_barrier(term_v).astype(jnp.float32)
            return running + term_v, None

        zero_weight = jnp.zeros((D, kv_width), jnp.float32)
        weight_sum, unused = lax.scan(weight_step, zero_weight, (inputs_s.reshape(block_total, block_rows, D), grad_v.reshape(block_total, block_rows, kv_width)))
        return grad_q.reshape(LENGTH, -1), grad_k, grad_v, weight_sum

    results = lax.map(one_sequence, (layer_input, query_heads, key_heads, value_heads, grad_out, doc_starts))
    token_scale = float(SEQS * LENGTH) ** -0.5
    grad_value_proj = jnp.sum(results[3], axis=0) * token_scale
    return results[0], results[1], results[2], grad_value_proj
```

```python
import functools

import jax
import jax.numpy as jnp
from jax import lax
from jax.experimental import pallas as pl
from jax.experimental.pallas import tpu as pltpu
from jax.sharding import PartitionSpec as P

HEAD_DIM = 256
SPAN = 768
RING = ("ctx", "sub")
NT = (((1,), (1,)), ((), ()))
TN = (((0,), (0,)), ((), ()))


def passed_along(value, axis, steps):
    count = lax.axis_size(axis)
    first, last = (max(0, -steps), min(count, count - steps))
    return lax.ppermute(value, axis, [(source, source + steps) for source in range(first, last)])


def rotated(value, axis, steps):
    count = lax.axis_size(axis)
    return lax.ppermute(value, axis, [(source, (source + steps) % count) for source in range(count)])


def doc_start_of(starts, positions):
    covered = starts[None, :] <= positions[:, None]
    return jnp.max(jnp.where(covered, starts[None, :], 0), axis=1)


def attention_kernel(lo_ref, q_ref, do_ref, kv_ref, dq_ref, dkv_ref, *, heads, kv_heads, margin):
    rows = q_ref.shape[0]
    keys = kv_ref.shape[0]
    scale = HEAD_DIM ** (-0.5)
    kv_width = kv_heads * HEAD_DIM
    per_group = heads // kv_heads
    col = lax.broadcasted_iota(jnp.int32, (rows, keys), 1)
    row = lax.broadcasted_iota(jnp.int32, (rows, keys), 0)
    allowed = (col >= lo_ref[...]) & (col <= row + margin)
    for group in range(kv_heads):
        k_cols = pl.ds(group * HEAD_DIM, HEAD_DIM)
        v_cols = pl.ds(kv_width + group * HEAD_DIM, HEAD_DIM)
        key_g = kv_ref[:, k_cols]
        value_g = kv_ref[:, v_cols]
        grad_k = None
        grad_v = None
        for member in range(per_group):
            q_cols = pl.ds((group * per_group + member) * HEAD_DIM, HEAD_DIM)
            query_h = q_ref[:, q_cols]
            grad_h = do_ref[:, q_cols]
            scores = lax.dot_general(query_h, key_g, NT, preferred_element_type=jnp.float32) * scale
            scores = jnp.where(allowed, scores, -1e30)
            largest = jnp.max(scores, axis=1, keepdims=True)
            raised = jnp.where(allowed, jnp.exp(scores - largest), 0.0)
            probs = raised / jnp.sum(raised, axis=1, keepdims=True)
            grad_probs = lax.dot_general(grad_h, value_g, NT, preferred_element_type=jnp.float32)
            row_dot = jnp.sum(probs * grad_probs, axis=1, keepdims=True)
            grad_scores = (probs * (grad_probs - row_dot) * scale).astype(jnp.bfloat16)
            probs_low = probs.astype(jnp.bfloat16)
            dq_ref[:, q_cols] = jnp.dot(
                grad_scores, key_g, preferred_element_type=jnp.float32
            ).astype(dq_ref.dtype)
            term_k = lax.dot_general(grad_scores, query_h, TN, preferred_element_type=jnp.float32)
            term_v = lax.dot_general(probs_low, grad_h, TN, preferred_element_type=jnp.float32)
            grad_k = term_k if grad_k is None else grad_k + term_k
            grad_v = term_v if grad_v is None else grad_v + term_v
        dkv_ref[:, k_cols] = grad_k
        dkv_ref[:, v_cols] = grad_v


def attention(lo_rel, queries, grads, kv_span, heads, kv_heads, margin):
    rows, width = queries.shape
    keys, kv_cols = kv_span.shape
    kernel = functools.partial(
        attention_kernel, heads=heads, kv_heads=kv_heads, margin=margin
    )
    vmem = pl.BlockSpec(memory_space=pltpu.VMEM)
    flops = 2 * 5 * heads * rows * keys * HEAD_DIM
    moved = 2 * (2 * rows * width + keys * kv_cols + rows * width) + 4 * keys * kv_cols
    return pl.pallas_call(
        kernel,
        out_shape=(
            jax.ShapeDtypeStruct((rows, width), jnp.bfloat16),
            jax.ShapeDtypeStruct((keys, kv_cols), jnp.float32),
        ),
        in_specs=[vmem] * 4,
        out_specs=(vmem, vmem),
        cost_estimate=pl.CostEstimate(
            flops=flops, transcendentals=heads * rows * keys, bytes_accessed=moved
        ),
    )(lo_rel, queries, grads, kv_span)


def body(layer_input, query_heads, key_heads, value_heads, grad_out, doc_starts):
    block_rows = query_heads.shape[1]
    window = min(SPAN, lax.axis_size(RING) * block_rows // 2)
    reach = (window + block_rows - 2) // block_rows
    margin = reach * block_rows
    kv_width = key_heads.shape[2]
    heads = query_heads.shape[2] // HEAD_DIM
    kv_heads = kv_width // HEAD_DIM
    first_row = lax.axis_index(RING) * block_rows

    own_kv = jnp.concatenate([key_heads[0], value_heads[0]], axis=1)
    arrived = []
    moving = own_kv
    for _ in range(reach):
        moving = passed_along(moving, RING, 1)
        arrived.append(moving)
    kv_span = jnp.concatenate(arrived[::-1] + [own_kv], axis=0)
    query_pos = first_row + jnp.arange(block_rows, dtype=jnp.int32)
    lowest = jnp.maximum(doc_start_of(doc_starts[0], query_pos), query_pos - window + 1)
    lo_rel = (lowest - first_row + margin).astype(jnp.int32)[:, None]
    grad_q, grad_kv_span = attention(
        lo_rel, query_heads[0], grad_out[0], kv_span, heads, kv_heads, margin
    )

    def own_piece(distance):
        begin = (reach - distance) * block_rows
        return grad_kv_span[begin : begin + block_rows]

    total = own_piece(reach)
    for distance in range(reach - 1, -1, -1):
        moved = passed_along(total.astype(jnp.bfloat16), RING, -1).astype(jnp.float32)
        total = moved + own_piece(distance)
    grad_kv = total.astype(jnp.bfloat16)
    grad_key = grad_kv[:, :kv_width]
    grad_value = grad_kv[:, kv_width:]

    fsdp_count = lax.axis_size("fsdp")
    fsdp_at = lax.axis_index("fsdp")
    model_width = layer_input.shape[2]
    shard_rows = model_width // fsdp_count
    own_input = layer_input[0]
    inputs = [lax.dynamic_slice_in_dim(own_input, fsdp_at * shard_rows, shard_rows, axis=1)]
    values = [grad_value]
    for steps in range(1, fsdp_count):
        target = (fsdp_at + steps) % fsdp_count
        outgoing = lax.dynamic_slice_in_dim(own_input, target * shard_rows, shard_rows, axis=1)
        inputs.append(rotated(outgoing, "fsdp", steps))
        values.append(rotated(grad_value, "fsdp", steps))
    stacked_inputs = jnp.concatenate(inputs, axis=0)
    stacked_values = jnp.concatenate(values, axis=0)
    shard = lax.dot_general(stacked_inputs, stacked_values, TN, preferred_element_type=jnp.float32)

    sub_count = lax.axis_size("sub")
    sub_at = lax.axis_index("sub")
    piece_rows = shard_rows // sub_count
    mine = lax.dynamic_slice_in_dim(shard, sub_at * piece_rows, piece_rows, axis=0)
    for steps in range(1, sub_count):
        target = (sub_at + steps) % sub_count
        outgoing = lax.dynamic_slice_in_dim(shard, target * piece_rows, piece_rows, axis=0)
        mine = mine + rotated(outgoing.astype(jnp.bfloat16), "sub", steps).astype(jnp.float32)
    reduced = lax.psum(mine.astype(jnp.bfloat16), "ctx").astype(jnp.float32)
    if sub_count == 2:
        other = rotated(reduced.astype(jnp.bfloat16), "sub", 1).astype(jnp.float32)
        first = jnp.where(sub_at == 0, reduced, other)
        second = jnp.where(sub_at == 0, other, reduced)
        weight_v = jnp.concatenate([first, second], axis=0)
    else:
        weight_v = lax.all_gather(reduced, "sub", axis=0, tiled=True)
    token_scale = float(fsdp_count * lax.axis_size(RING) * block_rows) ** (-0.5)
    return (
        grad_q[None],
        grad_key[None],
        grad_value[None],
        weight_v * token_scale,
    )


def solution(mesh):
    placed = (
        P(("groups", "fsdp"), ("ctx", "sub"), None),
        P(("groups", "fsdp"), ("ctx", "sub"), None),
        P(("groups", "fsdp"), ("ctx", "sub"), None),
        P(("groups", "fsdp"), ("ctx", "sub"), None),
        P(("groups", "fsdp"), ("ctx", "sub"), None),
        P(("groups", "fsdp"), None),
    )
    return jax.shard_map(
        body,
        mesh=mesh,
        in_specs=placed,
        out_specs=(
            P(("groups", "fsdp"), ("ctx", "sub"), None),
            P(("groups", "fsdp"), ("ctx", "sub"), None),
            P(("groups", "fsdp"), ("ctx", "sub"), None),
            P(("groups", "fsdp"), None),
        ),
        check_vma=False,
    )
```

```python
import functools

import jax
import jax.numpy as jnp
from jax import lax
from jax.experimental import pallas as pl
from jax.experimental.pallas import tpu as pltpu
from jax.sharding import PartitionSpec as P

HEAD_DIM = 256
SPAN = 768
RING = ("ctx", "sub")
NT = (((1,), (1,)), ((), ()))
TN = (((0,), (0,)), ((), ()))


def passed_along(value, axis, steps):
    count = lax.axis_size(axis)
    first, last = (max(0, -steps), min(count, count - steps))
    return lax.ppermute(value, axis, [(source, source + steps) for source in range(first, last)])


def rotated(value, axis, steps):
    count = lax.axis_size(axis)
    return lax.ppermute(value, axis, [(source, (source + steps) % count) for source in range(count)])


def doc_start_of(starts, positions):
    covered = starts[None, :] <= positions[:, None]
    return jnp.max(jnp.where(covered, starts[None, :], 0), axis=1)


def attention_kernel(*refs, heads, kv_heads, margin, blocks):
    lo_ref, q_ref, do_ref = refs[:3]
    block_refs = refs[3 : 3 + blocks]
    dq_ref = refs[3 + blocks]
    out_refs = refs[4 + blocks : 4 + 2 * blocks]
    kv_ref = refs[4 + 2 * blocks]
    dkv_ref = refs[5 + 2 * blocks]
    block_rows = block_refs[0].shape[0]
    for index, block_ref in enumerate(block_refs):
        kv_ref[pl.ds(index * block_rows, block_rows), :] = block_ref[...]
    rows = q_ref.shape[0]
    keys = kv_ref.shape[0]
    scale = HEAD_DIM ** (-0.5)
    kv_width = kv_heads * HEAD_DIM
    per_group = heads // kv_heads
    col = lax.broadcasted_iota(jnp.int32, (rows, keys), 1)
    row = lax.broadcasted_iota(jnp.int32, (rows, keys), 0)
    allowed = (col >= lo_ref[...]) & (col <= row + margin)
    for group in range(kv_heads):
        k_cols = pl.ds(group * HEAD_DIM, HEAD_DIM)
        v_cols = pl.ds(kv_width + group * HEAD_DIM, HEAD_DIM)
        key_g = kv_ref[:, k_cols]
        value_g = kv_ref[:, v_cols]
        grad_k = None
        grad_v = None
        for member in range(per_group):
            q_cols = pl.ds((group * per_group + member) * HEAD_DIM, HEAD_DIM)
            query_h = q_ref[:, q_cols]
            grad_h = do_ref[:, q_cols]
            scores = lax.dot_general(query_h, key_g, NT, preferred_element_type=jnp.float32) * scale
            scores = jnp.where(allowed, scores, -1e30)
            largest = jnp.max(scores, axis=1, keepdims=True)
            raised = jnp.where(allowed, jnp.exp(scores - largest), 0.0)
            probs = raised / jnp.sum(raised, axis=1, keepdims=True)
            grad_probs = lax.dot_general(grad_h, value_g, NT, preferred_element_type=jnp.float32)
            row_dot = jnp.sum(probs * grad_probs, axis=1, keepdims=True)
            grad_scores = (probs * (grad_probs - row_dot) * scale).astype(jnp.bfloat16)
            probs_low = probs.astype(jnp.bfloat16)
            dq_ref[:, q_cols] = jnp.dot(
                grad_scores, key_g, preferred_element_type=jnp.float32
            ).astype(dq_ref.dtype)
            term_k = lax.dot_general(grad_scores, query_h, TN, preferred_element_type=jnp.float32)
            term_v = lax.dot_general(probs_low, grad_h, TN, preferred_element_type=jnp.float32)
            grad_k = term_k if grad_k is None else grad_k + term_k
            grad_v = term_v if grad_v is None else grad_v + term_v
        dkv_ref[:, k_cols] = grad_k
        dkv_ref[:, v_cols] = grad_v
    for index, out_ref in enumerate(out_refs):
        out_ref[...] = dkv_ref[pl.ds(index * block_rows, block_rows), :]


def attention(lo_rel, queries, grads, kv_blocks, heads, kv_heads, margin):
    rows, width = queries.shape
    blocks = len(kv_blocks)
    block_rows, kv_cols = kv_blocks[0].shape
    keys = blocks * block_rows
    kernel = functools.partial(
        attention_kernel, heads=heads, kv_heads=kv_heads, margin=margin, blocks=blocks
    )
    vmem = pl.BlockSpec(memory_space=pltpu.VMEM)
    flops = 2 * 5 * heads * rows * keys * HEAD_DIM
    moved = 2 * (2 * rows * width + keys * kv_cols + rows * width) + 4 * keys * kv_cols
    return pl.pallas_call(
        kernel,
        out_shape=(jax.ShapeDtypeStruct((rows, width), jnp.bfloat16),)
        + tuple(jax.ShapeDtypeStruct((block_rows, kv_cols), jnp.float32) for _ in kv_blocks),
        in_specs=[vmem] * (3 + blocks),
        out_specs=(vmem,) * (1 + blocks),
        scratch_shapes=[
            pltpu.VMEM((keys, kv_cols), kv_blocks[0].dtype),
            pltpu.VMEM((keys, kv_cols), jnp.float32),
        ],
        cost_estimate=pl.CostEstimate(
            flops=flops, transcendentals=heads * rows * keys, bytes_accessed=moved
        ),
    )(lo_rel, queries, grads, *kv_blocks)


def body(layer_input, query_heads, key_heads, value_heads, grad_out, doc_starts):
    block_rows = query_heads.shape[1]
    window = min(SPAN, lax.axis_size(RING) * block_rows // 2)
    reach = (window + block_rows - 2) // block_rows
    margin = reach * block_rows
    kv_width = key_heads.shape[2]
    heads = query_heads.shape[2] // HEAD_DIM
    kv_heads = kv_width // HEAD_DIM
    first_row = lax.axis_index(RING) * block_rows

    own_kv = jnp.concatenate([key_heads[0], value_heads[0]], axis=1)
    arrived = []
    moving = own_kv
    for _ in range(reach):
        moving = passed_along(moving, RING, 1)
        arrived.append(moving)
    query_pos = first_row + jnp.arange(block_rows, dtype=jnp.int32)
    lowest = jnp.maximum(doc_start_of(doc_starts[0], query_pos), query_pos - window + 1)
    lo_rel = (lowest - first_row + margin).astype(jnp.int32)[:, None]
    grad_q, *grad_pieces = attention(
        lo_rel, query_heads[0], grad_out[0], arrived[::-1] + [own_kv], heads, kv_heads, margin
    )

    def own_piece(distance):
        return grad_pieces[reach - distance]

    total = own_piece(reach)
    for distance in range(reach - 1, -1, -1):
        moved = passed_along(total.astype(jnp.bfloat16), RING, -1).astype(jnp.float32)
        total = moved + own_piece(distance)
    grad_kv = total.astype(jnp.bfloat16)
    grad_key = grad_kv[:, :kv_width]
    grad_value = grad_kv[:, kv_width:]

    fsdp_count = lax.axis_size("fsdp")
    fsdp_at = lax.axis_index("fsdp")
    model_width = layer_input.shape[2]
    shard_rows = model_width // fsdp_count
    own_input = layer_input[0]
    inputs = [lax.dynamic_slice_in_dim(own_input, fsdp_at * shard_rows, shard_rows, axis=1)]
    values = [grad_value]
    for steps in range(1, fsdp_count):
        target = (fsdp_at + steps) % fsdp_count
        outgoing = lax.dynamic_slice_in_dim(own_input, target * shard_rows, shard_rows, axis=1)
        inputs.append(rotated(outgoing, "fsdp", steps))
        values.append(rotated(grad_value, "fsdp", steps))
    stacked_inputs = jnp.concatenate(inputs, axis=0)
    stacked_values = jnp.concatenate(values, axis=0)
    shard = lax.dot_general(stacked_inputs, stacked_values, TN, preferred_element_type=jnp.float32)

    sub_count = lax.axis_size("sub")
    sub_at = lax.axis_index("sub")
    piece_rows = shard_rows // sub_count
    mine = lax.dynamic_slice_in_dim(shard, sub_at * piece_rows, piece_rows, axis=0)
    for steps in range(1, sub_count):
        target = (sub_at + steps) % sub_count
        outgoing = lax.dynamic_slice_in_dim(shard, target * piece_rows, piece_rows, axis=0)
        mine = mine + rotated(outgoing.astype(jnp.bfloat16), "sub", steps).astype(jnp.float32)
    scattered = lax.psum_scatter(mine.astype(jnp.bfloat16), "ctx", scatter_dimension=0, tiled=True)
    reduced = lax.all_gather(scattered, "ctx", axis=0, tiled=True).astype(jnp.float32)
    if sub_count == 2:
        other = rotated(reduced.astype(jnp.bfloat16), "sub", 1).astype(jnp.float32)
        first = jnp.where(sub_at == 0, reduced, other)
        second = jnp.where(sub_at == 0, other, reduced)
        weight_v = jnp.concatenate([first, second], axis=0)
    else:
        weight_v = lax.all_gather(reduced, "sub", axis=0, tiled=True)
    token_scale = float(fsdp_count * lax.axis_size(RING) * block_rows) ** (-0.5)
    return (
        grad_q[None],
        grad_key[None],
        grad_value[None],
        weight_v * token_scale,
    )


def solution(mesh):
    placed = (
        P(("groups", "fsdp"), ("ctx", "sub"), None),
        P(("groups", "fsdp"), ("ctx", "sub"), None),
        P(("groups", "fsdp"), ("ctx", "sub"), None),
        P(("groups", "fsdp"), ("ctx", "sub"), None),
        P(("groups", "fsdp"), ("ctx", "sub"), None),
        P(("groups", "fsdp"), None),
    )
    return jax.shard_map(
        body,
        mesh=mesh,
        in_specs=placed,
        out_specs=(
            P(("groups", "fsdp"), ("ctx", "sub"), None),
            P(("groups", "fsdp"), ("ctx", "sub"), None),
            P(("groups", "fsdp"), ("ctx", "sub"), None),
            P(("groups", "fsdp"), None),
        ),
        check_vma=False,
    )
```

```python
import functools

import jax
import jax.numpy as jnp
from jax import lax
from jax.experimental import pallas as pl
from jax.experimental.pallas import tpu as pltpu
from jax.sharding import PartitionSpec as P

HEAD_DIM = 256
SPAN = 768
RING = ("ctx", "sub")
NT = (((1,), (1,)), ((), ()))
TN = (((0,), (0,)), ((), ()))


def passed_along(value, axis, steps):
    count = lax.axis_size(axis)
    first, last = (max(0, -steps), min(count, count - steps))
    return lax.ppermute(value, axis, [(source, source + steps) for source in range(first, last)])


def rotated(value, axis, steps):
    count = lax.axis_size(axis)
    return lax.ppermute(value, axis, [(source, (source + steps) % count) for source in range(count)])


def ring_sum(piece, axis):
    count = lax.axis_size(axis)
    at = lax.axis_index(axis)
    rows = piece.shape[0] // count
    total = lax.dynamic_slice_in_dim(piece, at * rows, rows, axis=0)
    for steps in range(1, count):
        outgoing = lax.dynamic_slice_in_dim(piece, ((at + steps) % count) * rows, rows, axis=0)
        total = total + rotated(outgoing.astype(jnp.bfloat16), axis, steps).astype(jnp.float32)
    low = total.astype(jnp.bfloat16)
    gathered = jnp.zeros(piece.shape, jnp.float32)
    gathered = lax.dynamic_update_slice_in_dim(gathered, total, at * rows, axis=0)
    for steps in range(1, count):
        arrived = rotated(low, axis, steps).astype(jnp.float32)
        gathered = lax.dynamic_update_slice_in_dim(
            gathered, arrived, ((at - steps) % count) * rows, axis=0
        )
    return gathered


def doc_start_of(starts, positions):
    covered = starts[None, :] <= positions[:, None]
    return jnp.max(jnp.where(covered, starts[None, :], 0), axis=1)


def attention_kernel(*refs, heads, kv_heads, margin, blocks):
    lo_ref, q_ref, do_ref = refs[:3]
    block_refs = refs[3 : 3 + blocks]
    kv_ref, dkv_ref = refs[-2:]
    outs = refs[-3 - blocks : -2]
    dq_ref = outs[0]
    out_refs = outs[1:]
    block_rows = block_refs[0].shape[0]
    for index, block_ref in enumerate(block_refs):
        kv_ref[pl.ds(index * block_rows, block_rows), :] = block_ref[...]
    rows = q_ref.shape[0]
    keys = kv_ref.shape[0]
    scale = HEAD_DIM ** (-0.5)
    kv_width = kv_heads * HEAD_DIM
    per_group = heads // kv_heads
    col = lax.broadcasted_iota(jnp.int32, (rows, keys), 1)
    row = lax.broadcasted_iota(jnp.int32, (rows, keys), 0)
    allowed = (col >= lo_ref[...]) & (col <= row + margin)
    for group in range(kv_heads):
        k_cols = pl.ds(group * HEAD_DIM, HEAD_DIM)
        v_cols = pl.ds(kv_width + group * HEAD_DIM, HEAD_DIM)
        key_g = kv_ref[:, k_cols]
        value_g = kv_ref[:, v_cols]
        grad_k = None
        grad_v = None
        for member in range(per_group):
            q_cols = pl.ds((group * per_group + member) * HEAD_DIM, HEAD_DIM)
            query_h = q_ref[:, q_cols]
            grad_h = do_ref[:, q_cols]
            scores = lax.dot_general(query_h, key_g, NT, preferred_element_type=jnp.float32) * scale
            scores = jnp.where(allowed, scores, -1e30)
            largest = jnp.max(scores, axis=1, keepdims=True)
            raised = jnp.where(allowed, jnp.exp(scores - largest), 0.0)
            probs = raised / jnp.sum(raised, axis=1, keepdims=True)
            grad_probs = lax.dot_general(grad_h, value_g, NT, preferred_element_type=jnp.float32)
            row_dot = jnp.sum(probs * grad_probs, axis=1, keepdims=True)
            grad_scores = (probs * (grad_probs - row_dot) * scale).astype(jnp.bfloat16)
            probs_low = probs.astype(jnp.bfloat16)
            dq_ref[:, q_cols] = jnp.dot(
                grad_scores, key_g, preferred_element_type=jnp.float32
            ).astype(dq_ref.dtype)
            term_k = lax.dot_general(grad_scores, query_h, TN, preferred_element_type=jnp.float32)
            term_v = lax.dot_general(probs_low, grad_h, TN, preferred_element_type=jnp.float32)
            grad_k = term_k if grad_k is None else grad_k + term_k
            grad_v = term_v if grad_v is None else grad_v + term_v
        dkv_ref[:, k_cols] = grad_k
        dkv_ref[:, v_cols] = grad_v
    for index, out_ref in enumerate(out_refs):
        out_ref[...] = dkv_ref[pl.ds(index * block_rows, block_rows), :]


def attention(lo_rel, queries, grads, kv_blocks, heads, kv_heads, margin, early):
    rows, width = queries.shape
    blocks = len(kv_blocks)
    block_rows, kv_cols = kv_blocks[0].shape
    keys = blocks * block_rows
    kernel = functools.partial(
        attention_kernel, heads=heads, kv_heads=kv_heads, margin=margin, blocks=blocks
    )
    vmem = pl.BlockSpec(memory_space=pltpu.VMEM)
    flops = 2 * 5 * heads * rows * keys * HEAD_DIM
    moved = 2 * (2 * rows * width + keys * kv_cols + rows * width) + 4 * keys * kv_cols
    return pl.pallas_call(
        kernel,
        out_shape=(jax.ShapeDtypeStruct((rows, width), jnp.bfloat16),)
        + tuple(jax.ShapeDtypeStruct((block_rows, kv_cols), jnp.float32) for _ in kv_blocks),
        in_specs=[vmem] * (3 + blocks) + [pl.BlockSpec(memory_space=pl.ANY)] * len(early),
        out_specs=(vmem,) * (1 + blocks),
        scratch_shapes=[
            pltpu.VMEM((keys, kv_cols), kv_blocks[0].dtype),
            pltpu.VMEM((keys, kv_cols), jnp.float32),
        ],
        cost_estimate=pl.CostEstimate(
            flops=flops, transcendentals=heads * rows * keys, bytes_accessed=moved
        ),
    )(lo_rel, queries, grads, *kv_blocks, *early)


def body(layer_input, query_heads, key_heads, value_heads, grad_out, doc_starts):
    block_rows = query_heads.shape[1]
    window = min(SPAN, lax.axis_size(RING) * block_rows // 2)
    reach = (window + block_rows - 2) // block_rows
    margin = reach * block_rows
    kv_width = key_heads.shape[2]
    heads = query_heads.shape[2] // HEAD_DIM
    kv_heads = kv_width // HEAD_DIM
    first_row = lax.axis_index(RING) * block_rows

    fsdp_count = lax.axis_size("fsdp")
    fsdp_at = lax.axis_index("fsdp")
    model_width = layer_input.shape[2]
    shard_rows = model_width // fsdp_count
    own_input = layer_input[0]
    inputs = [lax.dynamic_slice_in_dim(own_input, fsdp_at * shard_rows, shard_rows, axis=1)]
    for steps in range(1, fsdp_count):
        target = (fsdp_at + steps) % fsdp_count
        outgoing = lax.dynamic_slice_in_dim(own_input, target * shard_rows, shard_rows, axis=1)
        inputs.append(rotated(outgoing, "fsdp", steps))

    own_kv = jnp.concatenate([key_heads[0], value_heads[0]], axis=1)
    arrived = []
    moving = own_kv
    for _ in range(reach):
        moving = passed_along(moving, RING, 1)
        arrived.append(moving)
    query_pos = first_row + jnp.arange(block_rows, dtype=jnp.int32)
    lowest = jnp.maximum(doc_start_of(doc_starts[0], query_pos), query_pos - window + 1)
    lo_rel = (lowest - first_row + margin).astype(jnp.int32)[:, None]
    grad_q, *grad_pieces = attention(
        lo_rel, query_heads[0], grad_out[0], arrived[::-1] + [own_kv], heads, kv_heads, margin,
        inputs[1:],
    )

    def own_piece(distance):
        return grad_pieces[reach - distance]

    total = own_piece(reach)
    for distance in range(reach - 1, -1, -1):
        moved = passed_along(total.astype(jnp.bfloat16), RING, -1).astype(jnp.float32)
        total = moved + own_piece(distance)
    grad_kv = total.astype(jnp.bfloat16)
    grad_key = grad_kv[:, :kv_width]
    grad_value = grad_kv[:, kv_width:]

    values = [grad_value]
    for steps in range(1, fsdp_count):
        values.append(rotated(grad_value, "fsdp", steps))
    stacked_inputs = jnp.concatenate(inputs, axis=0)
    stacked_values = jnp.concatenate(values, axis=0)
    shard = lax.dot_general(stacked_inputs, stacked_values, TN, preferred_element_type=jnp.float32)

    sub_count = lax.axis_size("sub")
    sub_at = lax.axis_index("sub")
    piece_rows = shard_rows // sub_count
    mine = lax.dynamic_slice_in_dim(shard, sub_at * piece_rows, piece_rows, axis=0)
    for steps in range(1, sub_count):
        target = (sub_at + steps) % sub_count
        outgoing = lax.dynamic_slice_in_dim(shard, target * piece_rows, piece_rows, axis=0)
        mine = mine + rotated(outgoing.astype(jnp.bfloat16), "sub", steps).astype(jnp.float32)
    reduced = ring_sum(mine, "ctx")
    if sub_count == 2:
        other = rotated(reduced.astype(jnp.bfloat16), "sub", 1).astype(jnp.float32)
        first = jnp.where(sub_at == 0, reduced, other)
        second = jnp.where(sub_at == 0, other, reduced)
        weight_v = jnp.concatenate([first, second], axis=0)
    else:
        weight_v = lax.all_gather(reduced, "sub", axis=0, tiled=True)
    token_scale = float(fsdp_count * lax.axis_size(RING) * block_rows) ** (-0.5)
    return (
        grad_q[None],
        grad_key[None],
        grad_value[None],
        weight_v * token_scale,
    )


def solution(mesh):
    placed = (
        P(("groups", "fsdp"), ("ctx", "sub"), None),
        P(("groups", "fsdp"), ("ctx", "sub"), None),
        P(("groups", "fsdp"), ("ctx", "sub"), None),
        P(("groups", "fsdp"), ("ctx", "sub"), None),
        P(("groups", "fsdp"), ("ctx", "sub"), None),
        P(("groups", "fsdp"), None),
    )
    return jax.shard_map(
        body,
        mesh=mesh,
        in_specs=placed,
        out_specs=(
            P(("groups", "fsdp"), ("ctx", "sub"), None),
            P(("groups", "fsdp"), ("ctx", "sub"), None),
            P(("groups", "fsdp"), ("ctx", "sub"), None),
            P(("groups", "fsdp"), None),
        ),
        check_vma=False,
    )
```

```python
import functools

import jax
import jax.numpy as jnp
from jax import lax
from jax.experimental import pallas as pl
from jax.experimental.pallas import tpu as pltpu
from jax.sharding import PartitionSpec as P

HEAD_DIM = 256
SPAN = 768
RING = ("ctx", "sub")
NT = (((1,), (1,)), ((), ()))
TN = (((0,), (0,)), ((), ()))


def passed_along(value, axis, steps):
    count = lax.axis_size(axis)
    first, last = (max(0, -steps), min(count, count - steps))
    return lax.ppermute(value, axis, [(source, source + steps) for source in range(first, last)])


def rotated(value, axis, steps):
    count = lax.axis_size(axis)
    return lax.ppermute(value, axis, [(source, (source + steps) % count) for source in range(count)])


def ring_sum(piece, axis):
    count = lax.axis_size(axis)
    at = lax.axis_index(axis)
    rows = piece.shape[0] // count
    total = lax.dynamic_slice_in_dim(piece, at * rows, rows, axis=0)
    for steps in range(1, count):
        outgoing = lax.dynamic_slice_in_dim(piece, ((at + steps) % count) * rows, rows, axis=0)
        total = total + rotated(outgoing.astype(jnp.bfloat16), axis, steps).astype(jnp.float32)
    low = total.astype(jnp.bfloat16)
    gathered = jnp.zeros(piece.shape, jnp.float32)
    gathered = lax.dynamic_update_slice_in_dim(gathered, total, at * rows, axis=0)
    for steps in range(1, count):
        arrived = rotated(low, axis, steps).astype(jnp.float32)
        gathered = lax.dynamic_update_slice_in_dim(
            gathered, arrived, ((at - steps) % count) * rows, axis=0
        )
    return gathered


def doc_start_of(starts, positions):
    covered = starts[None, :] <= positions[:, None]
    return jnp.max(jnp.where(covered, starts[None, :], 0), axis=1)


def attention_kernel(*refs, heads, kv_heads, margin, slots, blocks):
    flag_ref, lo_ref, q_ref, do_ref = refs[:4]
    block_refs = refs[4 : 4 + blocks]
    kv_ref, dkv_ref = refs[-2:]
    outs = refs[-3 - len(slots) : -2]
    dq_ref = outs[0]
    out_refs = outs[1:]
    block_rows = block_refs[0].shape[0]
    flag = flag_ref[0]
    for index, (when_low, when_high) in enumerate(slots):
        target = kv_ref.at[pl.ds(index * block_rows, block_rows), :]
        if when_low == when_high:
            target[...] = block_refs[when_low][...]
        else:

            @pl.when(flag == 0)
            def _():
                target[...] = block_refs[when_low][...]

            @pl.when(flag != 0)
            def _():
                target[...] = block_refs[when_high][...]

    rows = q_ref.shape[0]
    keys = kv_ref.shape[0]
    scale = HEAD_DIM ** (-0.5)
    kv_width = kv_heads * HEAD_DIM
    per_group = heads // kv_heads
    col = lax.broadcasted_iota(jnp.int32, (rows, keys), 1)
    row = lax.broadcasted_iota(jnp.int32, (rows, keys), 0)
    allowed = (col >= lo_ref[...]) & (col <= row + margin)
    for group in range(kv_heads):
        k_cols = pl.ds(group * HEAD_DIM, HEAD_DIM)
        v_cols = pl.ds(kv_width + group * HEAD_DIM, HEAD_DIM)
        key_g = kv_ref[:, k_cols]
        value_g = kv_ref[:, v_cols]
        grad_k = None
        grad_v = None
        for member in range(per_group):
            q_cols = pl.ds((group * per_group + member) * HEAD_DIM, HEAD_DIM)
            query_h = q_ref[:, q_cols]
            grad_h = do_ref[:, q_cols]
            scores = lax.dot_general(query_h, key_g, NT, preferred_element_type=jnp.float32) * scale
            scores = jnp.where(allowed, scores, -1e30)
            largest = jnp.max(scores, axis=1, keepdims=True)
            raised = jnp.where(allowed, jnp.exp(scores - largest), 0.0)
            probs = raised / jnp.sum(raised, axis=1, keepdims=True)
            grad_probs = lax.dot_general(grad_h, value_g, NT, preferred_element_type=jnp.float32)
            row_dot = jnp.sum(probs * grad_probs, axis=1, keepdims=True)
            grad_scores = (probs * (grad_probs - row_dot) * scale).astype(jnp.bfloat16)
            probs_low = probs.astype(jnp.bfloat16)
            dq_ref[:, q_cols] = jnp.dot(
                grad_scores, key_g, preferred_element_type=jnp.float32
            ).astype(dq_ref.dtype)
            term_k = lax.dot_general(grad_scores, query_h, TN, preferred_element_type=jnp.float32)
            term_v = lax.dot_general(probs_low, grad_h, TN, preferred_element_type=jnp.float32)
            grad_k = term_k if grad_k is None else grad_k + term_k
            grad_v = term_v if grad_v is None else grad_v + term_v
        dkv_ref[:, k_cols] = grad_k
        dkv_ref[:, v_cols] = grad_v
    for index, out_ref in enumerate(out_refs):
        out_ref[...] = dkv_ref[pl.ds(index * block_rows, block_rows), :]


def attention(flag, lo_rel, queries, grads, kv_blocks, slots, heads, kv_heads, margin, early):
    rows, width = queries.shape
    blocks = len(kv_blocks)
    block_rows, kv_cols = kv_blocks[0].shape
    keys = len(slots) * block_rows
    kernel = functools.partial(
        attention_kernel,
        heads=heads,
        kv_heads=kv_heads,
        margin=margin,
        slots=tuple(slots),
        blocks=blocks,
    )
    vmem = pl.BlockSpec(memory_space=pltpu.VMEM)
    smem = pl.BlockSpec(memory_space=pltpu.SMEM)
    flops = 2 * 5 * heads * rows * keys * HEAD_DIM
    moved = 2 * (2 * rows * width + keys * kv_cols + rows * width) + 4 * keys * kv_cols
    return pl.pallas_call(
        kernel,
        out_shape=(jax.ShapeDtypeStruct((rows, width), jnp.bfloat16),)
        + tuple(jax.ShapeDtypeStruct((block_rows, kv_cols), jnp.float32) for _ in slots),
        in_specs=[smem] + [vmem] * (3 + blocks) + [pl.BlockSpec(memory_space=pl.ANY)] * len(early),
        out_specs=(vmem,) * (1 + len(slots)),
        scratch_shapes=[
            pltpu.VMEM((keys, kv_cols), kv_blocks[0].dtype),
            pltpu.VMEM((keys, kv_cols), jnp.float32),
        ],
        cost_estimate=pl.CostEstimate(
            flops=flops, transcendentals=heads * rows * keys, bytes_accessed=moved
        ),
    )(flag, lo_rel, queries, grads, *kv_blocks, *early)


def body(layer_input, query_heads, key_heads, value_heads, grad_out, doc_starts):
    block_rows = query_heads.shape[1]
    window = min(SPAN, lax.axis_size(RING) * block_rows // 2)
    reach = (window + block_rows - 2) // block_rows
    margin = reach * block_rows
    kv_width = key_heads.shape[2]
    heads = query_heads.shape[2] // HEAD_DIM
    kv_heads = kv_width // HEAD_DIM
    first_row = lax.axis_index(RING) * block_rows

    fsdp_count = lax.axis_size("fsdp")
    fsdp_at = lax.axis_index("fsdp")
    model_width = layer_input.shape[2]
    shard_rows = model_width // fsdp_count
    own_input = layer_input[0]
    inputs = [lax.dynamic_slice_in_dim(own_input, fsdp_at * shard_rows, shard_rows, axis=1)]
    for steps in range(1, fsdp_count):
        target = (fsdp_at + steps) % fsdp_count
        outgoing = lax.dynamic_slice_in_dim(own_input, target * shard_rows, shard_rows, axis=1)
        inputs.append(rotated(outgoing, "fsdp", steps))

    own_kv = jnp.concatenate([key_heads[0], value_heads[0]], axis=1)
    query_pos = first_row + jnp.arange(block_rows, dtype=jnp.int32)
    lowest = jnp.maximum(doc_start_of(doc_starts[0], query_pos), query_pos - window + 1)
    lo_rel = (lowest - first_row + margin).astype(jnp.int32)[:, None]
    sub_count = lax.axis_size("sub")
    sub_at = lax.axis_index("sub")
    flag = jnp.reshape(sub_at, (1,)).astype(jnp.int32)
    chip_route = sub_count == 2 and reach == 3
    if chip_route:
        ring_count = lax.axis_size(RING)
        across = [(2 * chip + 1, 2 * chip + 2) for chip in range(ring_count // 2 - 1)]
        two_back = passed_along(own_kv, "ctx", 1)
        one_back_high = passed_along(own_kv, "sub", 1)
        three_back_low = lax.ppermute(two_back, RING, across)
        swapped = rotated(two_back, "sub", 1)
        kv_blocks = [two_back, one_back_high, three_back_low, swapped, own_kv]
        slots = [(2, 3), (0, 0), (3, 1), (4, 4)]
    else:
        arrived = []
        moving = own_kv
        for _ in range(reach):
            moving = passed_along(moving, RING, 1)
            arrived.append(moving)
        kv_blocks = arrived[::-1] + [own_kv]
        slots = [(index, index) for index in range(reach + 1)]
    grad_q, *grad_pieces = attention(
        flag, lo_rel, query_heads[0], grad_out[0], kv_blocks, slots, heads, kv_heads, margin,
        inputs[1:],
    )

    def low(value):
        return value.astype(jnp.bfloat16)

    if chip_route:
        back = [(target, source) for source, target in across]
        g3, g2, g1, g0 = grad_pieces
        from_next_chip = lax.ppermute(low(g3), RING, back).astype(jnp.float32)
        from_mate = rotated(low(jnp.where(sub_at == 0, g1, g3)), "sub", 1).astype(jnp.float32)
        from_high = passed_along(low(g1), "sub", -1).astype(jnp.float32)
        two_back_sum = g2 + from_mate + from_next_chip
        total = g0 + from_high + passed_along(low(two_back_sum), "ctx", -1).astype(jnp.float32)
    else:

        def own_piece(distance):
            return grad_pieces[reach - distance]

        total = own_piece(reach)
        for distance in range(reach - 1, -1, -1):
            moved = passed_along(low(total), RING, -1).astype(jnp.float32)
            total = moved + own_piece(distance)
    grad_kv = total.astype(jnp.bfloat16)
    grad_key = grad_kv[:, :kv_width]
    grad_value = grad_kv[:, kv_width:]

    values = [grad_value]
    for steps in range(1, fsdp_count):
        values.append(rotated(grad_value, "fsdp", steps))
    stacked_inputs = jnp.concatenate(inputs, axis=0)
    stacked_values = jnp.concatenate(values, axis=0)
    shard = lax.dot_general(stacked_inputs, stacked_values, TN, preferred_element_type=jnp.float32)

    sub_count = lax.axis_size("sub")
    sub_at = lax.axis_index("sub")
    piece_rows = shard_rows // sub_count
    mine = lax.dynamic_slice_in_dim(shard, sub_at * piece_rows, piece_rows, axis=0)
    for steps in range(1, sub_count):
        target = (sub_at + steps) % sub_count
        outgoing = lax.dynamic_slice_in_dim(shard, target * piece_rows, piece_rows, axis=0)
        mine = mine + rotated(outgoing.astype(jnp.bfloat16), "sub", steps).astype(jnp.float32)
    reduced = ring_sum(mine, "ctx")
    if sub_count == 2:
        other = rotated(reduced.astype(jnp.bfloat16), "sub", 1).astype(jnp.float32)
        first = jnp.where(sub_at == 0, reduced, other)
        second = jnp.where(sub_at == 0, other, reduced)
        weight_v = jnp.concatenate([first, second], axis=0)
    else:
        weight_v = lax.all_gather(reduced, "sub", axis=0, tiled=True)
    token_scale = float(fsdp_count * lax.axis_size(RING) * block_rows) ** (-0.5)
    return (
        grad_q[None],
        grad_key[None],
        grad_value[None],
        weight_v * token_scale,
    )


def solution(mesh):
    placed = (
        P(("groups", "fsdp"), ("ctx", "sub"), None),
        P(("groups", "fsdp"), ("ctx", "sub"), None),
        P(("groups", "fsdp"), ("ctx", "sub"), None),
        P(("groups", "fsdp"), ("ctx", "sub"), None),
        P(("groups", "fsdp"), ("ctx", "sub"), None),
        P(("groups", "fsdp"), None),
    )
    return jax.shard_map(
        body,
        mesh=mesh,
        in_specs=placed,
        out_specs=(
            P(("groups", "fsdp"), ("ctx", "sub"), None),
            P(("groups", "fsdp"), ("ctx", "sub"), None),
            P(("groups", "fsdp"), ("ctx", "sub"), None),
            P(("groups", "fsdp"), None),
        ),
        check_vma=False,
    )
```

```python
import functools

import jax
import jax.numpy as jnp
from jax import lax
from jax.experimental import pallas as pl
from jax.experimental.pallas import tpu as pltpu
from jax.sharding import PartitionSpec as P

HEAD_DIM = 256
SPAN = 768
RING = ("ctx", "sub")
NT = (((1,), (1,)), ((), ()))
TN = (((0,), (0,)), ((), ()))


def passed_along(value, axis, steps):
    count = lax.axis_size(axis)
    first, last = (max(0, -steps), min(count, count - steps))
    return lax.ppermute(value, axis, [(source, source + steps) for source in range(first, last)])


def rotated(value, axis, steps):
    count = lax.axis_size(axis)
    return lax.ppermute(value, axis, [(source, (source + steps) % count) for source in range(count)])


def ring_sum(piece, axis):
    count = lax.axis_size(axis)
    at = lax.axis_index(axis)
    rows = piece.shape[0] // count
    total = lax.dynamic_slice_in_dim(piece, at * rows, rows, axis=0)
    for steps in range(1, count):
        outgoing = lax.dynamic_slice_in_dim(piece, ((at + steps) % count) * rows, rows, axis=0)
        total = total + rotated(outgoing.astype(jnp.bfloat16), axis, steps).astype(jnp.float32)
    low = total.astype(jnp.bfloat16)
    gathered = jnp.zeros(piece.shape, jnp.float32)
    gathered = lax.dynamic_update_slice_in_dim(gathered, total, at * rows, axis=0)
    for steps in range(1, count):
        arrived = rotated(low, axis, steps).astype(jnp.float32)
        gathered = lax.dynamic_update_slice_in_dim(
            gathered, arrived, ((at - steps) % count) * rows, axis=0
        )
    return gathered


def doc_start_of(starts, positions):
    covered = starts[None, :] <= positions[:, None]
    return jnp.max(jnp.where(covered, starts[None, :], 0), axis=1)


def attention_kernel(*refs, heads, kv_heads, margin, slots, blocks):
    flag_ref, lo_ref, q_ref, do_ref = refs[:4]
    block_refs = refs[4 : 4 + blocks]
    kv_ref, dkv_ref = refs[-2:]
    outs = refs[-3 - len(slots) : -2]
    dq_ref = outs[0]
    out_refs = outs[1:]
    block_rows = block_refs[0].shape[0]
    flag = flag_ref[0]
    for index, (when_low, when_high) in enumerate(slots):
        target = kv_ref.at[pl.ds(index * block_rows, block_rows), :]
        if when_low == when_high:
            target[...] = block_refs[when_low][...]
        else:

            @pl.when(flag == 0)
            def _():
                target[...] = block_refs[when_low][...]

            @pl.when(flag != 0)
            def _():
                target[...] = block_refs[when_high][...]

    rows = q_ref.shape[0]
    keys = kv_ref.shape[0]
    scale = HEAD_DIM ** (-0.5)
    kv_width = kv_heads * HEAD_DIM
    per_group = heads // kv_heads
    col = lax.broadcasted_iota(jnp.int32, (rows, keys), 1)
    row = lax.broadcasted_iota(jnp.int32, (rows, keys), 0)
    allowed = (col >= lo_ref[...]) & (col <= row + margin)
    for group in range(kv_heads):
        k_cols = pl.ds(group * HEAD_DIM, HEAD_DIM)
        v_cols = pl.ds(kv_width + group * HEAD_DIM, HEAD_DIM)
        key_g = kv_ref[:, k_cols]
        value_g = kv_ref[:, v_cols]
        grad_k = None
        grad_v = None
        for member in range(per_group):
            q_cols = pl.ds((group * per_group + member) * HEAD_DIM, HEAD_DIM)
            query_h = q_ref[:, q_cols]
            grad_h = do_ref[:, q_cols]
            scores = lax.dot_general(query_h, key_g, NT, preferred_element_type=jnp.float32) * scale
            scores = jnp.where(allowed, scores, -1e30)
            largest = jnp.max(scores, axis=1, keepdims=True)
            raised = jnp.where(allowed, jnp.exp(scores - largest), 0.0)
            probs = raised / jnp.sum(raised, axis=1, keepdims=True)
            grad_probs = lax.dot_general(grad_h, value_g, NT, preferred_element_type=jnp.float32)
            row_dot = jnp.sum(probs * grad_probs, axis=1, keepdims=True)
            grad_scores = (probs * (grad_probs - row_dot) * scale).astype(jnp.bfloat16)
            probs_low = probs.astype(jnp.bfloat16)
            dq_ref[:, q_cols] = jnp.dot(
                grad_scores, key_g, preferred_element_type=jnp.float32
            ).astype(dq_ref.dtype)
            term_k = lax.dot_general(grad_scores, query_h, TN, preferred_element_type=jnp.float32)
            term_v = lax.dot_general(probs_low, grad_h, TN, preferred_element_type=jnp.float32)
            grad_k = term_k if grad_k is None else grad_k + term_k
            grad_v = term_v if grad_v is None else grad_v + term_v
        dkv_ref[:, k_cols] = grad_k
        dkv_ref[:, v_cols] = grad_v
    for index, out_ref in enumerate(out_refs):
        out_ref[...] = dkv_ref[pl.ds(index * block_rows, block_rows), :]


def attention(flag, lo_rel, queries, grads, kv_blocks, slots, heads, kv_heads, margin, early):
    rows, width = queries.shape
    blocks = len(kv_blocks)
    block_rows, kv_cols = kv_blocks[0].shape
    keys = len(slots) * block_rows
    kernel = functools.partial(
        attention_kernel,
        heads=heads,
        kv_heads=kv_heads,
        margin=margin,
        slots=tuple(slots),
        blocks=blocks,
    )
    vmem = pl.BlockSpec(memory_space=pltpu.VMEM)
    smem = pl.BlockSpec(memory_space=pltpu.SMEM)
    flops = 2 * 5 * heads * rows * keys * HEAD_DIM
    moved = 2 * (2 * rows * width + keys * kv_cols + rows * width) + 4 * keys * kv_cols
    return pl.pallas_call(
        kernel,
        out_shape=(jax.ShapeDtypeStruct((rows, width), jnp.bfloat16),)
        + tuple(jax.ShapeDtypeStruct((block_rows, kv_cols), jnp.float32) for _ in slots),
        in_specs=[smem] + [vmem] * (3 + blocks) + [pl.BlockSpec(memory_space=pl.ANY)] * len(early),
        out_specs=(vmem,) * (1 + len(slots)),
        scratch_shapes=[
            pltpu.VMEM((keys, kv_cols), kv_blocks[0].dtype),
            pltpu.VMEM((keys, kv_cols), jnp.float32),
        ],
        cost_estimate=pl.CostEstimate(
            flops=flops, transcendentals=heads * rows * keys, bytes_accessed=moved
        ),
    )(flag, lo_rel, queries, grads, *kv_blocks, *early)


def body(layer_input, query_heads, key_heads, value_heads, grad_out, doc_starts):
    block_rows = query_heads.shape[1]
    window = min(SPAN, lax.axis_size(RING) * block_rows // 2)
    reach = (window + block_rows - 2) // block_rows
    margin = reach * block_rows
    kv_width = key_heads.shape[2]
    heads = query_heads.shape[2] // HEAD_DIM
    kv_heads = kv_width // HEAD_DIM
    first_row = lax.axis_index(RING) * block_rows

    fsdp_count = lax.axis_size("fsdp")
    fsdp_at = lax.axis_index("fsdp")
    model_width = layer_input.shape[2]
    shard_rows = model_width // fsdp_count
    own_input = layer_input[0]
    inputs = [lax.dynamic_slice_in_dim(own_input, fsdp_at * shard_rows, shard_rows, axis=1)]
    for steps in range(1, fsdp_count):
        target = (fsdp_at + steps) % fsdp_count
        outgoing = lax.dynamic_slice_in_dim(own_input, target * shard_rows, shard_rows, axis=1)
        inputs.append(rotated(outgoing, "fsdp", steps))

    own_kv = jnp.concatenate([key_heads[0], value_heads[0]], axis=1)
    query_pos = first_row + jnp.arange(block_rows, dtype=jnp.int32)
    lowest = jnp.maximum(doc_start_of(doc_starts[0], query_pos), query_pos - window + 1)
    lo_rel = (lowest - first_row + margin).astype(jnp.int32)[:, None]
    sub_count = lax.axis_size("sub")
    sub_at = lax.axis_index("sub")
    flag = jnp.reshape(sub_at, (1,)).astype(jnp.int32)
    chip_route = sub_count == 2 and reach == 3
    if chip_route:
        ring_count = lax.axis_size(RING)
        across = [(2 * chip - 3, 2 * chip) for chip in range(2, ring_count // 2)]
        two_back = passed_along(own_kv, "ctx", 1)
        one_back_high = passed_along(own_kv, "sub", 1)
        three_back_low = lax.ppermute(own_kv, RING, across)
        swapped = rotated(two_back, "sub", 1)
        kv_blocks = [two_back, one_back_high, three_back_low, swapped, own_kv]
        slots = [(2, 3), (0, 0), (3, 1), (4, 4)]
    else:
        arrived = []
        moving = own_kv
        for _ in range(reach):
            moving = passed_along(moving, RING, 1)
            arrived.append(moving)
        kv_blocks = arrived[::-1] + [own_kv]
        slots = [(index, index) for index in range(reach + 1)]
    grad_q, *grad_pieces = attention(
        flag, lo_rel, query_heads[0], grad_out[0], kv_blocks, slots, heads, kv_heads, margin,
        inputs[1:],
    )

    def low(value):
        return value.astype(jnp.bfloat16)

    if chip_route:
        back = [(target, source) for source, target in across]
        g3, g2, g1, g0 = grad_pieces
        from_far = lax.ppermute(low(g3), RING, back).astype(jnp.float32)
        from_mate = rotated(low(jnp.where(sub_at == 0, g1, g3)), "sub", 1).astype(jnp.float32)
        from_high = passed_along(low(g1), "sub", -1).astype(jnp.float32)
        two_back_sum = g2 + from_mate
        from_next = passed_along(low(two_back_sum), "ctx", -1).astype(jnp.float32)
        total = g0 + from_high + from_far + from_next
    else:

        def own_piece(distance):
            return grad_pieces[reach - distance]

        total = own_piece(reach)
        for distance in range(reach - 1, -1, -1):
            moved = passed_along(low(total), RING, -1).astype(jnp.float32)
            total = moved + own_piece(distance)
    grad_kv = total.astype(jnp.bfloat16)
    grad_key = grad_kv[:, :kv_width]
    grad_value = grad_kv[:, kv_width:]

    values = [grad_value]
    for steps in range(1, fsdp_count):
        values.append(rotated(grad_value, "fsdp", steps))
    stacked_inputs = jnp.concatenate(inputs, axis=0)
    stacked_values = jnp.concatenate(values, axis=0)
    shard = lax.dot_general(stacked_inputs, stacked_values, TN, preferred_element_type=jnp.float32)

    sub_count = lax.axis_size("sub")
    sub_at = lax.axis_index("sub")
    piece_rows = shard_rows // sub_count
    mine = lax.dynamic_slice_in_dim(shard, sub_at * piece_rows, piece_rows, axis=0)
    for steps in range(1, sub_count):
        target = (sub_at + steps) % sub_count
        outgoing = lax.dynamic_slice_in_dim(shard, target * piece_rows, piece_rows, axis=0)
        mine = mine + rotated(outgoing.astype(jnp.bfloat16), "sub", steps).astype(jnp.float32)
    reduced = ring_sum(mine, "ctx")
    if sub_count == 2:
        other = rotated(reduced.astype(jnp.bfloat16), "sub", 1).astype(jnp.float32)
        first = jnp.where(sub_at == 0, reduced, other)
        second = jnp.where(sub_at == 0, other, reduced)
        weight_v = jnp.concatenate([first, second], axis=0)
    else:
        weight_v = lax.all_gather(reduced, "sub", axis=0, tiled=True)
    token_scale = float(fsdp_count * lax.axis_size(RING) * block_rows) ** (-0.5)
    return (
        grad_q[None],
        grad_key[None],
        grad_value[None],
        weight_v * token_scale,
    )


def solution(mesh):
    placed = (
        P(("groups", "fsdp"), ("ctx", "sub"), None),
        P(("groups", "fsdp"), ("ctx", "sub"), None),
        P(("groups", "fsdp"), ("ctx", "sub"), None),
        P(("groups", "fsdp"), ("ctx", "sub"), None),
        P(("groups", "fsdp"), ("ctx", "sub"), None),
        P(("groups", "fsdp"), None),
    )
    return jax.shard_map(
        body,
        mesh=mesh,
        in_specs=placed,
        out_specs=(
            P(("groups", "fsdp"), ("ctx", "sub"), None),
            P(("groups", "fsdp"), ("ctx", "sub"), None),
            P(("groups", "fsdp"), ("ctx", "sub"), None),
            P(("groups", "fsdp"), None),
        ),
        check_vma=False,
    )
```

```python
import functools

import jax
import jax.numpy as jnp
from jax import lax
from jax.experimental import pallas as pl
from jax.experimental.pallas import tpu as pltpu
from jax.sharding import PartitionSpec as P

HEAD_DIM = 256
SPAN = 768
RING = ("ctx", "sub")
NT = (((1,), (1,)), ((), ()))
TN = (((0,), (0,)), ((), ()))


def passed_along(value, axis, steps):
    count = lax.axis_size(axis)
    first, last = (max(0, -steps), min(count, count - steps))
    return lax.ppermute(value, axis, [(source, source + steps) for source in range(first, last)])


def rotated(value, axis, steps):
    count = lax.axis_size(axis)
    return lax.ppermute(value, axis, [(source, (source + steps) % count) for source in range(count)])


def ring_sum(piece, axis):
    count = lax.axis_size(axis)
    at = lax.axis_index(axis)
    rows = piece.shape[0] // count
    total = lax.dynamic_slice_in_dim(piece, at * rows, rows, axis=0)
    for steps in range(1, count):
        outgoing = lax.dynamic_slice_in_dim(piece, ((at + steps) % count) * rows, rows, axis=0)
        total = total + rotated(outgoing.astype(jnp.bfloat16), axis, steps).astype(jnp.float32)
    low = total.astype(jnp.bfloat16)
    gathered = jnp.zeros(piece.shape, jnp.float32)
    gathered = lax.dynamic_update_slice_in_dim(gathered, total, at * rows, axis=0)
    for steps in range(1, count):
        arrived = rotated(low, axis, steps).astype(jnp.float32)
        gathered = lax.dynamic_update_slice_in_dim(
            gathered, arrived, ((at - steps) % count) * rows, axis=0
        )
    return gathered


def doc_start_of(starts, positions):
    covered = starts[None, :] <= positions[:, None]
    return jnp.max(jnp.where(covered, starts[None, :], 0), axis=1)


def attention_kernel(*refs, heads, kv_heads, margin, slots, blocks):
    flag_ref, lo_ref, q_ref, do_ref = refs[:4]
    block_refs = refs[4 : 4 + blocks]
    kv_ref, dkv_ref = refs[-2:]
    outs = refs[-3 - len(slots) : -2]
    dq_ref = outs[0]
    out_refs = outs[1:]
    block_rows = block_refs[0].shape[0]
    flag = flag_ref[0]
    for index, (when_low, when_high) in enumerate(slots):
        target = kv_ref.at[pl.ds(index * block_rows, block_rows), :]
        if when_low == when_high:
            target[...] = block_refs[when_low][...]
        else:

            @pl.when(flag == 0)
            def _():
                target[...] = block_refs[when_low][...]

            @pl.when(flag != 0)
            def _():
                target[...] = block_refs[when_high][...]

    rows = q_ref.shape[0]
    keys = kv_ref.shape[0]
    scale = HEAD_DIM ** (-0.5)
    kv_width = kv_heads * HEAD_DIM
    per_group = heads // kv_heads
    col = lax.broadcasted_iota(jnp.int32, (rows, keys), 1)
    row = lax.broadcasted_iota(jnp.int32, (rows, keys), 0)
    allowed = (col >= lo_ref[...]) & (col <= row + margin)
    for group in range(kv_heads):
        k_cols = pl.ds(group * HEAD_DIM, HEAD_DIM)
        v_cols = pl.ds(kv_width + group * HEAD_DIM, HEAD_DIM)
        key_g = kv_ref[:, k_cols]
        value_g = kv_ref[:, v_cols]
        grad_k = None
        grad_v = None
        for member in range(per_group):
            q_cols = pl.ds((group * per_group + member) * HEAD_DIM, HEAD_DIM)
            query_h = q_ref[:, q_cols]
            grad_h = do_ref[:, q_cols]
            scores = lax.dot_general(query_h, key_g, NT, preferred_element_type=jnp.float32) * scale
            scores = jnp.where(allowed, scores, -1e30)
            largest = jnp.max(scores, axis=1, keepdims=True)
            raised = jnp.where(allowed, jnp.exp(scores - largest), 0.0)
            probs = raised / jnp.sum(raised, axis=1, keepdims=True)
            grad_probs = lax.dot_general(grad_h, value_g, NT, preferred_element_type=jnp.float32)
            row_dot = jnp.sum(probs * grad_probs, axis=1, keepdims=True)
            grad_scores = (probs * (grad_probs - row_dot) * scale).astype(jnp.bfloat16)
            probs_low = probs.astype(jnp.bfloat16)
            dq_ref[:, q_cols] = jnp.dot(
                grad_scores, key_g, preferred_element_type=jnp.float32
            ).astype(dq_ref.dtype)
            term_k = lax.dot_general(grad_scores, query_h, TN, preferred_element_type=jnp.float32)
            term_v = lax.dot_general(probs_low, grad_h, TN, preferred_element_type=jnp.float32)
            grad_k = term_k if grad_k is None else grad_k + term_k
            grad_v = term_v if grad_v is None else grad_v + term_v
        dkv_ref[:, k_cols] = grad_k
        dkv_ref[:, v_cols] = grad_v
    for index, out_ref in enumerate(out_refs):
        out_ref[...] = dkv_ref[pl.ds(index * block_rows, block_rows), :]


def attention(flag, lo_rel, queries, grads, kv_blocks, slots, heads, kv_heads, margin, early):
    rows, width = queries.shape
    blocks = len(kv_blocks)
    block_rows, kv_cols = kv_blocks[0].shape
    keys = len(slots) * block_rows
    kernel = functools.partial(
        attention_kernel,
        heads=heads,
        kv_heads=kv_heads,
        margin=margin,
        slots=tuple(slots),
        blocks=blocks,
    )
    vmem = pl.BlockSpec(memory_space=pltpu.VMEM)
    smem = pl.BlockSpec(memory_space=pltpu.SMEM)
    flops = 2 * 5 * heads * rows * keys * HEAD_DIM
    moved = 2 * (2 * rows * width + keys * kv_cols + rows * width) + 4 * keys * kv_cols
    return pl.pallas_call(
        kernel,
        out_shape=(jax.ShapeDtypeStruct((rows, width), jnp.bfloat16),)
        + tuple(jax.ShapeDtypeStruct((block_rows, kv_cols), jnp.float32) for _ in slots),
        in_specs=[smem] + [vmem] * (3 + blocks) + [pl.BlockSpec(memory_space=pl.ANY)] * len(early),
        out_specs=(vmem,) * (1 + len(slots)),
        scratch_shapes=[
            pltpu.VMEM((keys, kv_cols), kv_blocks[0].dtype),
            pltpu.VMEM((keys, kv_cols), jnp.float32),
        ],
        cost_estimate=pl.CostEstimate(
            flops=flops, transcendentals=heads * rows * keys, bytes_accessed=moved
        ),
    )(flag, lo_rel, queries, grads, *kv_blocks, *early)


def body(layer_input, query_heads, key_heads, value_heads, grad_out, doc_starts):
    block_rows = query_heads.shape[1]
    window = min(SPAN, lax.axis_size(RING) * block_rows // 2)
    reach = (window + block_rows - 2) // block_rows
    margin = reach * block_rows
    kv_width = key_heads.shape[2]
    heads = query_heads.shape[2] // HEAD_DIM
    kv_heads = kv_width // HEAD_DIM
    first_row = lax.axis_index(RING) * block_rows

    fsdp_count = lax.axis_size("fsdp")
    fsdp_at = lax.axis_index("fsdp")
    model_width = layer_input.shape[2]
    shard_rows = model_width // fsdp_count
    own_input = layer_input[0]
    inputs = [lax.dynamic_slice_in_dim(own_input, fsdp_at * shard_rows, shard_rows, axis=1)]
    for steps in range(1, fsdp_count):
        target = (fsdp_at + steps) % fsdp_count
        outgoing = lax.dynamic_slice_in_dim(own_input, target * shard_rows, shard_rows, axis=1)
        inputs.append(rotated(outgoing, "fsdp", steps))

    own_kv = jnp.concatenate([key_heads[0], value_heads[0]], axis=1)
    query_pos = first_row + jnp.arange(block_rows, dtype=jnp.int32)
    lowest = jnp.maximum(doc_start_of(doc_starts[0], query_pos), query_pos - window + 1)
    lo_rel = (lowest - first_row + margin).astype(jnp.int32)[:, None]
    sub_count = lax.axis_size("sub")
    sub_at = lax.axis_index("sub")
    flag = jnp.reshape(sub_at, (1,)).astype(jnp.int32)
    chip_route = sub_count == 2 and reach == 3
    if chip_route:
        ring_count = lax.axis_size(RING)
        across = [(2 * chip - 3, 2 * chip) for chip in range(2, ring_count // 2)]
        two_back = passed_along(own_kv, "ctx", 1)
        one_back_high = passed_along(own_kv, "sub", 1)
        three_back_low = lax.ppermute(own_kv, RING, across)
        swapped = rotated(two_back, "sub", 1)
        kv_blocks = [two_back, one_back_high, three_back_low, swapped, own_kv]
        slots = [(2, 3), (0, 0), (3, 1), (4, 4)]
    else:
        arrived = []
        moving = own_kv
        for _ in range(reach):
            moving = passed_along(moving, RING, 1)
            arrived.append(moving)
        kv_blocks = arrived[::-1] + [own_kv]
        slots = [(index, index) for index in range(reach + 1)]
    grad_q, *grad_pieces = attention(
        flag, lo_rel, query_heads[0], grad_out[0], kv_blocks, slots, heads, kv_heads, margin,
        inputs[1:],
    )

    def low(value):
        return value.astype(jnp.bfloat16)

    if chip_route:
        back = [(target, source) for source, target in across]

        def returned(g3, g2, g1, g0):
            from_far = lax.ppermute(low(g3), RING, back).astype(jnp.float32)
            from_mate = rotated(low(jnp.where(sub_at == 0, g1, g3)), "sub", 1).astype(jnp.float32)
            from_high = passed_along(low(g1), "sub", -1).astype(jnp.float32)
            two_back_sum = g2 + from_mate
            from_next = passed_along(low(two_back_sum), "ctx", -1).astype(jnp.float32)
            return g0 + from_high + from_far + from_next

        total_v = returned(*[piece[:, kv_width:] for piece in grad_pieces])
        total_v, key_pieces = lax.optimization_barrier(
            (total_v, [piece[:, :kv_width] for piece in grad_pieces])
        )
        total_k = returned(*key_pieces)
        total = jnp.concatenate([total_k, total_v], axis=1)
    else:

        def own_piece(distance):
            return grad_pieces[reach - distance]

        total = own_piece(reach)
        for distance in range(reach - 1, -1, -1):
            moved = passed_along(low(total), RING, -1).astype(jnp.float32)
            total = moved + own_piece(distance)
    grad_kv = total.astype(jnp.bfloat16)
    grad_key = grad_kv[:, :kv_width]
    grad_value = grad_kv[:, kv_width:]

    values = [grad_value]
    for steps in range(1, fsdp_count):
        values.append(rotated(grad_value, "fsdp", steps))
    stacked_inputs = jnp.concatenate(inputs, axis=0)
    stacked_values = jnp.concatenate(values, axis=0)
    shard = lax.dot_general(stacked_inputs, stacked_values, TN, preferred_element_type=jnp.float32)

    sub_count = lax.axis_size("sub")
    sub_at = lax.axis_index("sub")
    piece_rows = shard_rows // sub_count
    mine = lax.dynamic_slice_in_dim(shard, sub_at * piece_rows, piece_rows, axis=0)
    for steps in range(1, sub_count):
        target = (sub_at + steps) % sub_count
        outgoing = lax.dynamic_slice_in_dim(shard, target * piece_rows, piece_rows, axis=0)
        mine = mine + rotated(outgoing.astype(jnp.bfloat16), "sub", steps).astype(jnp.float32)
    reduced = ring_sum(mine, "ctx")
    if sub_count == 2:
        other = rotated(reduced.astype(jnp.bfloat16), "sub", 1).astype(jnp.float32)
        first = jnp.where(sub_at == 0, reduced, other)
        second = jnp.where(sub_at == 0, other, reduced)
        weight_v = jnp.concatenate([first, second], axis=0)
    else:
        weight_v = lax.all_gather(reduced, "sub", axis=0, tiled=True)
    token_scale = float(fsdp_count * lax.axis_size(RING) * block_rows) ** (-0.5)
    return (
        grad_q[None],
        grad_key[None],
        grad_value[None],
        weight_v * token_scale,
    )


def solution(mesh):
    placed = (
        P(("groups", "fsdp"), ("ctx", "sub"), None),
        P(("groups", "fsdp"), ("ctx", "sub"), None),
        P(("groups", "fsdp"), ("ctx", "sub"), None),
        P(("groups", "fsdp"), ("ctx", "sub"), None),
        P(("groups", "fsdp"), ("ctx", "sub"), None),
        P(("groups", "fsdp"), None),
    )
    return jax.shard_map(
        body,
        mesh=mesh,
        in_specs=placed,
        out_specs=(
            P(("groups", "fsdp"), ("ctx", "sub"), None),
            P(("groups", "fsdp"), ("ctx", "sub"), None),
            P(("groups", "fsdp"), ("ctx", "sub"), None),
            P(("groups", "fsdp"), None),
        ),
        check_vma=False,
    )
```

```python
import functools
import math

import jax
import jax.numpy as jnp
from jax import lax
from jax.experimental import pallas as pl
from jax.experimental.pallas import tpu as pltpu
from jax.sharding import PartitionSpec as P

HEAD_DIM = 256
SPAN = 768
RING = ("ctx", "sub")
NT = (((1,), (1,)), ((), ()))
TN = (((0,), (0,)), ((), ()))


def passed_along(value, axis, steps):
    count = lax.axis_size(axis)
    first, last = (max(0, -steps), min(count, count - steps))
    return lax.ppermute(value, axis, [(source, source + steps) for source in range(first, last)])


def rotated(value, axis, steps):
    count = lax.axis_size(axis)
    return lax.ppermute(value, axis, [(source, (source + steps) % count) for source in range(count)])


def ring_sum(piece, axis):
    count = lax.axis_size(axis)
    at = lax.axis_index(axis)
    rows = piece.shape[0] // count
    total = lax.dynamic_slice_in_dim(piece, at * rows, rows, axis=0)
    for steps in range(1, count):
        outgoing = lax.dynamic_slice_in_dim(piece, ((at + steps) % count) * rows, rows, axis=0)
        total = total + rotated(outgoing.astype(jnp.bfloat16), axis, steps).astype(jnp.float32)
    low = total.astype(jnp.bfloat16)
    gathered = jnp.zeros(piece.shape, jnp.float32)
    gathered = lax.dynamic_update_slice_in_dim(gathered, total, at * rows, axis=0)
    for steps in range(1, count):
        arrived = rotated(low, axis, steps).astype(jnp.float32)
        gathered = lax.dynamic_update_slice_in_dim(
            gathered, arrived, ((at - steps) % count) * rows, axis=0
        )
    return gathered


def doc_start_of(starts, positions):
    covered = starts[None, :] <= positions[:, None]
    return jnp.max(jnp.where(covered, starts[None, :], 0), axis=1)


def attention_kernel(*refs, heads, kv_heads, margin, slots, blocks, chip_outputs):
    flag_ref, lo_ref, q_ref, do_ref = refs[:4]
    block_refs = refs[4 : 4 + blocks]
    kv_ref, dkv_ref = refs[-2:]
    outs = refs[-3 - len(slots) : -2]
    dq_ref = outs[0]
    out_refs = outs[1:]
    block_rows = block_refs[0].shape[0]
    flag = flag_ref[0]
    for index, (when_low, when_high) in enumerate(slots):
        target = kv_ref.at[pl.ds(index * block_rows, block_rows), :]
        if when_low == when_high:
            target[...] = block_refs[when_low][...]
        else:

            @pl.when(flag == 0)
            def _():
                target[...] = block_refs[when_low][...]

            @pl.when(flag != 0)
            def _():
                target[...] = block_refs[when_high][...]

    rows = q_ref.shape[0]
    keys = kv_ref.shape[0]
    scale = HEAD_DIM ** (-0.5)
    kv_width = kv_heads * HEAD_DIM
    per_group = heads // kv_heads
    col = lax.broadcasted_iota(jnp.int32, (rows, keys), 1)
    row = lax.broadcasted_iota(jnp.int32, (rows, keys), 0)
    allowed = (col >= lo_ref[...]) & (col <= row + margin)
    for group in range(kv_heads):
        k_cols = pl.ds(group * HEAD_DIM, HEAD_DIM)
        v_cols = pl.ds(kv_width + group * HEAD_DIM, HEAD_DIM)
        key_g = kv_ref[:, k_cols]
        value_g = kv_ref[:, v_cols]
        grad_k = None
        grad_v = None
        for member in range(per_group):
            q_cols = pl.ds((group * per_group + member) * HEAD_DIM, HEAD_DIM)
            query_h = q_ref[:, q_cols]
            grad_h = do_ref[:, q_cols]
            scores = lax.dot_general(query_h, key_g, NT, preferred_element_type=jnp.float32) * scale
            scores = jnp.where(allowed, scores, -1e30)
            largest = jnp.max(scores, axis=1, keepdims=True)
            raised = jnp.exp(scores - largest)
            probs = raised * (1.0 / jnp.sum(raised, axis=1, keepdims=True))
            grad_probs = lax.dot_general(grad_h, value_g, NT, preferred_element_type=jnp.float32)
            row_dot = jnp.sum(probs * grad_probs, axis=1, keepdims=True)
            grad_scores = (probs * (grad_probs - row_dot) * scale).astype(jnp.bfloat16)
            probs_low = probs.astype(jnp.bfloat16)
            dq_ref[:, q_cols] = jnp.dot(
                grad_scores, key_g, preferred_element_type=jnp.float32
            ).astype(dq_ref.dtype)
            term_k = lax.dot_general(grad_scores, query_h, TN, preferred_element_type=jnp.float32)
            term_v = lax.dot_general(probs_low, grad_h, TN, preferred_element_type=jnp.float32)
            grad_k = term_k if grad_k is None else grad_k + term_k
            grad_v = term_v if grad_v is None else grad_v + term_v
        dkv_ref[:, k_cols] = grad_k
        dkv_ref[:, v_cols] = grad_v
    def slot_rows(index):
        return dkv_ref[pl.ds(index * block_rows, block_rows), :]

    if chip_outputs:
        mate_ref, other_ref, two_ref, own_ref = out_refs
        two_ref[...] = slot_rows(1)
        own_ref[...] = slot_rows(3)

        @pl.when(flag == 0)
        def _():
            mate_ref[...] = slot_rows(2).astype(mate_ref.dtype)
            other_ref[...] = slot_rows(0).astype(other_ref.dtype)

        @pl.when(flag != 0)
        def _():
            mate_ref[...] = slot_rows(0).astype(mate_ref.dtype)
            other_ref[...] = slot_rows(2).astype(other_ref.dtype)

    else:
        for index, out_ref in enumerate(out_refs):
            out_ref[...] = slot_rows(index)


def attention(
    flag, lo_rel, queries, grads, kv_blocks, slots, heads, kv_heads, margin, early, chip_outputs
):
    rows, width = queries.shape
    blocks = len(kv_blocks)
    block_rows, kv_cols = kv_blocks[0].shape
    keys = len(slots) * block_rows
    kernel = functools.partial(
        attention_kernel,
        heads=heads,
        kv_heads=kv_heads,
        margin=margin,
        slots=tuple(slots),
        blocks=blocks,
        chip_outputs=chip_outputs,
    )
    if chip_outputs:
        piece_types = [jnp.bfloat16, jnp.bfloat16, jnp.float32, jnp.float32]
    else:
        piece_types = [jnp.float32] * len(slots)
    vmem = pl.BlockSpec(memory_space=pltpu.VMEM)
    smem = pl.BlockSpec(memory_space=pltpu.SMEM)
    flops = 2 * 5 * heads * rows * keys * HEAD_DIM
    moved = 2 * (2 * rows * width + keys * kv_cols + rows * width) + 4 * keys * kv_cols
    return pl.pallas_call(
        kernel,
        out_shape=(jax.ShapeDtypeStruct((rows, width), jnp.bfloat16),)
        + tuple(jax.ShapeDtypeStruct((block_rows, kv_cols), kind) for kind in piece_types),
        in_specs=[smem] + [vmem] * (3 + blocks) + [pl.BlockSpec(memory_space=pl.ANY)] * len(early),
        out_specs=(vmem,) * (1 + len(slots)),
        scratch_shapes=[
            pltpu.VMEM((keys, kv_cols), kv_blocks[0].dtype),
            pltpu.VMEM((keys, kv_cols), jnp.float32),
        ],
        cost_estimate=pl.CostEstimate(
            flops=flops, transcendentals=heads * rows * keys, bytes_accessed=moved
        ),
    )(flag, lo_rel, queries, grads, *kv_blocks, *early)


def body(layer_input, query_heads, key_heads, value_heads, grad_out, doc_starts):
    block_rows = query_heads.shape[1]
    window = min(SPAN, lax.axis_size(RING) * block_rows // 2)
    reach = (window + block_rows - 2) // block_rows
    margin = reach * block_rows
    kv_width = key_heads.shape[2]
    heads = query_heads.shape[2] // HEAD_DIM
    kv_heads = kv_width // HEAD_DIM
    first_row = lax.axis_index(RING) * block_rows

    fsdp_count = lax.axis_size("fsdp")
    fsdp_at = lax.axis_index("fsdp")
    model_width = layer_input.shape[2]
    shard_rows = model_width // fsdp_count
    own_input = layer_input[0]
    inputs = [lax.dynamic_slice_in_dim(own_input, fsdp_at * shard_rows, shard_rows, axis=1)]
    for steps in range(1, fsdp_count):
        target = (fsdp_at + steps) % fsdp_count
        outgoing = lax.dynamic_slice_in_dim(own_input, target * shard_rows, shard_rows, axis=1)
        inputs.append(rotated(outgoing, "fsdp", steps))

    own_kv = jnp.concatenate([key_heads[0], value_heads[0]], axis=1)
    query_pos = first_row + jnp.arange(block_rows, dtype=jnp.int32)
    lowest = jnp.maximum(doc_start_of(doc_starts[0], query_pos), query_pos - window + 1)
    lo_rel = (lowest - first_row + margin).astype(jnp.int32)[:, None]
    sub_count = lax.axis_size("sub")
    sub_at = lax.axis_index("sub")
    flag = jnp.reshape(sub_at, (1,)).astype(jnp.int32)
    chip_route = sub_count == 2 and reach == 3
    if chip_route:
        ring_count = lax.axis_size(RING)
        across = [(2 * chip - 3, 2 * chip) for chip in range(2, ring_count // 2)]
        two_back = passed_along(own_kv, "ctx", 1)
        one_back_high = passed_along(own_kv, "sub", 1)
        three_back_low = lax.ppermute(own_kv, RING, across)
        swapped = rotated(two_back, "sub", 1)
        kv_blocks = [two_back, one_back_high, three_back_low, swapped, own_kv]
        slots = [(2, 3), (0, 0), (3, 1), (4, 4)]
    else:
        arrived = []
        moving = own_kv
        for _ in range(reach):
            moving = passed_along(moving, RING, 1)
            arrived.append(moving)
        kv_blocks = arrived[::-1] + [own_kv]
        slots = [(index, index) for index in range(reach + 1)]
    grad_q, *grad_pieces = attention(
        flag, lo_rel, query_heads[0], grad_out[0], kv_blocks, slots, heads, kv_heads, margin,
        inputs[1:],
        chip_route,
    )

    def low(value):
        return value.astype(jnp.bfloat16)

    if chip_route:
        back = [(target, source) for source, target in across]
        to_mate, to_other, g2, g0 = grad_pieces
        from_far = lax.ppermute(to_other, RING, back).astype(jnp.float32)
        from_mate = rotated(to_mate, "sub", 1).astype(jnp.float32)
        from_high = passed_along(to_other, "sub", -1).astype(jnp.float32)
        two_back_sum = g2 + from_mate
        from_next = passed_along(low(two_back_sum), "ctx", -1).astype(jnp.float32)
        total = g0 + from_high + from_far + from_next
    else:

        def own_piece(distance):
            return grad_pieces[reach - distance]

        total = own_piece(reach)
        for distance in range(reach - 1, -1, -1):
            moved = passed_along(low(total), RING, -1).astype(jnp.float32)
            total = moved + own_piece(distance)
    grad_kv = total.astype(jnp.bfloat16)
    grad_key = grad_kv[:, :kv_width]
    grad_value = grad_kv[:, kv_width:]

    values = [grad_value]
    for steps in range(1, fsdp_count):
        values.append(rotated(grad_value, "fsdp", steps))
    stacked_inputs = jnp.concatenate(inputs, axis=0)
    stacked_values = jnp.concatenate(values, axis=0)
    shard = lax.dot_general(stacked_inputs, stacked_values, TN, preferred_element_type=jnp.float32)
    token_scale = float(fsdp_count * lax.axis_size(RING) * block_rows) ** (-0.5)
    scale_early = token_scale == 2.0 ** round(math.log2(token_scale))
    if scale_early:
        shard = shard * token_scale

    sub_count = lax.axis_size("sub")
    sub_at = lax.axis_index("sub")
    piece_rows = shard_rows // sub_count
    mine = lax.dynamic_slice_in_dim(shard, sub_at * piece_rows, piece_rows, axis=0)
    for steps in range(1, sub_count):
        target = (sub_at + steps) % sub_count
        outgoing = lax.dynamic_slice_in_dim(shard, target * piece_rows, piece_rows, axis=0)
        mine = mine + rotated(outgoing.astype(jnp.bfloat16), "sub", steps).astype(jnp.float32)
    reduced = ring_sum(mine, "ctx")
    if sub_count == 2:
        other = rotated(reduced.astype(jnp.bfloat16), "sub", 1).astype(jnp.float32)
        first = jnp.where(sub_at == 0, reduced, other)
        second = jnp.where(sub_at == 0, other, reduced)
        weight_v = jnp.concatenate([first, second], axis=0)
    else:
        weight_v = lax.all_gather(reduced, "sub", axis=0, tiled=True)
    if not scale_early:
        weight_v = weight_v * token_scale
    return (
        grad_q[None],
        grad_key[None],
        grad_value[None],
        weight_v,
    )


def solution(mesh):
    placed = (
        P(("groups", "fsdp"), ("ctx", "sub"), None),
        P(("groups", "fsdp"), ("ctx", "sub"), None),
        P(("groups", "fsdp"), ("ctx", "sub"), None),
        P(("groups", "fsdp"), ("ctx", "sub"), None),
        P(("groups", "fsdp"), ("ctx", "sub"), None),
        P(("groups", "fsdp"), None),
    )
    return jax.shard_map(
        body,
        mesh=mesh,
        in_specs=placed,
        out_specs=(
            P(("groups", "fsdp"), ("ctx", "sub"), None),
            P(("groups", "fsdp"), ("ctx", "sub"), None),
            P(("groups", "fsdp"), ("ctx", "sub"), None),
            P(("groups", "fsdp"), None),
        ),
        check_vma=False,
    )
```

```python
import functools
import math

import jax
import jax.numpy as jnp
from jax import lax
from jax.experimental import pallas as pl
from jax.experimental.pallas import tpu as pltpu
from jax.sharding import PartitionSpec as P

HEAD_DIM = 256
SPAN = 768
RING = ("ctx", "sub")
NT = (((1,), (1,)), ((), ()))
TN = (((0,), (0,)), ((), ()))


def passed_along(value, axis, steps):
    count = lax.axis_size(axis)
    first, last = (max(0, -steps), min(count, count - steps))
    return lax.ppermute(value, axis, [(source, source + steps) for source in range(first, last)])


def rotated(value, axis, steps):
    count = lax.axis_size(axis)
    return lax.ppermute(value, axis, [(source, (source + steps) % count) for source in range(count)])


def ring_sum(piece, axis):
    count = lax.axis_size(axis)
    at = lax.axis_index(axis)
    rows = piece.shape[0] // count
    total = lax.dynamic_slice_in_dim(piece, at * rows, rows, axis=0)
    for steps in range(1, count):
        outgoing = lax.dynamic_slice_in_dim(piece, ((at + steps) % count) * rows, rows, axis=0)
        total = total + rotated(outgoing.astype(jnp.bfloat16), axis, steps).astype(jnp.float32)
    low = total.astype(jnp.bfloat16)
    gathered = jnp.zeros(piece.shape, jnp.float32)
    gathered = lax.dynamic_update_slice_in_dim(gathered, total, at * rows, axis=0)
    for steps in range(1, count):
        arrived = rotated(low, axis, steps).astype(jnp.float32)
        gathered = lax.dynamic_update_slice_in_dim(
            gathered, arrived, ((at - steps) % count) * rows, axis=0
        )
    return gathered


def doc_start_of(starts, positions):
    covered = starts[None, :] <= positions[:, None]
    return jnp.max(jnp.where(covered, starts[None, :], 0), axis=1)


def attention_kernel(*refs, heads, kv_heads, margin, slots, blocks, chip_outputs):
    flag_ref, lo_ref, q_ref, do_ref = refs[:4]
    block_refs = refs[4 : 4 + blocks]
    kv_ref, dkv_ref = refs[-2:]
    outs = refs[-3 - len(slots) : -2]
    dq_ref = outs[0]
    out_refs = outs[1:]
    block_rows = block_refs[0].shape[0]
    flag = flag_ref[0]
    for index, (when_low, when_high) in enumerate(slots):
        target = kv_ref.at[pl.ds(index * block_rows, block_rows), :]
        if when_low == when_high:
            target[...] = block_refs[when_low][...]
        else:

            @pl.when(flag == 0)
            def _():
                target[...] = block_refs[when_low][...]

            @pl.when(flag != 0)
            def _():
                target[...] = block_refs[when_high][...]

    rows = q_ref.shape[0]
    keys = kv_ref.shape[0]
    scale = HEAD_DIM ** (-0.5)
    kv_width = kv_heads * HEAD_DIM
    per_group = heads // kv_heads
    col = lax.broadcasted_iota(jnp.int32, (rows, keys), 1)
    row = lax.broadcasted_iota(jnp.int32, (rows, keys), 0)
    allowed = (col >= lo_ref[...]) & (col <= row + margin)
    for group in range(kv_heads):
        k_cols = pl.ds(group * HEAD_DIM, HEAD_DIM)
        v_cols = pl.ds(kv_width + group * HEAD_DIM, HEAD_DIM)
        key_g = kv_ref[:, k_cols]
        value_g = kv_ref[:, v_cols]
        grad_k = None
        grad_v = None
        for member in range(per_group):
            q_cols = pl.ds((group * per_group + member) * HEAD_DIM, HEAD_DIM)
            query_h = q_ref[:, q_cols]
            grad_h = do_ref[:, q_cols]
            scores = lax.dot_general(query_h, key_g, NT, preferred_element_type=jnp.float32) * scale
            scores = jnp.where(allowed, scores, -1e30)
            largest = jnp.max(scores, axis=1, keepdims=True)
            raised = jnp.exp(scores - largest)
            probs = raised * (1.0 / jnp.sum(raised, axis=1, keepdims=True))
            grad_probs = lax.dot_general(grad_h, value_g, NT, preferred_element_type=jnp.float32)
            row_dot = jnp.sum(probs * grad_probs, axis=1, keepdims=True)
            grad_scores = (probs * (grad_probs - row_dot) * scale).astype(jnp.bfloat16)
            probs_low = probs.astype(jnp.bfloat16)
            dq_ref[:, q_cols] = jnp.dot(
                grad_scores, key_g, preferred_element_type=jnp.float32
            ).astype(dq_ref.dtype)
            term_k = lax.dot_general(grad_scores, query_h, TN, preferred_element_type=jnp.float32)
            term_v = lax.dot_general(probs_low, grad_h, TN, preferred_element_type=jnp.float32)
            grad_k = term_k if grad_k is None else grad_k + term_k
            grad_v = term_v if grad_v is None else grad_v + term_v
        dkv_ref[:, k_cols] = grad_k
        dkv_ref[:, v_cols] = grad_v
    def slot_rows(index):
        return dkv_ref[pl.ds(index * block_rows, block_rows), :]

    if chip_outputs:
        mate_ref, other_ref, two_ref, own_ref = out_refs
        two_ref[...] = slot_rows(1)
        own_ref[...] = slot_rows(3)

        @pl.when(flag == 0)
        def _():
            mate_ref[...] = slot_rows(2).astype(mate_ref.dtype)
            other_ref[...] = slot_rows(0).astype(other_ref.dtype)

        @pl.when(flag != 0)
        def _():
            mate_ref[...] = slot_rows(0).astype(mate_ref.dtype)
            other_ref[...] = slot_rows(2).astype(other_ref.dtype)

    else:
        for index, out_ref in enumerate(out_refs):
            out_ref[...] = slot_rows(index)


def attention(
    flag, lo_rel, queries, grads, kv_blocks, slots, heads, kv_heads, margin, early, chip_outputs
):
    rows, width = queries.shape
    blocks = len(kv_blocks)
    block_rows, kv_cols = kv_blocks[0].shape
    keys = len(slots) * block_rows
    kernel = functools.partial(
        attention_kernel,
        heads=heads,
        kv_heads=kv_heads,
        margin=margin,
        slots=tuple(slots),
        blocks=blocks,
        chip_outputs=chip_outputs,
    )
    if chip_outputs:
        piece_types = [jnp.bfloat16, jnp.bfloat16, jnp.float32, jnp.float32]
    else:
        piece_types = [jnp.float32] * len(slots)
    vmem = pl.BlockSpec(memory_space=pltpu.VMEM)
    smem = pl.BlockSpec(memory_space=pltpu.SMEM)
    flops = 2 * 5 * heads * rows * keys * HEAD_DIM
    moved = 2 * (2 * rows * width + keys * kv_cols + rows * width) + 4 * keys * kv_cols
    return pl.pallas_call(
        kernel,
        out_shape=(jax.ShapeDtypeStruct((rows, width), jnp.bfloat16),)
        + tuple(jax.ShapeDtypeStruct((block_rows, kv_cols), kind) for kind in piece_types),
        in_specs=[smem] + [vmem] * (3 + blocks) + [pl.BlockSpec(memory_space=pl.ANY)] * len(early),
        out_specs=(vmem,) * (1 + len(slots)),
        scratch_shapes=[
            pltpu.VMEM((keys, kv_cols), kv_blocks[0].dtype),
            pltpu.VMEM((keys, kv_cols), jnp.float32),
        ],
        cost_estimate=pl.CostEstimate(
            flops=flops, transcendentals=heads * rows * keys, bytes_accessed=moved
        ),
    )(flag, lo_rel, queries, grads, *kv_blocks, *early)


def body(layer_input, query_heads, key_heads, value_heads, grad_out, doc_starts):
    block_rows = query_heads.shape[1]
    window = min(SPAN, lax.axis_size(RING) * block_rows // 2)
    reach = (window + block_rows - 2) // block_rows
    margin = reach * block_rows
    kv_width = key_heads.shape[2]
    heads = query_heads.shape[2] // HEAD_DIM
    kv_heads = kv_width // HEAD_DIM
    first_row = lax.axis_index(RING) * block_rows

    fsdp_count = lax.axis_size("fsdp")
    fsdp_at = lax.axis_index("fsdp")
    model_width = layer_input.shape[2]
    shard_rows = model_width // fsdp_count
    own_input = layer_input[0]
    inputs = [lax.dynamic_slice_in_dim(own_input, fsdp_at * shard_rows, shard_rows, axis=1)]
    for steps in range(1, fsdp_count):
        target = (fsdp_at + steps) % fsdp_count
        outgoing = lax.dynamic_slice_in_dim(own_input, target * shard_rows, shard_rows, axis=1)
        inputs.append(rotated(outgoing, "fsdp", steps))

    query_pos = first_row + jnp.arange(block_rows, dtype=jnp.int32)
    lowest = jnp.maximum(doc_start_of(doc_starts[0], query_pos), query_pos - window + 1)
    lo_rel = (lowest - first_row + margin).astype(jnp.int32)[:, None]
    sub_count = lax.axis_size("sub")
    sub_at = lax.axis_index("sub")
    flag = jnp.reshape(sub_at, (1,)).astype(jnp.int32)
    chip_route = sub_count == 2 and reach == 3
    ring_count = lax.axis_size(RING)
    across = [(2 * chip - 3, 2 * chip) for chip in range(2, ring_count // 2)]
    back = [(target, source) for source, target in across]
    per_group = heads // kv_heads

    def low(value):
        return value.astype(jnp.bfloat16)

    def forward_halo(own_kv):
        if chip_route:
            two_back = passed_along(own_kv, "ctx", 1)
            one_back_high = passed_along(own_kv, "sub", 1)
            three_back_low = lax.ppermute(own_kv, RING, across)
            swapped = rotated(two_back, "sub", 1)
            return [two_back, one_back_high, three_back_low, swapped, own_kv]
        arrived = []
        moving = own_kv
        for _ in range(reach):
            moving = passed_along(moving, RING, 1)
            arrived.append(moving)
        return arrived[::-1] + [own_kv]

    if chip_route:
        slots = [(2, 3), (0, 0), (3, 1), (4, 4)]
    else:
        slots = [(index, index) for index in range(reach + 1)]

    def backward_halo(grad_pieces):
        if chip_route:
            to_mate, to_other, g2, g0 = grad_pieces
            from_far = lax.ppermute(to_other, RING, back).astype(jnp.float32)
            from_mate = rotated(to_mate, "sub", 1).astype(jnp.float32)
            from_high = passed_along(to_other, "sub", -1).astype(jnp.float32)
            two_back_sum = g2 + from_mate
            from_next = passed_along(low(two_back_sum), "ctx", -1).astype(jnp.float32)
            return g0 + from_high + from_far + from_next
        total = grad_pieces[0]
        for distance in range(reach - 1, -1, -1):
            moved = passed_along(low(total), RING, -1).astype(jnp.float32)
            total = moved + grad_pieces[reach - distance]
        return total

    grad_q_parts, key_parts, value_parts = [], [], []
    previous = None
    for group in range(kv_heads):
        k_cols = slice(group * HEAD_DIM, (group + 1) * HEAD_DIM)
        q_cols = slice(group * per_group * HEAD_DIM, (group + 1) * per_group * HEAD_DIM)
        own_kv = jnp.concatenate([key_heads[0][:, k_cols], value_heads[0][:, k_cols]], axis=1)
        if previous is not None:
            own_kv, _ = lax.optimization_barrier((own_kv, previous))
        kv_blocks = forward_halo(own_kv)
        previous = kv_blocks[:-1]
        grad_q_g, *grad_pieces = attention(
            flag, lo_rel, query_heads[0][:, q_cols], grad_out[0][:, q_cols], kv_blocks, slots,
            per_group, 1, margin, inputs[1:] if group == 0 else [], chip_route,
        )
        total = low(backward_halo(grad_pieces))
        grad_q_parts.append(grad_q_g)
        key_parts.append(total[:, :HEAD_DIM])
        value_parts.append(total[:, HEAD_DIM:])
    grad_q = jnp.concatenate(grad_q_parts, axis=1)
    grad_key = jnp.concatenate(key_parts, axis=1)
    grad_value = jnp.concatenate(value_parts, axis=1)

    values = [grad_value]
    for steps in range(1, fsdp_count):
        values.append(rotated(grad_value, "fsdp", steps))
    stacked_inputs = jnp.concatenate(inputs, axis=0)
    stacked_values = jnp.concatenate(values, axis=0)
    shard = lax.dot_general(stacked_inputs, stacked_values, TN, preferred_element_type=jnp.float32)
    token_scale = float(fsdp_count * lax.axis_size(RING) * block_rows) ** (-0.5)
    scale_early = token_scale == 2.0 ** round(math.log2(token_scale))
    if scale_early:
        shard = shard * token_scale

    piece_rows = shard_rows // sub_count
    mine = lax.dynamic_slice_in_dim(shard, sub_at * piece_rows, piece_rows, axis=0)
    for steps in range(1, sub_count):
        target = (sub_at + steps) % sub_count
        outgoing = lax.dynamic_slice_in_dim(shard, target * piece_rows, piece_rows, axis=0)
        mine = mine + rotated(outgoing.astype(jnp.bfloat16), "sub", steps).astype(jnp.float32)
    reduced = ring_sum(mine, "ctx")
    if sub_count == 2:
        other = rotated(reduced.astype(jnp.bfloat16), "sub", 1).astype(jnp.float32)
        first = jnp.where(sub_at == 0, reduced, other)
        second = jnp.where(sub_at == 0, other, reduced)
        weight_v = jnp.concatenate([first, second], axis=0)
    else:
        weight_v = lax.all_gather(reduced, "sub", axis=0, tiled=True)
    if not scale_early:
        weight_v = weight_v * token_scale
    return (
        grad_q[None],
        grad_key[None],
        grad_value[None],
        weight_v,
    )


def solution(mesh):
    placed = (
        P(("groups", "fsdp"), ("ctx", "sub"), None),
        P(("groups", "fsdp"), ("ctx", "sub"), None),
        P(("groups", "fsdp"), ("ctx", "sub"), None),
        P(("groups", "fsdp"), ("ctx", "sub"), None),
        P(("groups", "fsdp"), ("ctx", "sub"), None),
        P(("groups", "fsdp"), None),
    )
    return jax.shard_map(
        body,
        mesh=mesh,
        in_specs=placed,
        out_specs=(
            P(("groups", "fsdp"), ("ctx", "sub"), None),
            P(("groups", "fsdp"), ("ctx", "sub"), None),
            P(("groups", "fsdp"), ("ctx", "sub"), None),
            P(("groups", "fsdp"), None),
        ),
        check_vma=False,
    )
```

```python
import functools
import math

import jax
import jax.numpy as jnp
from jax import lax
from jax.experimental import pallas as pl
from jax.experimental.pallas import tpu as pltpu
from jax.sharding import PartitionSpec as P

HEAD_DIM = 256
SPAN = 768
RING = ("ctx", "sub")
NT = (((1,), (1,)), ((), ()))
TN = (((0,), (0,)), ((), ()))


def passed_along(value, axis, steps):
    count = lax.axis_size(axis)
    first, last = (max(0, -steps), min(count, count - steps))
    return lax.ppermute(value, axis, [(source, source + steps) for source in range(first, last)])


def rotated(value, axis, steps):
    count = lax.axis_size(axis)
    return lax.ppermute(value, axis, [(source, (source + steps) % count) for source in range(count)])


def ring_sum(piece, axis):
    count = lax.axis_size(axis)
    at = lax.axis_index(axis)
    rows = piece.shape[0] // count
    total = lax.dynamic_slice_in_dim(piece, at * rows, rows, axis=0)
    for steps in range(1, count):
        outgoing = lax.dynamic_slice_in_dim(piece, ((at + steps) % count) * rows, rows, axis=0)
        total = total + rotated(outgoing.astype(jnp.bfloat16), axis, steps).astype(jnp.float32)
    low = total.astype(jnp.bfloat16)
    gathered = jnp.zeros(piece.shape, jnp.float32)
    gathered = lax.dynamic_update_slice_in_dim(gathered, total, at * rows, axis=0)
    for steps in range(1, count):
        arrived = rotated(low, axis, steps).astype(jnp.float32)
        gathered = lax.dynamic_update_slice_in_dim(
            gathered, arrived, ((at - steps) % count) * rows, axis=0
        )
    return gathered


def doc_start_of(starts, positions):
    covered = starts[None, :] <= positions[:, None]
    return jnp.max(jnp.where(covered, starts[None, :], 0), axis=1)


def attention_kernel(*refs, heads, kv_heads, margin, slots, blocks, chip_outputs):
    flag_ref, lo_ref, q_ref, do_ref = refs[:4]
    block_refs = refs[4 : 4 + blocks]
    kv_ref, dkv_ref = refs[-2:]
    outs = refs[-3 - len(slots) : -2]
    dq_ref = outs[0]
    out_refs = outs[1:]
    block_rows = block_refs[0].shape[0]
    flag = flag_ref[0]
    for index, (when_low, when_high) in enumerate(slots):
        target = kv_ref.at[pl.ds(index * block_rows, block_rows), :]
        if when_low == when_high:
            target[...] = block_refs[when_low][...]
        else:

            @pl.when(flag == 0)
            def _():
                target[...] = block_refs[when_low][...]

            @pl.when(flag != 0)
            def _():
                target[...] = block_refs[when_high][...]

    rows = q_ref.shape[0]
    keys = kv_ref.shape[0]
    scale = HEAD_DIM ** (-0.5)
    kv_width = kv_heads * HEAD_DIM
    per_group = heads // kv_heads
    col = lax.broadcasted_iota(jnp.int32, (rows, keys), 1)
    row = lax.broadcasted_iota(jnp.int32, (rows, keys), 0)
    allowed = (col >= lo_ref[...]) & (col <= row + margin)
    for group in range(kv_heads):
        k_cols = pl.ds(group * HEAD_DIM, HEAD_DIM)
        v_cols = pl.ds(kv_width + group * HEAD_DIM, HEAD_DIM)
        key_g = kv_ref[:, k_cols]
        value_g = kv_ref[:, v_cols]
        grad_k = None
        grad_v = None
        for member in range(per_group):
            q_cols = pl.ds((group * per_group + member) * HEAD_DIM, HEAD_DIM)
            query_h = q_ref[:, q_cols]
            grad_h = do_ref[:, q_cols]
            scores = lax.dot_general(query_h, key_g, NT, preferred_element_type=jnp.float32) * scale
            scores = jnp.where(allowed, scores, -1e30)
            largest = jnp.max(scores, axis=1, keepdims=True)
            raised = jnp.exp(scores - largest)
            probs = raised * (1.0 / jnp.sum(raised, axis=1, keepdims=True))
            grad_probs = lax.dot_general(grad_h, value_g, NT, preferred_element_type=jnp.float32)
            row_dot = jnp.sum(probs * grad_probs, axis=1, keepdims=True)
            grad_scores = (probs * (grad_probs - row_dot) * scale).astype(jnp.bfloat16)
            probs_low = probs.astype(jnp.bfloat16)
            dq_ref[:, q_cols] = jnp.dot(
                grad_scores, key_g, preferred_element_type=jnp.float32
            ).astype(dq_ref.dtype)
            term_k = lax.dot_general(grad_scores, query_h, TN, preferred_element_type=jnp.float32)
            term_v = lax.dot_general(probs_low, grad_h, TN, preferred_element_type=jnp.float32)
            grad_k = term_k if grad_k is None else grad_k + term_k
            grad_v = term_v if grad_v is None else grad_v + term_v
        dkv_ref[:, k_cols] = grad_k
        dkv_ref[:, v_cols] = grad_v
    def slot_rows(index):
        return dkv_ref[pl.ds(index * block_rows, block_rows), :]

    if chip_outputs:
        mate_ref, other_ref, two_ref, own_ref = out_refs
        two_ref[...] = slot_rows(1)
        own_ref[...] = slot_rows(3)

        @pl.when(flag == 0)
        def _():
            mate_ref[...] = slot_rows(2).astype(mate_ref.dtype)
            other_ref[...] = slot_rows(0).astype(other_ref.dtype)

        @pl.when(flag != 0)
        def _():
            mate_ref[...] = slot_rows(0).astype(mate_ref.dtype)
            other_ref[...] = slot_rows(2).astype(other_ref.dtype)

    else:
        for index, out_ref in enumerate(out_refs):
            out_ref[...] = slot_rows(index)


def attention(
    flag, lo_rel, queries, grads, kv_blocks, slots, heads, kv_heads, margin, early, chip_outputs
):
    rows, width = queries.shape
    blocks = len(kv_blocks)
    block_rows, kv_cols = kv_blocks[0].shape
    keys = len(slots) * block_rows
    kernel = functools.partial(
        attention_kernel,
        heads=heads,
        kv_heads=kv_heads,
        margin=margin,
        slots=tuple(slots),
        blocks=blocks,
        chip_outputs=chip_outputs,
    )
    if chip_outputs:
        piece_types = [jnp.bfloat16, jnp.bfloat16, jnp.float32, jnp.float32]
    else:
        piece_types = [jnp.float32] * len(slots)
    vmem = pl.BlockSpec(memory_space=pltpu.VMEM)
    smem = pl.BlockSpec(memory_space=pltpu.SMEM)
    flops = 2 * 5 * heads * rows * keys * HEAD_DIM
    moved = 2 * (2 * rows * width + keys * kv_cols + rows * width) + 4 * keys * kv_cols
    return pl.pallas_call(
        kernel,
        out_shape=(jax.ShapeDtypeStruct((rows, width), jnp.bfloat16),)
        + tuple(jax.ShapeDtypeStruct((block_rows, kv_cols), kind) for kind in piece_types),
        in_specs=[smem] + [vmem] * (3 + blocks) + [pl.BlockSpec(memory_space=pl.ANY)] * len(early),
        out_specs=(vmem,) * (1 + len(slots)),
        scratch_shapes=[
            pltpu.VMEM((keys, kv_cols), kv_blocks[0].dtype),
            pltpu.VMEM((keys, kv_cols), jnp.float32),
        ],
        cost_estimate=pl.CostEstimate(
            flops=flops, transcendentals=heads * rows * keys, bytes_accessed=moved
        ),
    )(flag, lo_rel, queries, grads, *kv_blocks, *early)


def body(layer_input, query_heads, key_heads, value_heads, grad_out, doc_starts):
    block_rows = query_heads.shape[1]
    window = min(SPAN, lax.axis_size(RING) * block_rows // 2)
    reach = (window + block_rows - 2) // block_rows
    margin = reach * block_rows
    kv_width = key_heads.shape[2]
    heads = query_heads.shape[2] // HEAD_DIM
    kv_heads = kv_width // HEAD_DIM
    first_row = lax.axis_index(RING) * block_rows

    fsdp_count = lax.axis_size("fsdp")
    fsdp_at = lax.axis_index("fsdp")
    model_width = layer_input.shape[2]
    shard_rows = model_width // fsdp_count
    own_input = layer_input[0]
    inputs = [lax.dynamic_slice_in_dim(own_input, fsdp_at * shard_rows, shard_rows, axis=1)]
    for steps in range(1, fsdp_count):
        target = (fsdp_at + steps) % fsdp_count
        outgoing = lax.dynamic_slice_in_dim(own_input, target * shard_rows, shard_rows, axis=1)
        inputs.append(rotated(outgoing, "fsdp", steps))

    query_pos = first_row + jnp.arange(block_rows, dtype=jnp.int32)
    lowest = jnp.maximum(doc_start_of(doc_starts[0], query_pos), query_pos - window + 1)
    lo_rel = (lowest - first_row + margin).astype(jnp.int32)[:, None]
    sub_count = lax.axis_size("sub")
    sub_at = lax.axis_index("sub")
    flag = jnp.reshape(sub_at, (1,)).astype(jnp.int32)
    chip_route = sub_count == 2 and reach == 3
    ring_count = lax.axis_size(RING)
    across = [(2 * chip - 3, 2 * chip) for chip in range(2, ring_count // 2)]
    back = [(target, source) for source, target in across]
    per_group = heads // kv_heads

    def low(value):
        return value.astype(jnp.bfloat16)

    def forward_halo(own_kv):
        if chip_route:
            two_back = passed_along(own_kv, "ctx", 1)
            one_back_high = passed_along(own_kv, "sub", 1)
            three_back_low = lax.ppermute(own_kv, RING, across)
            swapped = rotated(two_back, "sub", 1)
            return [two_back, one_back_high, three_back_low, swapped, own_kv]
        arrived = []
        moving = own_kv
        for _ in range(reach):
            moving = passed_along(moving, RING, 1)
            arrived.append(moving)
        return arrived[::-1] + [own_kv]

    if chip_route:
        slots = [(2, 3), (0, 0), (3, 1), (4, 4)]
    else:
        slots = [(index, index) for index in range(reach + 1)]

    def backward_halo(grad_pieces):
        if chip_route:
            to_mate, to_other, g2, g0 = grad_pieces
            from_far = lax.ppermute(to_other, RING, back).astype(jnp.float32)
            from_mate = rotated(to_mate, "sub", 1).astype(jnp.float32)
            from_high = passed_along(to_other, "sub", -1).astype(jnp.float32)
            two_back_sum = g2 + from_mate
            from_next = passed_along(low(two_back_sum), "ctx", -1).astype(jnp.float32)
            return g0 + from_high + from_far + from_next
        total = grad_pieces[0]
        for distance in range(reach - 1, -1, -1):
            moved = passed_along(low(total), RING, -1).astype(jnp.float32)
            total = moved + grad_pieces[reach - distance]
        return total

    grad_q_parts, key_parts, value_parts = [], [], []
    previous = None
    for group in range(kv_heads):
        k_cols = slice(group * HEAD_DIM, (group + 1) * HEAD_DIM)
        q_cols = slice(group * per_group * HEAD_DIM, (group + 1) * per_group * HEAD_DIM)
        own_kv = jnp.concatenate([key_heads[0][:, k_cols], value_heads[0][:, k_cols]], axis=1)
        if previous is not None:
            own_kv, _ = lax.optimization_barrier((own_kv, previous))
        kv_blocks = forward_halo(own_kv)
        if key_parts:
            kv_blocks, _ = lax.optimization_barrier((kv_blocks, (key_parts[-1], value_parts[-1])))
        grad_q_g, *grad_pieces = attention(
            flag, lo_rel, query_heads[0][:, q_cols], grad_out[0][:, q_cols], kv_blocks, slots,
            per_group, 1, margin, inputs[1:] if group == 0 else [], chip_route,
        )
        previous = grad_q_g
        total = low(backward_halo(grad_pieces))
        grad_q_parts.append(grad_q_g)
        key_parts.append(total[:, :HEAD_DIM])
        value_parts.append(total[:, HEAD_DIM:])
    grad_q = jnp.concatenate(grad_q_parts, axis=1)
    grad_key = jnp.concatenate(key_parts, axis=1)
    grad_value = jnp.concatenate(value_parts, axis=1)

    values = [grad_value]
    for steps in range(1, fsdp_count):
        values.append(rotated(grad_value, "fsdp", steps))
    stacked_inputs = jnp.concatenate(inputs, axis=0)
    stacked_values = jnp.concatenate(values, axis=0)
    shard = lax.dot_general(stacked_inputs, stacked_values, TN, preferred_element_type=jnp.float32)
    token_scale = float(fsdp_count * lax.axis_size(RING) * block_rows) ** (-0.5)
    scale_early = token_scale == 2.0 ** round(math.log2(token_scale))
    if scale_early:
        shard = shard * token_scale

    piece_rows = shard_rows // sub_count
    mine = lax.dynamic_slice_in_dim(shard, sub_at * piece_rows, piece_rows, axis=0)
    for steps in range(1, sub_count):
        target = (sub_at + steps) % sub_count
        outgoing = lax.dynamic_slice_in_dim(shard, target * piece_rows, piece_rows, axis=0)
        mine = mine + rotated(outgoing.astype(jnp.bfloat16), "sub", steps).astype(jnp.float32)
    reduced = ring_sum(mine, "ctx")
    if sub_count == 2:
        other = rotated(reduced.astype(jnp.bfloat16), "sub", 1).astype(jnp.float32)
        first = jnp.where(sub_at == 0, reduced, other)
        second = jnp.where(sub_at == 0, other, reduced)
        weight_v = jnp.concatenate([first, second], axis=0)
    else:
        weight_v = lax.all_gather(reduced, "sub", axis=0, tiled=True)
    if not scale_early:
        weight_v = weight_v * token_scale
    return (
        grad_q[None],
        grad_key[None],
        grad_value[None],
        weight_v,
    )


def solution(mesh):
    placed = (
        P(("groups", "fsdp"), ("ctx", "sub"), None),
        P(("groups", "fsdp"), ("ctx", "sub"), None),
        P(("groups", "fsdp"), ("ctx", "sub"), None),
        P(("groups", "fsdp"), ("ctx", "sub"), None),
        P(("groups", "fsdp"), ("ctx", "sub"), None),
        P(("groups", "fsdp"), None),
    )
    return jax.shard_map(
        body,
        mesh=mesh,
        in_specs=placed,
        out_specs=(
            P(("groups", "fsdp"), ("ctx", "sub"), None),
            P(("groups", "fsdp"), ("ctx", "sub"), None),
            P(("groups", "fsdp"), ("ctx", "sub"), None),
            P(("groups", "fsdp"), None),
        ),
        check_vma=False,
    )
```

```python
import functools
import math

import jax
import jax.numpy as jnp
from jax import lax
from jax.experimental import pallas as pl
from jax.experimental.pallas import tpu as pltpu
from jax.sharding import PartitionSpec as P

HEAD_DIM = 256
SPAN = 768
RING = ("ctx", "sub")
TRADE = ("fsdp", "sub")
NT = (((1,), (1,)), ((), ()))
TN = (((0,), (0,)), ((), ()))


def passed_along(value, axis, steps):
    count = lax.axis_size(axis)
    first, last = (max(0, -steps), min(count, count - steps))
    return lax.ppermute(value, axis, [(source, source + steps) for source in range(first, last)])


def rotated(value, axis, steps):
    count = lax.axis_size(axis)
    return lax.ppermute(value, axis, [(source, (source + steps) % count) for source in range(count)])


def ring_sum(piece, axis):
    count = lax.axis_size(axis)
    at = lax.axis_index(axis)
    rows = piece.shape[0] // count
    total = lax.dynamic_slice_in_dim(piece, at * rows, rows, axis=0)
    for steps in range(1, count):
        outgoing = lax.dynamic_slice_in_dim(piece, ((at + steps) % count) * rows, rows, axis=0)
        total = total + rotated(outgoing.astype(jnp.bfloat16), axis, steps).astype(jnp.float32)
    low = total.astype(jnp.bfloat16)
    gathered = jnp.zeros(piece.shape, jnp.float32)
    gathered = lax.dynamic_update_slice_in_dim(gathered, total, at * rows, axis=0)
    for steps in range(1, count):
        arrived = rotated(low, axis, steps).astype(jnp.float32)
        gathered = lax.dynamic_update_slice_in_dim(
            gathered, arrived, ((at - steps) % count) * rows, axis=0
        )
    return gathered


def doc_start_of(starts, positions):
    covered = starts[None, :] <= positions[:, None]
    return jnp.max(jnp.where(covered, starts[None, :], 0), axis=1)


def attention_kernel(*refs, heads, kv_heads, margin, slots, blocks, chip_outputs):
    flag_ref, lo_ref, q_ref, do_ref = refs[:4]
    block_refs = refs[4 : 4 + blocks]
    kv_ref, dkv_ref = refs[-2:]
    outs = refs[-3 - len(slots) : -2]
    dq_ref = outs[0]
    out_refs = outs[1:]
    block_rows = block_refs[0].shape[0]
    flag = flag_ref[0]
    for index, (when_low, when_high) in enumerate(slots):
        target = kv_ref.at[pl.ds(index * block_rows, block_rows), :]
        if when_low == when_high:
            target[...] = block_refs[when_low][...]
        else:

            @pl.when(flag == 0)
            def _():
                target[...] = block_refs[when_low][...]

            @pl.when(flag != 0)
            def _():
                target[...] = block_refs[when_high][...]

    rows = q_ref.shape[0]
    keys = kv_ref.shape[0]
    scale = HEAD_DIM ** (-0.5)
    kv_width = kv_heads * HEAD_DIM
    per_group = heads // kv_heads
    col = lax.broadcasted_iota(jnp.int32, (rows, keys), 1)
    row = lax.broadcasted_iota(jnp.int32, (rows, keys), 0)
    allowed = (col >= lo_ref[...]) & (col <= row + margin)
    for group in range(kv_heads):
        k_cols = pl.ds(group * HEAD_DIM, HEAD_DIM)
        v_cols = pl.ds(kv_width + group * HEAD_DIM, HEAD_DIM)
        key_g = kv_ref[:, k_cols]
        value_g = kv_ref[:, v_cols]
        grad_k = None
        grad_v = None
        for member in range(per_group):
            q_cols = pl.ds((group * per_group + member) * HEAD_DIM, HEAD_DIM)
            query_h = q_ref[:, q_cols]
            grad_h = do_ref[:, q_cols]
            scores = lax.dot_general(query_h, key_g, NT, preferred_element_type=jnp.float32) * scale
            scores = jnp.where(allowed, scores, -1e30)
            largest = jnp.max(scores, axis=1, keepdims=True)
            raised = jnp.exp(scores - largest)
            probs = raised * (1.0 / jnp.sum(raised, axis=1, keepdims=True))
            grad_probs = lax.dot_general(grad_h, value_g, NT, preferred_element_type=jnp.float32)
            row_dot = jnp.sum(probs * grad_probs, axis=1, keepdims=True)
            grad_scores = (probs * (grad_probs - row_dot) * scale).astype(jnp.bfloat16)
            probs_low = probs.astype(jnp.bfloat16)
            dq_ref[:, q_cols] = jnp.dot(
                grad_scores, key_g, preferred_element_type=jnp.float32
            ).astype(dq_ref.dtype)
            term_k = lax.dot_general(grad_scores, query_h, TN, preferred_element_type=jnp.float32)
            term_v = lax.dot_general(probs_low, grad_h, TN, preferred_element_type=jnp.float32)
            grad_k = term_k if grad_k is None else grad_k + term_k
            grad_v = term_v if grad_v is None else grad_v + term_v
        dkv_ref[:, k_cols] = grad_k
        dkv_ref[:, v_cols] = grad_v
    def slot_rows(index):
        return dkv_ref[pl.ds(index * block_rows, block_rows), :]

    if chip_outputs:
        mate_ref, other_ref, two_ref, own_ref = out_refs
        two_ref[...] = slot_rows(1)
        own_ref[...] = slot_rows(3)

        @pl.when(flag == 0)
        def _():
            mate_ref[...] = slot_rows(2).astype(mate_ref.dtype)
            other_ref[...] = slot_rows(0).astype(other_ref.dtype)

        @pl.when(flag != 0)
        def _():
            mate_ref[...] = slot_rows(0).astype(mate_ref.dtype)
            other_ref[...] = slot_rows(2).astype(other_ref.dtype)

    else:
        for index, out_ref in enumerate(out_refs):
            out_ref[...] = slot_rows(index)


def attention(
    flag, lo_rel, queries, grads, kv_blocks, slots, heads, kv_heads, margin, early, chip_outputs
):
    rows, width = queries.shape
    blocks = len(kv_blocks)
    block_rows, kv_cols = kv_blocks[0].shape
    keys = len(slots) * block_rows
    kernel = functools.partial(
        attention_kernel,
        heads=heads,
        kv_heads=kv_heads,
        margin=margin,
        slots=tuple(slots),
        blocks=blocks,
        chip_outputs=chip_outputs,
    )
    if chip_outputs:
        piece_types = [jnp.bfloat16, jnp.bfloat16, jnp.float32, jnp.float32]
    else:
        piece_types = [jnp.float32] * len(slots)
    vmem = pl.BlockSpec(memory_space=pltpu.VMEM)
    smem = pl.BlockSpec(memory_space=pltpu.SMEM)
    flops = 2 * 5 * heads * rows * keys * HEAD_DIM
    moved = 2 * (2 * rows * width + keys * kv_cols + rows * width) + 4 * keys * kv_cols
    return pl.pallas_call(
        kernel,
        out_shape=(jax.ShapeDtypeStruct((rows, width), jnp.bfloat16),)
        + tuple(jax.ShapeDtypeStruct((block_rows, kv_cols), kind) for kind in piece_types),
        in_specs=[smem] + [vmem] * (3 + blocks) + [pl.BlockSpec(memory_space=pl.ANY)] * len(early),
        out_specs=(vmem,) * (1 + len(slots)),
        scratch_shapes=[
            pltpu.VMEM((keys, kv_cols), kv_blocks[0].dtype),
            pltpu.VMEM((keys, kv_cols), jnp.float32),
        ],
        cost_estimate=pl.CostEstimate(
            flops=flops, transcendentals=heads * rows * keys, bytes_accessed=moved
        ),
    )(flag, lo_rel, queries, grads, *kv_blocks, *early)


def body(layer_input, query_heads, key_heads, value_heads, grad_out, doc_starts):
    block_rows = query_heads.shape[1]
    window = min(SPAN, lax.axis_size(RING) * block_rows // 2)
    reach = (window + block_rows - 2) // block_rows
    margin = reach * block_rows
    kv_width = key_heads.shape[2]
    heads = query_heads.shape[2] // HEAD_DIM
    kv_heads = kv_width // HEAD_DIM
    first_row = lax.axis_index(RING) * block_rows

    fsdp_count = lax.axis_size("fsdp")
    model_width = layer_input.shape[2]
    shard_rows = model_width // fsdp_count
    trade_count = lax.axis_size(TRADE)
    trade_at = lax.axis_index(TRADE)
    piece_rows = model_width // trade_count
    own_input = layer_input[0]
    inputs = [lax.dynamic_slice_in_dim(own_input, trade_at * piece_rows, piece_rows, axis=1)]
    for steps in range(1, trade_count):
        target = (trade_at + steps) % trade_count
        outgoing = lax.dynamic_slice_in_dim(own_input, target * piece_rows, piece_rows, axis=1)
        inputs.append(rotated(outgoing, TRADE, steps))

    own_kv = jnp.concatenate([key_heads[0], value_heads[0]], axis=1)
    query_pos = first_row + jnp.arange(block_rows, dtype=jnp.int32)
    lowest = jnp.maximum(doc_start_of(doc_starts[0], query_pos), query_pos - window + 1)
    lo_rel = (lowest - first_row + margin).astype(jnp.int32)[:, None]
    sub_count = lax.axis_size("sub")
    sub_at = lax.axis_index("sub")
    flag = jnp.reshape(sub_at, (1,)).astype(jnp.int32)
    chip_route = sub_count == 2 and reach == 3
    if chip_route:
        ring_count = lax.axis_size(RING)
        across = [(2 * chip - 3, 2 * chip) for chip in range(2, ring_count // 2)]
        two_back = passed_along(own_kv, "ctx", 1)
        one_back_high = passed_along(own_kv, "sub", 1)
        three_back_low = lax.ppermute(own_kv, RING, across)
        swapped = rotated(two_back, "sub", 1)
        kv_blocks = [two_back, one_back_high, three_back_low, swapped, own_kv]
        slots = [(2, 3), (0, 0), (3, 1), (4, 4)]
    else:
        arrived = []
        moving = own_kv
        for _ in range(reach):
            moving = passed_along(moving, RING, 1)
            arrived.append(moving)
        kv_blocks = arrived[::-1] + [own_kv]
        slots = [(index, index) for index in range(reach + 1)]
    grad_q, *grad_pieces = attention(
        flag, lo_rel, query_heads[0], grad_out[0], kv_blocks, slots, heads, kv_heads, margin,
        inputs[1:],
        chip_route,
    )

    def low(value):
        return value.astype(jnp.bfloat16)

    if chip_route:
        back = [(target, source) for source, target in across]
        to_mate, to_other, g2, g0 = grad_pieces
        from_far = lax.ppermute(to_other, RING, back).astype(jnp.float32)
        from_mate = rotated(to_mate, "sub", 1).astype(jnp.float32)
        from_high = passed_along(to_other, "sub", -1).astype(jnp.float32)
        two_back_sum = g2 + from_mate
        from_next = passed_along(low(two_back_sum), "ctx", -1).astype(jnp.float32)
        total = g0 + from_high + from_far + from_next
    else:

        def own_piece(distance):
            return grad_pieces[reach - distance]

        total = own_piece(reach)
        for distance in range(reach - 1, -1, -1):
            moved = passed_along(low(total), RING, -1).astype(jnp.float32)
            total = moved + own_piece(distance)
    grad_kv = total.astype(jnp.bfloat16)
    grad_key = grad_kv[:, :kv_width]
    grad_value = grad_kv[:, kv_width:]

    values = [grad_value]
    for steps in range(1, trade_count):
        values.append(rotated(grad_value, TRADE, steps))
    stacked_inputs = jnp.concatenate(inputs, axis=0)
    stacked_values = jnp.concatenate(values, axis=0)
    mine = lax.dot_general(stacked_inputs, stacked_values, TN, preferred_element_type=jnp.float32)
    token_scale = float(fsdp_count * lax.axis_size(RING) * block_rows) ** (-0.5)
    scale_early = token_scale == 2.0 ** round(math.log2(token_scale))
    if scale_early:
        mine = mine * token_scale

    reduced = ring_sum(mine, "ctx")
    if sub_count == 2:
        other = rotated(reduced.astype(jnp.bfloat16), "sub", 1).astype(jnp.float32)
        first = jnp.where(sub_at == 0, reduced, other)
        second = jnp.where(sub_at == 0, other, reduced)
        weight_v = jnp.concatenate([first, second], axis=0)
    else:
        weight_v = lax.all_gather(reduced, "sub", axis=0, tiled=True)
    if not scale_early:
        weight_v = weight_v * token_scale
    return (
        grad_q[None],
        grad_key[None],
        grad_value[None],
        weight_v,
    )


def solution(mesh):
    placed = (
        P(("groups", "fsdp"), ("ctx", "sub"), None),
        P(("groups", "fsdp"), ("ctx", "sub"), None),
        P(("groups", "fsdp"), ("ctx", "sub"), None),
        P(("groups", "fsdp"), ("ctx", "sub"), None),
        P(("groups", "fsdp"), ("ctx", "sub"), None),
        P(("groups", "fsdp"), None),
    )
    return jax.shard_map(
        body,
        mesh=mesh,
        in_specs=placed,
        out_specs=(
            P(("groups", "fsdp"), ("ctx", "sub"), None),
            P(("groups", "fsdp"), ("ctx", "sub"), None),
            P(("groups", "fsdp"), ("ctx", "sub"), None),
            P(("groups", "fsdp"), None),
        ),
        check_vma=False,
    )
```

```python
import functools
import math

import jax
import jax.numpy as jnp
from jax import lax
from jax.experimental import pallas as pl
from jax.experimental.pallas import tpu as pltpu
from jax.sharding import PartitionSpec as P

HEAD_DIM = 256
SPAN = 768
RING = ("ctx", "sub")
NT = (((1,), (1,)), ((), ()))
TN = (((0,), (0,)), ((), ()))


def passed_along(value, axis, steps):
    count = lax.axis_size(axis)
    first, last = (max(0, -steps), min(count, count - steps))
    return lax.ppermute(value, axis, [(source, source + steps) for source in range(first, last)])


def rotated(value, axis, steps):
    count = lax.axis_size(axis)
    return lax.ppermute(value, axis, [(source, (source + steps) % count) for source in range(count)])


def ring_sum(piece, axis):
    count = lax.axis_size(axis)
    at = lax.axis_index(axis)
    rows = piece.shape[0] // count
    total = lax.dynamic_slice_in_dim(piece, at * rows, rows, axis=0)
    for steps in range(1, count):
        outgoing = lax.dynamic_slice_in_dim(piece, ((at + steps) % count) * rows, rows, axis=0)
        total = total + rotated(outgoing.astype(jnp.bfloat16), axis, steps).astype(jnp.float32)
    low = total.astype(jnp.bfloat16)
    gathered = jnp.zeros(piece.shape, jnp.float32)
    gathered = lax.dynamic_update_slice_in_dim(gathered, total, at * rows, axis=0)
    for steps in range(1, count):
        arrived = rotated(low, axis, steps).astype(jnp.float32)
        gathered = lax.dynamic_update_slice_in_dim(
            gathered, arrived, ((at - steps) % count) * rows, axis=0
        )
    return gathered


def doc_start_of(starts, positions):
    covered = starts[None, :] <= positions[:, None]
    return jnp.max(jnp.where(covered, starts[None, :], 0), axis=1)


def attention_kernel(*refs, heads, kv_heads, margin, slots, blocks, chip_outputs):
    flag_ref, lo_ref, q_ref, do_ref = refs[:4]
    block_refs = refs[4 : 4 + blocks]
    kv_ref, dkv_ref = refs[-2:]
    outs = refs[-3 - len(slots) : -2]
    dq_ref = outs[0]
    out_refs = outs[1:]
    block_rows = block_refs[0].shape[0]
    flag = flag_ref[0]
    for index, (when_low, when_high) in enumerate(slots):
        target = kv_ref.at[pl.ds(index * block_rows, block_rows), :]
        if when_low == when_high:
            target[...] = block_refs[when_low][...]
        else:

            @pl.when(flag == 0)
            def _():
                target[...] = block_refs[when_low][...]

            @pl.when(flag != 0)
            def _():
                target[...] = block_refs[when_high][...]

    rows = q_ref.shape[0]
    keys = kv_ref.shape[0]
    scale = HEAD_DIM ** (-0.5)
    kv_width = kv_heads * HEAD_DIM
    per_group = heads // kv_heads
    col = lax.broadcasted_iota(jnp.int32, (rows, keys), 1)
    row = lax.broadcasted_iota(jnp.int32, (rows, keys), 0)
    allowed = (col >= lo_ref[...]) & (col <= row + margin)
    for group in range(kv_heads):
        k_cols = pl.ds(group * HEAD_DIM, HEAD_DIM)
        v_cols = pl.ds(kv_width + group * HEAD_DIM, HEAD_DIM)
        key_g = kv_ref[:, k_cols]
        value_g = kv_ref[:, v_cols]
        grad_k = None
        grad_v = None
        for member in range(per_group):
            q_cols = pl.ds((group * per_group + member) * HEAD_DIM, HEAD_DIM)
            query_h = q_ref[:, q_cols]
            grad_h = do_ref[:, q_cols]
            scores = lax.dot_general(query_h, key_g, NT, preferred_element_type=jnp.float32) * scale
            scores = jnp.where(allowed, scores, -1e30)
            largest = jnp.max(scores, axis=1, keepdims=True)
            raised = jnp.exp(scores - largest)
            probs = raised * (1.0 / jnp.sum(raised, axis=1, keepdims=True))
            grad_probs = lax.dot_general(grad_h, value_g, NT, preferred_element_type=jnp.float32)
            row_dot = jnp.sum(probs * grad_probs, axis=1, keepdims=True)
            grad_scores = (probs * (grad_probs - row_dot) * scale).astype(jnp.bfloat16)
            probs_low = probs.astype(jnp.bfloat16)
            dq_ref[:, q_cols] = jnp.dot(
                grad_scores, key_g, preferred_element_type=jnp.float32
            ).astype(dq_ref.dtype)
            term_k = lax.dot_general(grad_scores, query_h, TN, preferred_element_type=jnp.float32)
            term_v = lax.dot_general(probs_low, grad_h, TN, preferred_element_type=jnp.float32)
            grad_k = term_k if grad_k is None else grad_k + term_k
            grad_v = term_v if grad_v is None else grad_v + term_v
        dkv_ref[:, k_cols] = grad_k
        dkv_ref[:, v_cols] = grad_v
    def slot_rows(index):
        return dkv_ref[pl.ds(index * block_rows, block_rows), :]

    if chip_outputs:
        mate_ref, other_ref, two_ref, own_ref = out_refs
        two_ref[...] = slot_rows(1)
        own_ref[...] = slot_rows(3)

        @pl.when(flag == 0)
        def _():
            mate_ref[...] = slot_rows(2).astype(mate_ref.dtype)
            other_ref[...] = slot_rows(0).astype(other_ref.dtype)

        @pl.when(flag != 0)
        def _():
            mate_ref[...] = slot_rows(0).astype(mate_ref.dtype)
            other_ref[...] = slot_rows(2).astype(other_ref.dtype)

    else:
        for index, out_ref in enumerate(out_refs):
            out_ref[...] = slot_rows(index)


def attention(
    flag, lo_rel, queries, grads, kv_blocks, slots, heads, kv_heads, margin, early, chip_outputs
):
    rows, width = queries.shape
    blocks = len(kv_blocks)
    block_rows, kv_cols = kv_blocks[0].shape
    keys = len(slots) * block_rows
    kernel = functools.partial(
        attention_kernel,
        heads=heads,
        kv_heads=kv_heads,
        margin=margin,
        slots=tuple(slots),
        blocks=blocks,
        chip_outputs=chip_outputs,
    )
    if chip_outputs:
        piece_types = [jnp.bfloat16, jnp.bfloat16, jnp.float32, jnp.float32]
    else:
        piece_types = [jnp.float32] * len(slots)
    vmem = pl.BlockSpec(memory_space=pltpu.VMEM)
    smem = pl.BlockSpec(memory_space=pltpu.SMEM)
    flops = 2 * 5 * heads * rows * keys * HEAD_DIM
    moved = 2 * (2 * rows * width + keys * kv_cols + rows * width) + 4 * keys * kv_cols
    return pl.pallas_call(
        kernel,
        out_shape=(jax.ShapeDtypeStruct((rows, width), jnp.bfloat16),)
        + tuple(jax.ShapeDtypeStruct((block_rows, kv_cols), kind) for kind in piece_types),
        in_specs=[smem] + [vmem] * (3 + blocks) + [pl.BlockSpec(memory_space=pl.ANY)] * len(early),
        out_specs=(vmem,) * (1 + len(slots)),
        scratch_shapes=[
            pltpu.VMEM((keys, kv_cols), kv_blocks[0].dtype),
            pltpu.VMEM((keys, kv_cols), jnp.float32),
        ],
        cost_estimate=pl.CostEstimate(
            flops=flops, transcendentals=heads * rows * keys, bytes_accessed=moved
        ),
    )(flag, lo_rel, queries, grads, *kv_blocks, *early)


def body(layer_input, query_heads, key_heads, value_heads, grad_out, doc_starts):
    block_rows = query_heads.shape[1]
    window = min(SPAN, lax.axis_size(RING) * block_rows // 2)
    reach = (window + block_rows - 2) // block_rows
    margin = reach * block_rows
    kv_width = key_heads.shape[2]
    heads = query_heads.shape[2] // HEAD_DIM
    kv_heads = kv_width // HEAD_DIM
    first_row = lax.axis_index(RING) * block_rows

    fsdp_count = lax.axis_size("fsdp")
    fsdp_at = lax.axis_index("fsdp")
    model_width = layer_input.shape[2]
    shard_rows = model_width // fsdp_count
    own_input = layer_input[0]
    inputs = [lax.dynamic_slice_in_dim(own_input, fsdp_at * shard_rows, shard_rows, axis=1)]
    for steps in range(1, fsdp_count):
        target = (fsdp_at + steps) % fsdp_count
        outgoing = lax.dynamic_slice_in_dim(own_input, target * shard_rows, shard_rows, axis=1)
        inputs.append(rotated(outgoing, "fsdp", steps))

    own_kv = jnp.concatenate([key_heads[0], value_heads[0]], axis=1)
    query_pos = first_row + jnp.arange(block_rows, dtype=jnp.int32)
    lowest = jnp.maximum(doc_start_of(doc_starts[0], query_pos), query_pos - window + 1)
    lo_rel = (lowest - first_row + margin).astype(jnp.int32)[:, None]
    sub_count = lax.axis_size("sub")
    sub_at = lax.axis_index("sub")
    flag = jnp.reshape(sub_at, (1,)).astype(jnp.int32)
    chip_route = sub_count == 2 and reach == 3
    if chip_route:
        ring_count = lax.axis_size(RING)
        across = [(2 * chip - 3, 2 * chip) for chip in range(2, ring_count // 2)]
        two_back = passed_along(own_kv, "ctx", 1)
        one_back_high = passed_along(own_kv, "sub", 1)
        three_back_low = lax.ppermute(own_kv, RING, across)
        swapped = rotated(two_back, "sub", 1)
        kv_blocks = [two_back, one_back_high, three_back_low, swapped, own_kv]
        slots = [(2, 3), (0, 0), (3, 1), (4, 4)]
    else:
        arrived = []
        moving = own_kv
        for _ in range(reach):
            moving = passed_along(moving, RING, 1)
            arrived.append(moving)
        kv_blocks = arrived[::-1] + [own_kv]
        slots = [(index, index) for index in range(reach + 1)]
    grad_q, *grad_pieces = attention(
        flag, lo_rel, query_heads[0], grad_out[0], kv_blocks, slots, heads, kv_heads, margin,
        inputs[1:],
        chip_route,
    )

    def low(value):
        return value.astype(jnp.bfloat16)

    if chip_route:
        back = [(target, source) for source, target in across]

        def returned(to_mate, to_other, g2, g0):
            from_far = lax.ppermute(to_other, RING, back).astype(jnp.float32)
            from_mate = rotated(to_mate, "sub", 1).astype(jnp.float32)
            from_high = passed_along(to_other, "sub", -1).astype(jnp.float32)
            two_back_sum = g2 + from_mate
            from_next = passed_along(low(two_back_sum), "ctx", -1).astype(jnp.float32)
            return g0 + from_high + from_far + from_next

        total_v = returned(*[piece[:, kv_width:] for piece in grad_pieces])
        total_v, key_pieces = lax.optimization_barrier(
            (total_v, [piece[:, :kv_width] for piece in grad_pieces])
        )
        total_k = returned(*key_pieces)
        total = jnp.concatenate([total_k, total_v], axis=1)
    else:

        def own_piece(distance):
            return grad_pieces[reach - distance]

        total = own_piece(reach)
        for distance in range(reach - 1, -1, -1):
            moved = passed_along(low(total), RING, -1).astype(jnp.float32)
            total = moved + own_piece(distance)
    grad_kv = total.astype(jnp.bfloat16)
    grad_key = grad_kv[:, :kv_width]
    grad_value = grad_kv[:, kv_width:]

    values = [grad_value]
    for steps in range(1, fsdp_count):
        values.append(rotated(grad_value, "fsdp", steps))
    stacked_inputs = jnp.concatenate(inputs, axis=0)
    stacked_values = jnp.concatenate(values, axis=0)
    shard = lax.dot_general(stacked_inputs, stacked_values, TN, preferred_element_type=jnp.float32)
    token_scale = float(fsdp_count * lax.axis_size(RING) * block_rows) ** (-0.5)
    scale_early = token_scale == 2.0 ** round(math.log2(token_scale))
    if scale_early:
        shard = shard * token_scale

    sub_count = lax.axis_size("sub")
    sub_at = lax.axis_index("sub")
    piece_rows = shard_rows // sub_count
    mine = lax.dynamic_slice_in_dim(shard, sub_at * piece_rows, piece_rows, axis=0)
    for steps in range(1, sub_count):
        target = (sub_at + steps) % sub_count
        outgoing = lax.dynamic_slice_in_dim(shard, target * piece_rows, piece_rows, axis=0)
        mine = mine + rotated(outgoing.astype(jnp.bfloat16), "sub", steps).astype(jnp.float32)
    if chip_route:
        mine, _ = lax.optimization_barrier((mine, total_k))
    reduced = ring_sum(mine, "ctx")
    if sub_count == 2:
        other = rotated(reduced.astype(jnp.bfloat16), "sub", 1).astype(jnp.float32)
        first = jnp.where(sub_at == 0, reduced, other)
        second = jnp.where(sub_at == 0, other, reduced)
        weight_v = jnp.concatenate([first, second], axis=0)
    else:
        weight_v = lax.all_gather(reduced, "sub", axis=0, tiled=True)
    if not scale_early:
        weight_v = weight_v * token_scale
    return (
        grad_q[None],
        grad_key[None],
        grad_value[None],
        weight_v,
    )


def solution(mesh):
    placed = (
        P(("groups", "fsdp"), ("ctx", "sub"), None),
        P(("groups", "fsdp"), ("ctx", "sub"), None),
        P(("groups", "fsdp"), ("ctx", "sub"), None),
        P(("groups", "fsdp"), ("ctx", "sub"), None),
        P(("groups", "fsdp"), ("ctx", "sub"), None),
        P(("groups", "fsdp"), None),
    )
    return jax.shard_map(
        body,
        mesh=mesh,
        in_specs=placed,
        out_specs=(
            P(("groups", "fsdp"), ("ctx", "sub"), None),
            P(("groups", "fsdp"), ("ctx", "sub"), None),
            P(("groups", "fsdp"), ("ctx", "sub"), None),
            P(("groups", "fsdp"), None),
        ),
        check_vma=False,
    )
```

```python
import functools
import math

import jax
import jax.numpy as jnp
from jax import lax
from jax.experimental import pallas as pl
from jax.experimental.pallas import tpu as pltpu
from jax.sharding import PartitionSpec as P

HEAD_DIM = 256
SPAN = 768
RING = ("ctx", "sub")
NT = (((1,), (1,)), ((), ()))
TN = (((0,), (0,)), ((), ()))


def passed_along(value, axis, steps):
    count = lax.axis_size(axis)
    first, last = (max(0, -steps), min(count, count - steps))
    return lax.ppermute(value, axis, [(source, source + steps) for source in range(first, last)])


def rotated(value, axis, steps):
    count = lax.axis_size(axis)
    return lax.ppermute(value, axis, [(source, (source + steps) % count) for source in range(count)])


def ring_sum(piece, axis):
    count = lax.axis_size(axis)
    at = lax.axis_index(axis)
    rows = piece.shape[0] // count
    total = lax.dynamic_slice_in_dim(piece, at * rows, rows, axis=0)
    for steps in range(1, count):
        outgoing = lax.dynamic_slice_in_dim(piece, ((at + steps) % count) * rows, rows, axis=0)
        total = total + rotated(outgoing.astype(jnp.bfloat16), axis, steps).astype(jnp.float32)
    low = total.astype(jnp.bfloat16)
    gathered = jnp.zeros(piece.shape, jnp.float32)
    gathered = lax.dynamic_update_slice_in_dim(gathered, total, at * rows, axis=0)
    for steps in range(1, count):
        arrived = rotated(low, axis, steps).astype(jnp.float32)
        gathered = lax.dynamic_update_slice_in_dim(
            gathered, arrived, ((at - steps) % count) * rows, axis=0
        )
    return gathered


def doc_start_of(starts, positions):
    covered = starts[None, :] <= positions[:, None]
    return jnp.max(jnp.where(covered, starts[None, :], 0), axis=1)


def attention_kernel(*refs, heads, kv_heads, margin, slots, blocks, chip_outputs):
    flag_ref, lo_ref, q_ref, do_ref = refs[:4]
    block_refs = refs[4 : 4 + blocks]
    kv_ref, dkv_ref = refs[-2:]
    outs = refs[-3 - len(slots) : -2]
    dq_ref = outs[0]
    out_refs = outs[1:]
    block_rows = block_refs[0].shape[0]
    flag = flag_ref[0]
    for index, (when_low, when_high) in enumerate(slots):
        target = kv_ref.at[pl.ds(index * block_rows, block_rows), :]
        if when_low == when_high:
            target[...] = block_refs[when_low][...]
        else:

            @pl.when(flag == 0)
            def _():
                target[...] = block_refs[when_low][...]

            @pl.when(flag != 0)
            def _():
                target[...] = block_refs[when_high][...]

    rows = q_ref.shape[0]
    keys = kv_ref.shape[0]
    scale = HEAD_DIM ** (-0.5)
    kv_width = kv_heads * HEAD_DIM
    per_group = heads // kv_heads
    col = lax.broadcasted_iota(jnp.int32, (rows, keys), 1)
    row = lax.broadcasted_iota(jnp.int32, (rows, keys), 0)
    allowed = (col >= lo_ref[...]) & (col <= row + margin)
    for group in range(kv_heads):
        k_cols = pl.ds(group * HEAD_DIM, HEAD_DIM)
        v_cols = pl.ds(kv_width + group * HEAD_DIM, HEAD_DIM)
        key_g = kv_ref[:, k_cols]
        value_g = kv_ref[:, v_cols]
        grad_k = None
        grad_v = None
        for member in range(per_group):
            q_cols = pl.ds((group * per_group + member) * HEAD_DIM, HEAD_DIM)
            query_h = q_ref[:, q_cols]
            grad_h = do_ref[:, q_cols]
            scores = lax.dot_general(query_h, key_g, NT, preferred_element_type=jnp.float32) * scale
            scores = jnp.where(allowed, scores, -1e30)
            largest = jnp.max(scores, axis=1, keepdims=True)
            raised = jnp.exp(scores - largest)
            probs = raised * (1.0 / jnp.sum(raised, axis=1, keepdims=True))
            grad_probs = lax.dot_general(grad_h, value_g, NT, preferred_element_type=jnp.float32)
            row_dot = jnp.sum(probs * grad_probs, axis=1, keepdims=True)
            grad_scores = (probs * (grad_probs - row_dot) * scale).astype(jnp.bfloat16)
            probs_low = probs.astype(jnp.bfloat16)
            dq_ref[:, q_cols] = jnp.dot(
                grad_scores, key_g, preferred_element_type=jnp.float32
            ).astype(dq_ref.dtype)
            term_k = lax.dot_general(grad_scores, query_h, TN, preferred_element_type=jnp.float32)
            term_v = lax.dot_general(probs_low, grad_h, TN, preferred_element_type=jnp.float32)
            grad_k = term_k if grad_k is None else grad_k + term_k
            grad_v = term_v if grad_v is None else grad_v + term_v
        dkv_ref[:, k_cols] = grad_k
        dkv_ref[:, v_cols] = grad_v
    def slot_rows(index):
        return dkv_ref[pl.ds(index * block_rows, block_rows), :]

    if chip_outputs:
        mate_ref, other_ref, two_ref, own_ref = out_refs
        two_ref[...] = slot_rows(1)
        own_ref[...] = slot_rows(3)

        @pl.when(flag == 0)
        def _():
            mate_ref[...] = slot_rows(2).astype(mate_ref.dtype)
            other_ref[...] = slot_rows(0).astype(other_ref.dtype)

        @pl.when(flag != 0)
        def _():
            mate_ref[...] = slot_rows(0).astype(mate_ref.dtype)
            other_ref[...] = slot_rows(2).astype(other_ref.dtype)

    else:
        for index, out_ref in enumerate(out_refs):
            out_ref[...] = slot_rows(index)


def attention(
    flag, lo_rel, queries, grads, kv_blocks, slots, heads, kv_heads, margin, early, chip_outputs
):
    rows, width = queries.shape
    blocks = len(kv_blocks)
    block_rows, kv_cols = kv_blocks[0].shape
    keys = len(slots) * block_rows
    kernel = functools.partial(
        attention_kernel,
        heads=heads,
        kv_heads=kv_heads,
        margin=margin,
        slots=tuple(slots),
        blocks=blocks,
        chip_outputs=chip_outputs,
    )
    if chip_outputs:
        piece_types = [jnp.bfloat16, jnp.bfloat16, jnp.float32, jnp.float32]
    else:
        piece_types = [jnp.float32] * len(slots)
    vmem = pl.BlockSpec(memory_space=pltpu.VMEM)
    smem = pl.BlockSpec(memory_space=pltpu.SMEM)
    flops = 2 * 5 * heads * rows * keys * HEAD_DIM
    moved = 2 * (2 * rows * width + keys * kv_cols + rows * width) + 4 * keys * kv_cols
    return pl.pallas_call(
        kernel,
        out_shape=(jax.ShapeDtypeStruct((rows, width), jnp.bfloat16),)
        + tuple(jax.ShapeDtypeStruct((block_rows, kv_cols), kind) for kind in piece_types),
        in_specs=[smem] + [vmem] * (3 + blocks) + [pl.BlockSpec(memory_space=pl.ANY)] * len(early),
        out_specs=(vmem,) * (1 + len(slots)),
        scratch_shapes=[
            pltpu.VMEM((keys, kv_cols), kv_blocks[0].dtype),
            pltpu.VMEM((keys, kv_cols), jnp.float32),
        ],
        cost_estimate=pl.CostEstimate(
            flops=flops, transcendentals=heads * rows * keys, bytes_accessed=moved
        ),
    )(flag, lo_rel, queries, grads, *kv_blocks, *early)


def body(layer_input, query_heads, key_heads, value_heads, grad_out, doc_starts):
    block_rows = query_heads.shape[1]
    window = min(SPAN, lax.axis_size(RING) * block_rows // 2)
    reach = (window + block_rows - 2) // block_rows
    margin = reach * block_rows
    kv_width = key_heads.shape[2]
    heads = query_heads.shape[2] // HEAD_DIM
    kv_heads = kv_width // HEAD_DIM
    first_row = lax.axis_index(RING) * block_rows

    fsdp_count = lax.axis_size("fsdp")
    fsdp_at = lax.axis_index("fsdp")
    model_width = layer_input.shape[2]
    shard_rows = model_width // fsdp_count
    own_input = layer_input[0]
    inputs = [lax.dynamic_slice_in_dim(own_input, fsdp_at * shard_rows, shard_rows, axis=1)]
    for steps in range(1, fsdp_count):
        target = (fsdp_at + steps) % fsdp_count
        outgoing = lax.dynamic_slice_in_dim(own_input, target * shard_rows, shard_rows, axis=1)
        inputs.append(rotated(outgoing, "fsdp", steps))

    own_kv = jnp.concatenate([key_heads[0], value_heads[0]], axis=1)
    query_pos = first_row + jnp.arange(block_rows, dtype=jnp.int32)
    lowest = jnp.maximum(doc_start_of(doc_starts[0], query_pos), query_pos - window + 1)
    lo_rel = (lowest - first_row + margin).astype(jnp.int32)[:, None]
    sub_count = lax.axis_size("sub")
    sub_at = lax.axis_index("sub")
    flag = jnp.reshape(sub_at, (1,)).astype(jnp.int32)
    chip_route = sub_count == 2 and reach == 3
    if chip_route:
        ring_count = lax.axis_size(RING)
        across = [(2 * chip - 3, 2 * chip) for chip in range(2, ring_count // 2)]
        two_back = passed_along(own_kv, "ctx", 1)
        one_back_high = passed_along(own_kv, "sub", 1)
        three_back_low = lax.ppermute(own_kv, RING, across)
        swapped = rotated(two_back, "sub", 1)
        kv_blocks = [two_back, one_back_high, three_back_low, swapped, own_kv]
        slots = [(2, 3), (0, 0), (3, 1), (4, 4)]
    else:
        arrived = []
        moving = own_kv
        for _ in range(reach):
            moving = passed_along(moving, RING, 1)
            arrived.append(moving)
        kv_blocks = arrived[::-1] + [own_kv]
        slots = [(index, index) for index in range(reach + 1)]
    grad_q, *grad_pieces = attention(
        flag, lo_rel, query_heads[0], grad_out[0], kv_blocks, slots, heads, kv_heads, margin,
        [],
        chip_route,
    )

    def low(value):
        return value.astype(jnp.bfloat16)

    if chip_route:
        back = [(target, source) for source, target in across]
        to_mate, to_other, g2, g0 = grad_pieces
        from_far = lax.ppermute(to_other, RING, back).astype(jnp.float32)
        from_mate = rotated(to_mate, "sub", 1).astype(jnp.float32)
        from_high = passed_along(to_other, "sub", -1).astype(jnp.float32)
        two_back_sum = g2 + from_mate
        from_next = passed_along(low(two_back_sum), "ctx", -1).astype(jnp.float32)
        total = g0 + from_high + from_far + from_next
    else:

        def own_piece(distance):
            return grad_pieces[reach - distance]

        total = own_piece(reach)
        for distance in range(reach - 1, -1, -1):
            moved = passed_along(low(total), RING, -1).astype(jnp.float32)
            total = moved + own_piece(distance)
    grad_kv = total.astype(jnp.bfloat16)
    grad_key = grad_kv[:, :kv_width]
    grad_value = grad_kv[:, kv_width:]

    values = [grad_value]
    for steps in range(1, fsdp_count):
        values.append(rotated(grad_value, "fsdp", steps))
    stacked_inputs = jnp.concatenate(inputs, axis=0)
    stacked_values = jnp.concatenate(values, axis=0)
    shard = lax.dot_general(stacked_inputs, stacked_values, TN, preferred_element_type=jnp.float32)
    token_scale = float(fsdp_count * lax.axis_size(RING) * block_rows) ** (-0.5)
    scale_early = token_scale == 2.0 ** round(math.log2(token_scale))
    if scale_early:
        shard = shard * token_scale

    sub_count = lax.axis_size("sub")
    sub_at = lax.axis_index("sub")
    piece_rows = shard_rows // sub_count
    mine = lax.dynamic_slice_in_dim(shard, sub_at * piece_rows, piece_rows, axis=0)
    for steps in range(1, sub_count):
        target = (sub_at + steps) % sub_count
        outgoing = lax.dynamic_slice_in_dim(shard, target * piece_rows, piece_rows, axis=0)
        mine = mine + rotated(outgoing.astype(jnp.bfloat16), "sub", steps).astype(jnp.float32)
    reduced = ring_sum(mine, "ctx")
    if sub_count == 2:
        other = rotated(reduced.astype(jnp.bfloat16), "sub", 1).astype(jnp.float32)
        first = jnp.where(sub_at == 0, reduced, other)
        second = jnp.where(sub_at == 0, other, reduced)
        weight_v = jnp.concatenate([first, second], axis=0)
    else:
        weight_v = lax.all_gather(reduced, "sub", axis=0, tiled=True)
    if not scale_early:
        weight_v = weight_v * token_scale
    return (
        grad_q[None],
        grad_key[None],
        grad_value[None],
        weight_v,
    )


def solution(mesh):
    placed = (
        P(("groups", "fsdp"), ("ctx", "sub"), None),
        P(("groups", "fsdp"), ("ctx", "sub"), None),
        P(("groups", "fsdp"), ("ctx", "sub"), None),
        P(("groups", "fsdp"), ("ctx", "sub"), None),
        P(("groups", "fsdp"), ("ctx", "sub"), None),
        P(("groups", "fsdp"), None),
    )
    return jax.shard_map(
        body,
        mesh=mesh,
        in_specs=placed,
        out_specs=(
            P(("groups", "fsdp"), ("ctx", "sub"), None),
            P(("groups", "fsdp"), ("ctx", "sub"), None),
            P(("groups", "fsdp"), ("ctx", "sub"), None),
            P(("groups", "fsdp"), None),
        ),
        check_vma=False,
    )
```

```python
import functools
import math

import jax
import jax.numpy as jnp
from jax import lax
from jax.experimental import pallas as pl
from jax.experimental.pallas import tpu as pltpu
from jax.sharding import PartitionSpec as P

HEAD_DIM = 256
SPAN = 768
RING = ("ctx", "sub")
NT = (((1,), (1,)), ((), ()))
TN = (((0,), (0,)), ((), ()))


def passed_along(value, axis, steps):
    count = lax.axis_size(axis)
    first, last = (max(0, -steps), min(count, count - steps))
    return lax.ppermute(value, axis, [(source, source + steps) for source in range(first, last)])


def rotated(value, axis, steps):
    count = lax.axis_size(axis)
    return lax.ppermute(value, axis, [(source, (source + steps) % count) for source in range(count)])


def ring_sum(piece, axis):
    count = lax.axis_size(axis)
    at = lax.axis_index(axis)
    rows = piece.shape[0] // count
    total = lax.dynamic_slice_in_dim(piece, at * rows, rows, axis=0)
    for steps in range(1, count):
        outgoing = lax.dynamic_slice_in_dim(piece, ((at + steps) % count) * rows, rows, axis=0)
        total = total + rotated(outgoing.astype(jnp.bfloat16), axis, steps).astype(jnp.float32)
    low = total.astype(jnp.bfloat16)
    gathered = jnp.zeros(piece.shape, jnp.float32)
    gathered = lax.dynamic_update_slice_in_dim(gathered, total, at * rows, axis=0)
    for steps in range(1, count):
        arrived = rotated(low, axis, steps).astype(jnp.float32)
        gathered = lax.dynamic_update_slice_in_dim(
            gathered, arrived, ((at - steps) % count) * rows, axis=0
        )
    return gathered


def doc_start_of(starts, positions):
    covered = starts[None, :] <= positions[:, None]
    return jnp.max(jnp.where(covered, starts[None, :], 0), axis=1)


def attention_kernel(*refs, heads, kv_heads, margin, slots, blocks, chip_outputs):
    flag_ref, lo_ref, q_ref, do_ref = refs[:4]
    block_refs = refs[4 : 4 + blocks]
    kv_ref, dkv_ref = refs[-2:]
    outs = refs[-3 - len(slots) : -2]
    dq_ref = outs[0]
    out_refs = outs[1:]
    block_rows = block_refs[0].shape[0]
    flag = flag_ref[0]
    for index, (when_low, when_high) in enumerate(slots):
        target = kv_ref.at[pl.ds(index * block_rows, block_rows), :]
        if when_low == when_high:
            target[...] = block_refs[when_low][...]
        else:

            @pl.when(flag == 0)
            def _():
                target[...] = block_refs[when_low][...]

            @pl.when(flag != 0)
            def _():
                target[...] = block_refs[when_high][...]

    rows = q_ref.shape[0]
    keys = kv_ref.shape[0]
    scale = HEAD_DIM ** (-0.5)
    kv_width = kv_heads * HEAD_DIM
    per_group = heads // kv_heads
    query_at = lax.broadcasted_iota(jnp.int32, (keys, rows), 1)
    key_at = lax.broadcasted_iota(jnp.int32, (keys, rows), 0)
    allowed = (key_at >= lo_ref[...]) & (key_at <= query_at + margin)
    for group in range(kv_heads):
        k_cols = pl.ds(group * HEAD_DIM, HEAD_DIM)
        v_cols = pl.ds(kv_width + group * HEAD_DIM, HEAD_DIM)
        key_g = kv_ref[:, k_cols]
        value_g = kv_ref[:, v_cols]
        grad_k = None
        grad_v = None
        for member in range(per_group):
            q_cols = pl.ds((group * per_group + member) * HEAD_DIM, HEAD_DIM)
            query_h = q_ref[:, q_cols]
            grad_h = do_ref[:, q_cols]
            scores = lax.dot_general(key_g, query_h, NT, preferred_element_type=jnp.float32) * scale
            scores = jnp.where(allowed, scores, -1e30)
            largest = jnp.max(scores, axis=0, keepdims=True)
            raised = jnp.exp(scores - largest)
            probs = raised * (1.0 / jnp.sum(raised, axis=0, keepdims=True))
            grad_probs = lax.dot_general(value_g, grad_h, NT, preferred_element_type=jnp.float32)
            row_dot = jnp.sum(probs * grad_probs, axis=0, keepdims=True)
            grad_scores = (probs * (grad_probs - row_dot) * scale).astype(jnp.bfloat16)
            probs_low = probs.astype(jnp.bfloat16)
            dq_ref[:, q_cols] = lax.dot_general(
                grad_scores, key_g, TN, preferred_element_type=jnp.float32
            ).astype(dq_ref.dtype)
            term_k = jnp.dot(grad_scores, query_h, preferred_element_type=jnp.float32)
            term_v = jnp.dot(probs_low, grad_h, preferred_element_type=jnp.float32)
            grad_k = term_k if grad_k is None else grad_k + term_k
            grad_v = term_v if grad_v is None else grad_v + term_v
        dkv_ref[:, k_cols] = grad_k
        dkv_ref[:, v_cols] = grad_v
    def slot_rows(index):
        return dkv_ref[pl.ds(index * block_rows, block_rows), :]

    if chip_outputs:
        mate_ref, other_ref, two_ref, own_ref = out_refs
        two_ref[...] = slot_rows(1)
        own_ref[...] = slot_rows(3)

        @pl.when(flag == 0)
        def _():
            mate_ref[...] = slot_rows(2).astype(mate_ref.dtype)
            other_ref[...] = slot_rows(0).astype(other_ref.dtype)

        @pl.when(flag != 0)
        def _():
            mate_ref[...] = slot_rows(0).astype(mate_ref.dtype)
            other_ref[...] = slot_rows(2).astype(other_ref.dtype)

    else:
        for index, out_ref in enumerate(out_refs):
            out_ref[...] = slot_rows(index)


def attention(
    flag, lo_rel, queries, grads, kv_blocks, slots, heads, kv_heads, margin, early, chip_outputs
):
    rows, width = queries.shape
    blocks = len(kv_blocks)
    block_rows, kv_cols = kv_blocks[0].shape
    keys = len(slots) * block_rows
    kernel = functools.partial(
        attention_kernel,
        heads=heads,
        kv_heads=kv_heads,
        margin=margin,
        slots=tuple(slots),
        blocks=blocks,
        chip_outputs=chip_outputs,
    )
    if chip_outputs:
        piece_types = [jnp.bfloat16, jnp.bfloat16, jnp.float32, jnp.float32]
    else:
        piece_types = [jnp.float32] * len(slots)
    vmem = pl.BlockSpec(memory_space=pltpu.VMEM)
    smem = pl.BlockSpec(memory_space=pltpu.SMEM)
    flops = 2 * 5 * heads * rows * keys * HEAD_DIM
    moved = 2 * (2 * rows * width + keys * kv_cols + rows * width) + 4 * keys * kv_cols
    return pl.pallas_call(
        kernel,
        out_shape=(jax.ShapeDtypeStruct((rows, width), jnp.bfloat16),)
        + tuple(jax.ShapeDtypeStruct((block_rows, kv_cols), kind) for kind in piece_types),
        in_specs=[smem] + [vmem] * (3 + blocks) + [pl.BlockSpec(memory_space=pl.ANY)] * len(early),
        out_specs=(vmem,) * (1 + len(slots)),
        scratch_shapes=[
            pltpu.VMEM((keys, kv_cols), kv_blocks[0].dtype),
            pltpu.VMEM((keys, kv_cols), jnp.float32),
        ],
        cost_estimate=pl.CostEstimate(
            flops=flops, transcendentals=heads * rows * keys, bytes_accessed=moved
        ),
    )(flag, lo_rel, queries, grads, *kv_blocks, *early)


def body(layer_input, query_heads, key_heads, value_heads, grad_out, doc_starts):
    block_rows = query_heads.shape[1]
    window = min(SPAN, lax.axis_size(RING) * block_rows // 2)
    reach = (window + block_rows - 2) // block_rows
    margin = reach * block_rows
    kv_width = key_heads.shape[2]
    heads = query_heads.shape[2] // HEAD_DIM
    kv_heads = kv_width // HEAD_DIM
    first_row = lax.axis_index(RING) * block_rows

    fsdp_count = lax.axis_size("fsdp")
    fsdp_at = lax.axis_index("fsdp")
    model_width = layer_input.shape[2]
    shard_rows = model_width // fsdp_count
    own_input = layer_input[0]
    inputs = [lax.dynamic_slice_in_dim(own_input, fsdp_at * shard_rows, shard_rows, axis=1)]
    for steps in range(1, fsdp_count):
        target = (fsdp_at + steps) % fsdp_count
        outgoing = lax.dynamic_slice_in_dim(own_input, target * shard_rows, shard_rows, axis=1)
        inputs.append(rotated(outgoing, "fsdp", steps))

    own_kv = jnp.concatenate([key_heads[0], value_heads[0]], axis=1)
    query_pos = first_row + jnp.arange(block_rows, dtype=jnp.int32)
    lowest = jnp.maximum(doc_start_of(doc_starts[0], query_pos), query_pos - window + 1)
    lo_rel = (lowest - first_row + margin).astype(jnp.int32)[None, :]
    sub_count = lax.axis_size("sub")
    sub_at = lax.axis_index("sub")
    flag = jnp.reshape(sub_at, (1,)).astype(jnp.int32)
    chip_route = sub_count == 2 and reach == 3
    if chip_route:
        ring_count = lax.axis_size(RING)
        across = [(2 * chip - 3, 2 * chip) for chip in range(2, ring_count // 2)]
        two_back = passed_along(own_kv, "ctx", 1)
        one_back_high = passed_along(own_kv, "sub", 1)
        three_back_low = lax.ppermute(own_kv, RING, across)
        swapped = rotated(two_back, "sub", 1)
        kv_blocks = [two_back, one_back_high, three_back_low, swapped, own_kv]
        slots = [(2, 3), (0, 0), (3, 1), (4, 4)]
    else:
        arrived = []
        moving = own_kv
        for _ in range(reach):
            moving = passed_along(moving, RING, 1)
            arrived.append(moving)
        kv_blocks = arrived[::-1] + [own_kv]
        slots = [(index, index) for index in range(reach + 1)]
    grad_q, *grad_pieces = attention(
        flag, lo_rel, query_heads[0], grad_out[0], kv_blocks, slots, heads, kv_heads, margin,
        inputs[1:],
        chip_route,
    )

    def low(value):
        return value.astype(jnp.bfloat16)

    if chip_route:
        back = [(target, source) for source, target in across]
        to_mate, to_other, g2, g0 = grad_pieces
        from_far = lax.ppermute(to_other, RING, back).astype(jnp.float32)
        from_mate = rotated(to_mate, "sub", 1).astype(jnp.float32)
        from_high = passed_along(to_other, "sub", -1).astype(jnp.float32)
        two_back_sum = g2 + from_mate
        from_next = passed_along(low(two_back_sum), "ctx", -1).astype(jnp.float32)
        total = g0 + from_high + from_far + from_next
    else:

        def own_piece(distance):
            return grad_pieces[reach - distance]

        total = own_piece(reach)
        for distance in range(reach - 1, -1, -1):
            moved = passed_along(low(total), RING, -1).astype(jnp.float32)
            total = moved + own_piece(distance)
    grad_kv = total.astype(jnp.bfloat16)
    grad_key = grad_kv[:, :kv_width]
    grad_value = grad_kv[:, kv_width:]

    values = [grad_value]
    for steps in range(1, fsdp_count):
        values.append(rotated(grad_value, "fsdp", steps))
    stacked_inputs = jnp.concatenate(inputs, axis=0)
    stacked_values = jnp.concatenate(values, axis=0)
    shard = lax.dot_general(stacked_inputs, stacked_values, TN, preferred_element_type=jnp.float32)
    token_scale = float(fsdp_count * lax.axis_size(RING) * block_rows) ** (-0.5)
    scale_early = token_scale == 2.0 ** round(math.log2(token_scale))
    if scale_early:
        shard = shard * token_scale

    sub_count = lax.axis_size("sub")
    sub_at = lax.axis_index("sub")
    piece_rows = shard_rows // sub_count
    mine = lax.dynamic_slice_in_dim(shard, sub_at * piece_rows, piece_rows, axis=0)
    for steps in range(1, sub_count):
        target = (sub_at + steps) % sub_count
        outgoing = lax.dynamic_slice_in_dim(shard, target * piece_rows, piece_rows, axis=0)
        mine = mine + rotated(outgoing.astype(jnp.bfloat16), "sub", steps).astype(jnp.float32)
    reduced = ring_sum(mine, "ctx")
    if sub_count == 2:
        other = rotated(reduced.astype(jnp.bfloat16), "sub", 1).astype(jnp.float32)
        first = jnp.where(sub_at == 0, reduced, other)
        second = jnp.where(sub_at == 0, other, reduced)
        weight_v = jnp.concatenate([first, second], axis=0)
    else:
        weight_v = lax.all_gather(reduced, "sub", axis=0, tiled=True)
    if not scale_early:
        weight_v = weight_v * token_scale
    return (
        grad_q[None],
        grad_key[None],
        grad_value[None],
        weight_v,
    )


def solution(mesh):
    placed = (
        P(("groups", "fsdp"), ("ctx", "sub"), None),
        P(("groups", "fsdp"), ("ctx", "sub"), None),
        P(("groups", "fsdp"), ("ctx", "sub"), None),
        P(("groups", "fsdp"), ("ctx", "sub"), None),
        P(("groups", "fsdp"), ("ctx", "sub"), None),
        P(("groups", "fsdp"), None),
    )
    return jax.shard_map(
        body,
        mesh=mesh,
        in_specs=placed,
        out_specs=(
            P(("groups", "fsdp"), ("ctx", "sub"), None),
            P(("groups", "fsdp"), ("ctx", "sub"), None),
            P(("groups", "fsdp"), ("ctx", "sub"), None),
            P(("groups", "fsdp"), None),
        ),
        check_vma=False,
    )
```

```python
import functools
import math

import jax
import jax.numpy as jnp
from jax import lax
from jax.experimental import pallas as pl
from jax.experimental.pallas import tpu as pltpu
from jax.sharding import PartitionSpec as P

HEAD_DIM = 256
SPAN = 768
RING = ("ctx", "sub")
NT = (((1,), (1,)), ((), ()))
TN = (((0,), (0,)), ((), ()))


def passed_along(value, axis, steps):
    count = lax.axis_size(axis)
    first, last = (max(0, -steps), min(count, count - steps))
    return lax.ppermute(value, axis, [(source, source + steps) for source in range(first, last)])


def rotated(value, axis, steps):
    count = lax.axis_size(axis)
    return lax.ppermute(value, axis, [(source, (source + steps) % count) for source in range(count)])


def ring_sum(piece, axis):
    count = lax.axis_size(axis)
    at = lax.axis_index(axis)
    rows = piece.shape[0] // count
    total = lax.dynamic_slice_in_dim(piece, at * rows, rows, axis=0)
    for steps in range(1, count):
        outgoing = lax.dynamic_slice_in_dim(piece, ((at + steps) % count) * rows, rows, axis=0)
        total = total + rotated(outgoing.astype(jnp.bfloat16), axis, steps).astype(jnp.float32)
    low = total.astype(jnp.bfloat16)
    gathered = jnp.zeros(piece.shape, jnp.float32)
    gathered = lax.dynamic_update_slice_in_dim(gathered, total, at * rows, axis=0)
    for steps in range(1, count):
        arrived = rotated(low, axis, steps).astype(jnp.float32)
        gathered = lax.dynamic_update_slice_in_dim(
            gathered, arrived, ((at - steps) % count) * rows, axis=0
        )
    return gathered


def doc_start_of(starts, positions):
    covered = starts[None, :] <= positions[:, None]
    return jnp.max(jnp.where(covered, starts[None, :], 0), axis=1)


def attention_kernel(*refs, heads, kv_heads, margin, slots, blocks, chip_outputs):
    flag_ref, lo_ref, q_ref, do_ref = refs[:4]
    block_refs = refs[4 : 4 + blocks]
    kv_ref, dkv_ref = refs[-2:]
    outs = refs[-3 - len(slots) : -2]
    dq_ref = outs[0]
    out_refs = outs[1:]
    block_rows = block_refs[0].shape[0]
    flag = flag_ref[0]
    for index, (when_low, when_high) in enumerate(slots):
        target = kv_ref.at[pl.ds(index * block_rows, block_rows), :]
        if when_low == when_high:
            target[...] = block_refs[when_low][...]
        else:

            @pl.when(flag == 0)
            def _():
                target[...] = block_refs[when_low][...]

            @pl.when(flag != 0)
            def _():
                target[...] = block_refs[when_high][...]

    rows = q_ref.shape[0]
    keys = kv_ref.shape[0]
    scale = HEAD_DIM ** (-0.5)
    kv_width = kv_heads * HEAD_DIM
    per_group = heads // kv_heads
    col = lax.broadcasted_iota(jnp.int32, (rows, keys), 1)
    row = lax.broadcasted_iota(jnp.int32, (rows, keys), 0)
    allowed = (col >= lo_ref[...]) & (col <= row + margin)
    for group in range(kv_heads):
        k_cols = pl.ds(group * HEAD_DIM, HEAD_DIM)
        v_cols = pl.ds(kv_width + group * HEAD_DIM, HEAD_DIM)
        key_g = kv_ref[:, k_cols]
        value_g = kv_ref[:, v_cols]
        grad_k = None
        grad_v = None
        for member in range(per_group):
            q_cols = pl.ds((group * per_group + member) * HEAD_DIM, HEAD_DIM)
            query_h = q_ref[:, q_cols]
            grad_h = do_ref[:, q_cols]
            scores = lax.dot_general(query_h, key_g, NT, preferred_element_type=jnp.float32) * scale
            scores = jnp.where(allowed, scores, -1e30)
            largest = jnp.max(scores, axis=1, keepdims=True)
            raised = jnp.exp(scores - largest)
            probs = raised * (1.0 / jnp.sum(raised, axis=1, keepdims=True))
            grad_probs = lax.dot_general(grad_h, value_g, NT, preferred_element_type=jnp.float32)
            row_dot = jnp.sum(probs * grad_probs, axis=1, keepdims=True)
            grad_scores = (probs * (grad_probs - row_dot) * scale).astype(jnp.bfloat16)
            probs_low = probs.astype(jnp.bfloat16)
            dq_ref[:, q_cols] = jnp.dot(
                grad_scores, key_g, preferred_element_type=jnp.float32
            ).astype(dq_ref.dtype)
            term_k = lax.dot_general(grad_scores, query_h, TN, preferred_element_type=jnp.float32)
            term_v = lax.dot_general(probs_low, grad_h, TN, preferred_element_type=jnp.float32)
            grad_k = term_k if grad_k is None else grad_k + term_k
            grad_v = term_v if grad_v is None else grad_v + term_v
        dkv_ref[:, k_cols] = grad_k
        dkv_ref[:, v_cols] = grad_v
    def slot_rows(index):
        return dkv_ref[pl.ds(index * block_rows, block_rows), :]

    if chip_outputs:
        mate_ref, other_ref, two_ref, own_ref = out_refs
        two_ref[...] = slot_rows(1)
        own_ref[...] = slot_rows(3)

        @pl.when(flag == 0)
        def _():
            mate_ref[...] = slot_rows(2).astype(mate_ref.dtype)
            other_ref[...] = slot_rows(0).astype(other_ref.dtype)

        @pl.when(flag != 0)
        def _():
            mate_ref[...] = slot_rows(0).astype(mate_ref.dtype)
            other_ref[...] = slot_rows(2).astype(other_ref.dtype)

    else:
        for index, out_ref in enumerate(out_refs):
            out_ref[...] = slot_rows(index)


def attention(
    flag, lo_rel, queries, grads, kv_blocks, slots, heads, kv_heads, margin, early, chip_outputs
):
    rows, width = queries.shape
    blocks = len(kv_blocks)
    block_rows, kv_cols = kv_blocks[0].shape
    keys = len(slots) * block_rows
    kernel = functools.partial(
        attention_kernel,
        heads=heads,
        kv_heads=kv_heads,
        margin=margin,
        slots=tuple(slots),
        blocks=blocks,
        chip_outputs=chip_outputs,
    )
    if chip_outputs:
        piece_types = [jnp.bfloat16, jnp.bfloat16, jnp.float32, jnp.float32]
    else:
        piece_types = [jnp.float32] * len(slots)
    vmem = pl.BlockSpec(memory_space=pltpu.VMEM)
    smem = pl.BlockSpec(memory_space=pltpu.SMEM)
    flops = 2 * 5 * heads * rows * keys * HEAD_DIM
    moved = 2 * (2 * rows * width + keys * kv_cols + rows * width) + 4 * keys * kv_cols
    return pl.pallas_call(
        kernel,
        out_shape=(jax.ShapeDtypeStruct((rows, width), jnp.bfloat16),)
        + tuple(jax.ShapeDtypeStruct((block_rows, kv_cols), kind) for kind in piece_types),
        in_specs=[smem] + [vmem] * (3 + blocks) + [pl.BlockSpec(memory_space=pl.ANY)] * len(early),
        out_specs=(vmem,) * (1 + len(slots)),
        scratch_shapes=[
            pltpu.VMEM((keys, kv_cols), kv_blocks[0].dtype),
            pltpu.VMEM((keys, kv_cols), jnp.float32),
        ],
        cost_estimate=pl.CostEstimate(
            flops=flops, transcendentals=heads * rows * keys, bytes_accessed=moved
        ),
    )(flag, lo_rel, queries, grads, *kv_blocks, *early)


def body(layer_input, query_heads, key_heads, value_heads, grad_out, doc_starts):
    block_rows = query_heads.shape[1]
    window = min(SPAN, lax.axis_size(RING) * block_rows // 2)
    reach = (window + block_rows - 2) // block_rows
    margin = reach * block_rows
    kv_width = key_heads.shape[2]
    heads = query_heads.shape[2] // HEAD_DIM
    kv_heads = kv_width // HEAD_DIM
    first_row = lax.axis_index(RING) * block_rows

    fsdp_count = lax.axis_size("fsdp")
    fsdp_at = lax.axis_index("fsdp")
    model_width = layer_input.shape[2]
    shard_rows = model_width // fsdp_count
    own_input = layer_input[0]
    inputs = [lax.dynamic_slice_in_dim(own_input, fsdp_at * shard_rows, shard_rows, axis=1)]
    for steps in range(1, fsdp_count):
        target = (fsdp_at + steps) % fsdp_count
        outgoing = lax.dynamic_slice_in_dim(own_input, target * shard_rows, shard_rows, axis=1)
        inputs.append(rotated(outgoing, "fsdp", steps))

    own_kv = jnp.concatenate([key_heads[0], value_heads[0]], axis=1)
    query_pos = first_row + jnp.arange(block_rows, dtype=jnp.int32)
    lowest = jnp.maximum(doc_start_of(doc_starts[0], query_pos), query_pos - window + 1)
    lo_rel = (lowest - first_row + margin).astype(jnp.int32)[:, None]
    sub_count = lax.axis_size("sub")
    sub_at = lax.axis_index("sub")
    flag = jnp.reshape(sub_at, (1,)).astype(jnp.int32)
    chip_route = sub_count == 2 and reach == 3
    if chip_route:
        ring_count = lax.axis_size(RING)
        across = [(2 * chip - 3, 2 * chip) for chip in range(2, ring_count // 2)]
        two_back = passed_along(own_kv, "ctx", 1)
        one_back_high = passed_along(own_kv, "sub", 1)
        three_back_low = lax.ppermute(own_kv, RING, across)
        swapped = rotated(two_back, "sub", 1)
        kv_blocks = [two_back, one_back_high, three_back_low, swapped, own_kv]
        slots = [(2, 3), (0, 0), (3, 1), (4, 4)]
    else:
        arrived = []
        moving = own_kv
        for _ in range(reach):
            moving = passed_along(moving, RING, 1)
            arrived.append(moving)
        kv_blocks = arrived[::-1] + [own_kv]
        slots = [(index, index) for index in range(reach + 1)]
    grad_q, *grad_pieces = attention(
        flag, lo_rel, query_heads[0], grad_out[0], kv_blocks, slots, heads, kv_heads, margin,
        inputs[1:],
        chip_route,
    )

    def low(value):
        return value.astype(jnp.bfloat16)

    if chip_route:
        back = [(target, source) for source, target in across]
        to_mate, to_other, g2, g0 = grad_pieces
        from_far = lax.ppermute(to_other, RING, back).astype(jnp.float32)
        from_mate = rotated(to_mate, "sub", 1).astype(jnp.float32)
        from_high = passed_along(to_other, "sub", -1).astype(jnp.float32)
        two_back_sum = g2 + from_mate
        from_next = passed_along(low(two_back_sum), "ctx", -1).astype(jnp.float32)
        total = g0 + from_high + from_far + from_next
    else:

        def own_piece(distance):
            return grad_pieces[reach - distance]

        total = own_piece(reach)
        for distance in range(reach - 1, -1, -1):
            moved = passed_along(low(total), RING, -1).astype(jnp.float32)
            total = moved + own_piece(distance)
    grad_kv = total.astype(jnp.bfloat16)
    grad_key = grad_kv[:, :kv_width]
    grad_value = grad_kv[:, kv_width:]

    values = [grad_value]
    for steps in range(1, fsdp_count):
        values.append(rotated(grad_value, "fsdp", steps))
    stacked_inputs = jnp.concatenate(inputs, axis=0)
    stacked_values = jnp.concatenate(values, axis=0)
    shard = lax.dot_general(stacked_inputs, stacked_values, TN, preferred_element_type=jnp.float32)
    token_scale = float(fsdp_count * lax.axis_size(RING) * block_rows) ** (-0.5)
    scale_early = token_scale == 2.0 ** round(math.log2(token_scale))
    if scale_early:
        shard = shard * token_scale

    sub_count = lax.axis_size("sub")
    sub_at = lax.axis_index("sub")
    piece_rows = shard_rows // sub_count
    mine = lax.dynamic_slice_in_dim(shard, sub_at * piece_rows, piece_rows, axis=0)
    for steps in range(1, sub_count):
        target = (sub_at + steps) % sub_count
        outgoing = lax.dynamic_slice_in_dim(shard, target * piece_rows, piece_rows, axis=0)
        mine = mine + rotated(outgoing.astype(jnp.bfloat16), "sub", steps).astype(jnp.float32)
    reduced = ring_sum(mine, "ctx")
    if sub_count == 2:
        other = rotated(reduced.astype(jnp.bfloat16), "sub", 1).astype(jnp.float32)
        weight_v = jnp.zeros((shard_rows, reduced.shape[1]), jnp.float32)
        weight_v = lax.dynamic_update_slice_in_dim(weight_v, reduced, sub_at * piece_rows, axis=0)
        weight_v = lax.dynamic_update_slice_in_dim(
            weight_v, other, (1 - sub_at) * piece_rows, axis=0
        )
    else:
        weight_v = lax.all_gather(reduced, "sub", axis=0, tiled=True)
    if not scale_early:
        weight_v = weight_v * token_scale
    return (
        grad_q[None],
        grad_key[None],
        grad_value[None],
        weight_v,
    )


def solution(mesh):
    placed = (
        P(("groups", "fsdp"), ("ctx", "sub"), None),
        P(("groups", "fsdp"), ("ctx", "sub"), None),
        P(("groups", "fsdp"), ("ctx", "sub"), None),
        P(("groups", "fsdp"), ("ctx", "sub"), None),
        P(("groups", "fsdp"), ("ctx", "sub"), None),
        P(("groups", "fsdp"), None),
    )
    return jax.shard_map(
        body,
        mesh=mesh,
        in_specs=placed,
        out_specs=(
            P(("groups", "fsdp"), ("ctx", "sub"), None),
            P(("groups", "fsdp"), ("ctx", "sub"), None),
            P(("groups", "fsdp"), ("ctx", "sub"), None),
            P(("groups", "fsdp"), None),
        ),
        check_vma=False,
    )
```

```python
import functools
import math

import jax
import jax.numpy as jnp
from jax import lax
from jax.experimental import pallas as pl
from jax.experimental.pallas import tpu as pltpu
from jax.sharding import PartitionSpec as P

HEAD_DIM = 256
SPAN = 768
RING = ("ctx", "sub")
NT = (((1,), (1,)), ((), ()))
TN = (((0,), (0,)), ((), ()))


def passed_along(value, axis, steps):
    count = lax.axis_size(axis)
    first, last = (max(0, -steps), min(count, count - steps))
    return lax.ppermute(value, axis, [(source, source + steps) for source in range(first, last)])


def rotated(value, axis, steps):
    count = lax.axis_size(axis)
    return lax.ppermute(value, axis, [(source, (source + steps) % count) for source in range(count)])


def ring_sum(piece, axis):
    count = lax.axis_size(axis)
    at = lax.axis_index(axis)
    rows = piece.shape[0] // count
    total = lax.dynamic_slice_in_dim(piece, at * rows, rows, axis=0)
    for steps in range(1, count):
        outgoing = lax.dynamic_slice_in_dim(piece, ((at + steps) % count) * rows, rows, axis=0)
        total = total + rotated(outgoing.astype(jnp.bfloat16), axis, steps).astype(jnp.float32)
    low = total.astype(jnp.bfloat16)
    gathered = jnp.zeros(piece.shape, jnp.float32)
    gathered = lax.dynamic_update_slice_in_dim(gathered, total, at * rows, axis=0)
    for steps in range(1, count):
        arrived = rotated(low, axis, steps).astype(jnp.float32)
        gathered = lax.dynamic_update_slice_in_dim(
            gathered, arrived, ((at - steps) % count) * rows, axis=0
        )
    return gathered


def doc_start_of(starts, positions):
    covered = starts[None, :] <= positions[:, None]
    return jnp.max(jnp.where(covered, starts[None, :], 0), axis=1)


def attention_kernel(*refs, heads, kv_heads, margin, slots, blocks, chip_outputs):
    flag_ref, lo_ref, q_ref, do_ref = refs[:4]
    block_refs = refs[4 : 4 + blocks]
    kv_ref, dkv_ref = refs[-2:]
    outs = refs[-3 - len(slots) : -2]
    dq_ref = outs[0]
    out_refs = outs[1:]
    block_rows = block_refs[0].shape[0]
    flag = flag_ref[0]
    for index, (when_low, when_high) in enumerate(slots):
        target = kv_ref.at[pl.ds(index * block_rows, block_rows), :]
        if when_low == when_high:
            target[...] = block_refs[when_low][...]
        else:

            @pl.when(flag == 0)
            def _():
                target[...] = block_refs[when_low][...]

            @pl.when(flag != 0)
            def _():
                target[...] = block_refs[when_high][...]

    rows = q_ref.shape[0]
    keys = kv_ref.shape[0]
    scale = HEAD_DIM ** (-0.5)
    kv_width = kv_heads * HEAD_DIM
    per_group = heads // kv_heads
    half = rows // 2
    reach_keys = keys - half
    col = lax.broadcasted_iota(jnp.int32, (half, reach_keys), 1)
    row = lax.broadcasted_iota(jnp.int32, (half, reach_keys), 0)
    allowed = [
        (col + part * half >= lo_ref[pl.ds(part * half, half), :])
        & (col + part * half <= row + part * half + margin)
        for part in range(2)
    ]
    for group in range(kv_heads):
        k_cols = pl.ds(group * HEAD_DIM, HEAD_DIM)
        v_cols = pl.ds(kv_width + group * HEAD_DIM, HEAD_DIM)
        sums_k = [None, None]
        sums_v = [None, None]
        for member in range(per_group):
            q_cols = pl.ds((group * per_group + member) * HEAD_DIM, HEAD_DIM)
            for part in range(2):
                part_rows = pl.ds(part * half, half)
                part_keys = pl.ds(part * half, reach_keys)
                key_g = kv_ref[part_keys, k_cols]
                value_g = kv_ref[part_keys, v_cols]
                query_h = q_ref[part_rows, q_cols]
                grad_h = do_ref[part_rows, q_cols]
                scores = lax.dot_general(query_h, key_g, NT, preferred_element_type=jnp.float32) * scale
                scores = jnp.where(allowed[part], scores, -1e30)
                largest = jnp.max(scores, axis=1, keepdims=True)
                raised = jnp.exp(scores - largest)
                probs = raised * (1.0 / jnp.sum(raised, axis=1, keepdims=True))
                grad_probs = lax.dot_general(grad_h, value_g, NT, preferred_element_type=jnp.float32)
                row_dot = jnp.sum(probs * grad_probs, axis=1, keepdims=True)
                grad_scores = (probs * (grad_probs - row_dot) * scale).astype(jnp.bfloat16)
                probs_low = probs.astype(jnp.bfloat16)
                dq_ref[part_rows, q_cols] = jnp.dot(
                    grad_scores, key_g, preferred_element_type=jnp.float32
                ).astype(dq_ref.dtype)
                term_k = lax.dot_general(grad_scores, query_h, TN, preferred_element_type=jnp.float32)
                term_v = lax.dot_general(probs_low, grad_h, TN, preferred_element_type=jnp.float32)
                sums_k[part] = term_k if sums_k[part] is None else sums_k[part] + term_k
                sums_v[part] = term_v if sums_v[part] is None else sums_v[part] + term_v
        for cols, sums in ((k_cols, sums_k), (v_cols, sums_v)):
            dkv_ref[pl.ds(0, half), cols] = sums[0][:half]
            dkv_ref[pl.ds(half, reach_keys - half), cols] = sums[0][half:] + sums[1][: reach_keys - half]
            dkv_ref[pl.ds(reach_keys, half), cols] = sums[1][reach_keys - half :]
    def slot_rows(index):
        return dkv_ref[pl.ds(index * block_rows, block_rows), :]

    if chip_outputs:
        mate_ref, other_ref, two_ref, own_ref = out_refs
        two_ref[...] = slot_rows(1)
        own_ref[...] = slot_rows(3)

        @pl.when(flag == 0)
        def _():
            mate_ref[...] = slot_rows(2).astype(mate_ref.dtype)
            other_ref[...] = slot_rows(0).astype(other_ref.dtype)

        @pl.when(flag != 0)
        def _():
            mate_ref[...] = slot_rows(0).astype(mate_ref.dtype)
            other_ref[...] = slot_rows(2).astype(other_ref.dtype)

    else:
        for index, out_ref in enumerate(out_refs):
            out_ref[...] = slot_rows(index)


def attention(
    flag, lo_rel, queries, grads, kv_blocks, slots, heads, kv_heads, margin, early, chip_outputs
):
    rows, width = queries.shape
    blocks = len(kv_blocks)
    block_rows, kv_cols = kv_blocks[0].shape
    keys = len(slots) * block_rows
    kernel = functools.partial(
        attention_kernel,
        heads=heads,
        kv_heads=kv_heads,
        margin=margin,
        slots=tuple(slots),
        blocks=blocks,
        chip_outputs=chip_outputs,
    )
    if chip_outputs:
        piece_types = [jnp.bfloat16, jnp.bfloat16, jnp.float32, jnp.float32]
    else:
        piece_types = [jnp.float32] * len(slots)
    vmem = pl.BlockSpec(memory_space=pltpu.VMEM)
    smem = pl.BlockSpec(memory_space=pltpu.SMEM)
    flops = 2 * 5 * heads * rows * keys * HEAD_DIM
    moved = 2 * (2 * rows * width + keys * kv_cols + rows * width) + 4 * keys * kv_cols
    return pl.pallas_call(
        kernel,
        out_shape=(jax.ShapeDtypeStruct((rows, width), jnp.bfloat16),)
        + tuple(jax.ShapeDtypeStruct((block_rows, kv_cols), kind) for kind in piece_types),
        in_specs=[smem] + [vmem] * (3 + blocks) + [pl.BlockSpec(memory_space=pl.ANY)] * len(early),
        out_specs=(vmem,) * (1 + len(slots)),
        scratch_shapes=[
            pltpu.VMEM((keys, kv_cols), kv_blocks[0].dtype),
            pltpu.VMEM((keys, kv_cols), jnp.float32),
        ],
        cost_estimate=pl.CostEstimate(
            flops=flops, transcendentals=heads * rows * keys, bytes_accessed=moved
        ),
    )(flag, lo_rel, queries, grads, *kv_blocks, *early)


def body(layer_input, query_heads, key_heads, value_heads, grad_out, doc_starts):
    block_rows = query_heads.shape[1]
    window = min(SPAN, lax.axis_size(RING) * block_rows // 2)
    reach = (window + block_rows - 2) // block_rows
    margin = reach * block_rows
    kv_width = key_heads.shape[2]
    heads = query_heads.shape[2] // HEAD_DIM
    kv_heads = kv_width // HEAD_DIM
    first_row = lax.axis_index(RING) * block_rows

    fsdp_count = lax.axis_size("fsdp")
    fsdp_at = lax.axis_index("fsdp")
    model_width = layer_input.shape[2]
    shard_rows = model_width // fsdp_count
    own_input = layer_input[0]
    inputs = [lax.dynamic_slice_in_dim(own_input, fsdp_at * shard_rows, shard_rows, axis=1)]
    for steps in range(1, fsdp_count):
        target = (fsdp_at + steps) % fsdp_count
        outgoing = lax.dynamic_slice_in_dim(own_input, target * shard_rows, shard_rows, axis=1)
        inputs.append(rotated(outgoing, "fsdp", steps))

    own_kv = jnp.concatenate([key_heads[0], value_heads[0]], axis=1)
    query_pos = first_row + jnp.arange(block_rows, dtype=jnp.int32)
    lowest = jnp.maximum(doc_start_of(doc_starts[0], query_pos), query_pos - window + 1)
    lo_rel = (lowest - first_row + margin).astype(jnp.int32)[:, None]
    sub_count = lax.axis_size("sub")
    sub_at = lax.axis_index("sub")
    flag = jnp.reshape(sub_at, (1,)).astype(jnp.int32)
    chip_route = sub_count == 2 and reach == 3
    if chip_route:
        ring_count = lax.axis_size(RING)
        across = [(2 * chip - 3, 2 * chip) for chip in range(2, ring_count // 2)]
        two_back = passed_along(own_kv, "ctx", 1)
        one_back_high = passed_along(own_kv, "sub", 1)
        three_back_low = lax.ppermute(own_kv, RING, across)
        swapped = rotated(two_back, "sub", 1)
        kv_blocks = [two_back, one_back_high, three_back_low, swapped, own_kv]
        slots = [(2, 3), (0, 0), (3, 1), (4, 4)]
    else:
        arrived = []
        moving = own_kv
        for _ in range(reach):
            moving = passed_along(moving, RING, 1)
            arrived.append(moving)
        kv_blocks = arrived[::-1] + [own_kv]
        slots = [(index, index) for index in range(reach + 1)]
    grad_q, *grad_pieces = attention(
        flag, lo_rel, query_heads[0], grad_out[0], kv_blocks, slots, heads, kv_heads, margin,
        inputs[1:],
        chip_route,
    )

    def low(value):
        return value.astype(jnp.bfloat16)

    if chip_route:
        back = [(target, source) for source, target in across]
        to_mate, to_other, g2, g0 = grad_pieces
        from_far = lax.ppermute(to_other, RING, back).astype(jnp.float32)
        from_mate = rotated(to_mate, "sub", 1).astype(jnp.float32)
        from_high = passed_along(to_other, "sub", -1).astype(jnp.float32)
        two_back_sum = g2 + from_mate
        from_next = passed_along(low(two_back_sum), "ctx", -1).astype(jnp.float32)
        total = g0 + from_high + from_far + from_next
    else:

        def own_piece(distance):
            return grad_pieces[reach - distance]

        total = own_piece(reach)
        for distance in range(reach - 1, -1, -1):
            moved = passed_along(low(total), RING, -1).astype(jnp.float32)
            total = moved + own_piece(distance)
    grad_kv = total.astype(jnp.bfloat16)
    grad_key = grad_kv[:, :kv_width]
    grad_value = grad_kv[:, kv_width:]

    values = [grad_value]
    for steps in range(1, fsdp_count):
        values.append(rotated(grad_value, "fsdp", steps))
    stacked_inputs = jnp.concatenate(inputs, axis=0)
    stacked_values = jnp.concatenate(values, axis=0)
    shard = lax.dot_general(stacked_inputs, stacked_values, TN, preferred_element_type=jnp.float32)
    token_scale = float(fsdp_count * lax.axis_size(RING) * block_rows) ** (-0.5)
    scale_early = token_scale == 2.0 ** round(math.log2(token_scale))
    if scale_early:
        shard = shard * token_scale

    sub_count = lax.axis_size("sub")
    sub_at = lax.axis_index("sub")
    piece_rows = shard_rows // sub_count
    mine = lax.dynamic_slice_in_dim(shard, sub_at * piece_rows, piece_rows, axis=0)
    for steps in range(1, sub_count):
        target = (sub_at + steps) % sub_count
        outgoing = lax.dynamic_slice_in_dim(shard, target * piece_rows, piece_rows, axis=0)
        mine = mine + rotated(outgoing.astype(jnp.bfloat16), "sub", steps).astype(jnp.float32)
    reduced = ring_sum(mine, "ctx")
    if sub_count == 2:
        other = rotated(reduced.astype(jnp.bfloat16), "sub", 1).astype(jnp.float32)
        first = jnp.where(sub_at == 0, reduced, other)
        second = jnp.where(sub_at == 0, other, reduced)
        weight_v = jnp.concatenate([first, second], axis=0)
    else:
        weight_v = lax.all_gather(reduced, "sub", axis=0, tiled=True)
    if not scale_early:
        weight_v = weight_v * token_scale
    return (
        grad_q[None],
        grad_key[None],
        grad_value[None],
        weight_v,
    )


def solution(mesh):
    placed = (
        P(("groups", "fsdp"), ("ctx", "sub"), None),
        P(("groups", "fsdp"), ("ctx", "sub"), None),
        P(("groups", "fsdp"), ("ctx", "sub"), None),
        P(("groups", "fsdp"), ("ctx", "sub"), None),
        P(("groups", "fsdp"), ("ctx", "sub"), None),
        P(("groups", "fsdp"), None),
    )
    return jax.shard_map(
        body,
        mesh=mesh,
        in_specs=placed,
        out_specs=(
            P(("groups", "fsdp"), ("ctx", "sub"), None),
            P(("groups", "fsdp"), ("ctx", "sub"), None),
            P(("groups", "fsdp"), ("ctx", "sub"), None),
            P(("groups", "fsdp"), None),
        ),
        check_vma=False,
    )
```

```python
import functools
import math

import jax
import jax.numpy as jnp
from jax import lax
from jax.experimental import pallas as pl
from jax.experimental.pallas import tpu as pltpu
from jax.sharding import PartitionSpec as P

HEAD_DIM = 256
SPAN = 768
RING = ("ctx", "sub")
NT = (((1,), (1,)), ((), ()))
TN = (((0,), (0,)), ((), ()))


def passed_along(value, axis, steps):
    count = lax.axis_size(axis)
    first, last = (max(0, -steps), min(count, count - steps))
    return lax.ppermute(value, axis, [(source, source + steps) for source in range(first, last)])


def rotated(value, axis, steps):
    count = lax.axis_size(axis)
    return lax.ppermute(value, axis, [(source, (source + steps) % count) for source in range(count)])


def ring_sum(piece, axis):
    count = lax.axis_size(axis)
    at = lax.axis_index(axis)
    rows = piece.shape[0] // count
    total = lax.dynamic_slice_in_dim(piece, at * rows, rows, axis=0)
    for steps in range(1, count):
        outgoing = lax.dynamic_slice_in_dim(piece, ((at + steps) % count) * rows, rows, axis=0)
        total = total + rotated(outgoing.astype(jnp.bfloat16), axis, steps).astype(jnp.float32)
    low = total.astype(jnp.bfloat16)
    gathered = jnp.zeros(piece.shape, jnp.float32)
    gathered = lax.dynamic_update_slice_in_dim(gathered, total, at * rows, axis=0)
    for steps in range(1, count):
        arrived = rotated(low, axis, steps).astype(jnp.float32)
        gathered = lax.dynamic_update_slice_in_dim(
            gathered, arrived, ((at - steps) % count) * rows, axis=0
        )
    return gathered


def doc_start_of(starts, positions):
    covered = starts[None, :] <= positions[:, None]
    return jnp.max(jnp.where(covered, starts[None, :], 0), axis=1)


def attention_kernel(*refs, heads, kv_heads, margin, slots, blocks, chip_outputs):
    flag_ref, lo_ref, q_ref, do_ref = refs[:4]
    block_refs = refs[4 : 4 + blocks]
    kv_ref = refs[-1]
    outs = refs[-2 - len(slots) : -1]
    dq_ref = outs[0]
    out_refs = outs[1:]
    block_rows = block_refs[0].shape[0]
    flag = flag_ref[0]
    for index, (when_low, when_high) in enumerate(slots):
        target = kv_ref.at[pl.ds(index * block_rows, block_rows), :]
        if when_low == when_high:
            target[...] = block_refs[when_low][...]
        else:

            @pl.when(flag == 0)
            def _():
                target[...] = block_refs[when_low][...]

            @pl.when(flag != 0)
            def _():
                target[...] = block_refs[when_high][...]

    rows = q_ref.shape[0]
    keys = kv_ref.shape[0]
    scale = HEAD_DIM ** (-0.5)
    kv_width = kv_heads * HEAD_DIM
    per_group = heads // kv_heads
    col = lax.broadcasted_iota(jnp.int32, (rows, keys), 1)
    row = lax.broadcasted_iota(jnp.int32, (rows, keys), 0)
    allowed = (col >= lo_ref[...]) & (col <= row + margin)

    def emit(cols, full):
        pieces = [full[index * block_rows : (index + 1) * block_rows] for index in range(len(slots))]
        if not chip_outputs:
            for out_ref, piece in zip(out_refs, pieces):
                out_ref[:, cols] = piece
            return
        mate_ref, other_ref, two_ref, own_ref = out_refs
        two_ref[:, cols] = pieces[1]
        own_ref[:, cols] = pieces[3]

        @pl.when(flag == 0)
        def _():
            mate_ref[:, cols] = pieces[2].astype(mate_ref.dtype)
            other_ref[:, cols] = pieces[0].astype(other_ref.dtype)

        @pl.when(flag != 0)
        def _():
            mate_ref[:, cols] = pieces[0].astype(mate_ref.dtype)
            other_ref[:, cols] = pieces[2].astype(other_ref.dtype)

    for group in range(kv_heads):
        k_cols = pl.ds(group * HEAD_DIM, HEAD_DIM)
        v_cols = pl.ds(kv_width + group * HEAD_DIM, HEAD_DIM)
        key_g = kv_ref[:, k_cols]
        value_g = kv_ref[:, v_cols]
        grad_k = None
        grad_v = None
        for member in range(per_group):
            q_cols = pl.ds((group * per_group + member) * HEAD_DIM, HEAD_DIM)
            query_h = q_ref[:, q_cols]
            grad_h = do_ref[:, q_cols]
            scores = lax.dot_general(query_h, key_g, NT, preferred_element_type=jnp.float32) * scale
            scores = jnp.where(allowed, scores, -1e30)
            largest = jnp.max(scores, axis=1, keepdims=True)
            raised = jnp.exp(scores - largest)
            probs = raised * (1.0 / jnp.sum(raised, axis=1, keepdims=True))
            grad_probs = lax.dot_general(grad_h, value_g, NT, preferred_element_type=jnp.float32)
            row_dot = jnp.sum(probs * grad_probs, axis=1, keepdims=True)
            grad_scores = (probs * (grad_probs - row_dot) * scale).astype(jnp.bfloat16)
            probs_low = probs.astype(jnp.bfloat16)
            dq_ref[:, q_cols] = jnp.dot(
                grad_scores, key_g, preferred_element_type=jnp.float32
            ).astype(dq_ref.dtype)
            term_k = lax.dot_general(grad_scores, query_h, TN, preferred_element_type=jnp.float32)
            term_v = lax.dot_general(probs_low, grad_h, TN, preferred_element_type=jnp.float32)
            grad_k = term_k if grad_k is None else grad_k + term_k
            grad_v = term_v if grad_v is None else grad_v + term_v
        emit(k_cols, grad_k)
        emit(v_cols, grad_v)


def attention(
    flag, lo_rel, queries, grads, kv_blocks, slots, heads, kv_heads, margin, early, chip_outputs
):
    rows, width = queries.shape
    blocks = len(kv_blocks)
    block_rows, kv_cols = kv_blocks[0].shape
    keys = len(slots) * block_rows
    kernel = functools.partial(
        attention_kernel,
        heads=heads,
        kv_heads=kv_heads,
        margin=margin,
        slots=tuple(slots),
        blocks=blocks,
        chip_outputs=chip_outputs,
    )
    if chip_outputs:
        piece_types = [jnp.bfloat16, jnp.bfloat16, jnp.float32, jnp.float32]
    else:
        piece_types = [jnp.float32] * len(slots)
    vmem = pl.BlockSpec(memory_space=pltpu.VMEM)
    smem = pl.BlockSpec(memory_space=pltpu.SMEM)
    flops = 2 * 5 * heads * rows * keys * HEAD_DIM
    moved = 2 * (2 * rows * width + keys * kv_cols + rows * width) + 4 * keys * kv_cols
    return pl.pallas_call(
        kernel,
        out_shape=(jax.ShapeDtypeStruct((rows, width), jnp.bfloat16),)
        + tuple(jax.ShapeDtypeStruct((block_rows, kv_cols), kind) for kind in piece_types),
        in_specs=[smem] + [vmem] * (3 + blocks) + [pl.BlockSpec(memory_space=pl.ANY)] * len(early),
        out_specs=(vmem,) * (1 + len(slots)),
        scratch_shapes=[pltpu.VMEM((keys, kv_cols), kv_blocks[0].dtype)],
        cost_estimate=pl.CostEstimate(
            flops=flops, transcendentals=heads * rows * keys, bytes_accessed=moved
        ),
    )(flag, lo_rel, queries, grads, *kv_blocks, *early)


def body(layer_input, query_heads, key_heads, value_heads, grad_out, doc_starts):
    block_rows = query_heads.shape[1]
    window = min(SPAN, lax.axis_size(RING) * block_rows // 2)
    reach = (window + block_rows - 2) // block_rows
    margin = reach * block_rows
    kv_width = key_heads.shape[2]
    heads = query_heads.shape[2] // HEAD_DIM
    kv_heads = kv_width // HEAD_DIM
    first_row = lax.axis_index(RING) * block_rows

    fsdp_count = lax.axis_size("fsdp")
    fsdp_at = lax.axis_index("fsdp")
    model_width = layer_input.shape[2]
    shard_rows = model_width // fsdp_count
    own_input = layer_input[0]
    inputs = [lax.dynamic_slice_in_dim(own_input, fsdp_at * shard_rows, shard_rows, axis=1)]
    for steps in range(1, fsdp_count):
        target = (fsdp_at + steps) % fsdp_count
        outgoing = lax.dynamic_slice_in_dim(own_input, target * shard_rows, shard_rows, axis=1)
        inputs.append(rotated(outgoing, "fsdp", steps))

    own_kv = jnp.concatenate([key_heads[0], value_heads[0]], axis=1)
    query_pos = first_row + jnp.arange(block_rows, dtype=jnp.int32)
    lowest = jnp.maximum(doc_start_of(doc_starts[0], query_pos), query_pos - window + 1)
    lo_rel = (lowest - first_row + margin).astype(jnp.int32)[:, None]
    sub_count = lax.axis_size("sub")
    sub_at = lax.axis_index("sub")
    flag = jnp.reshape(sub_at, (1,)).astype(jnp.int32)
    chip_route = sub_count == 2 and reach == 3
    if chip_route:
        ring_count = lax.axis_size(RING)
        across = [(2 * chip - 3, 2 * chip) for chip in range(2, ring_count // 2)]
        two_back = passed_along(own_kv, "ctx", 1)
        one_back_high = passed_along(own_kv, "sub", 1)
        three_back_low = lax.ppermute(own_kv, RING, across)
        swapped = rotated(two_back, "sub", 1)
        kv_blocks = [two_back, one_back_high, three_back_low, swapped, own_kv]
        slots = [(2, 3), (0, 0), (3, 1), (4, 4)]
    else:
        arrived = []
        moving = own_kv
        for _ in range(reach):
            moving = passed_along(moving, RING, 1)
            arrived.append(moving)
        kv_blocks = arrived[::-1] + [own_kv]
        slots = [(index, index) for index in range(reach + 1)]
    grad_q, *grad_pieces = attention(
        flag, lo_rel, query_heads[0], grad_out[0], kv_blocks, slots, heads, kv_heads, margin,
        inputs[1:],
        chip_route,
    )

    def low(value):
        return value.astype(jnp.bfloat16)

    if chip_route:
        back = [(target, source) for source, target in across]
        to_mate, to_other, g2, g0 = grad_pieces
        from_far = lax.ppermute(to_other, RING, back).astype(jnp.float32)
        from_mate = rotated(to_mate, "sub", 1).astype(jnp.float32)
        from_high = passed_along(to_other, "sub", -1).astype(jnp.float32)
        two_back_sum = g2 + from_mate
        from_next = passed_along(low(two_back_sum), "ctx", -1).astype(jnp.float32)
        total = g0 + from_high + from_far + from_next
    else:

        def own_piece(distance):
            return grad_pieces[reach - distance]

        total = own_piece(reach)
        for distance in range(reach - 1, -1, -1):
            moved = passed_along(low(total), RING, -1).astype(jnp.float32)
            total = moved + own_piece(distance)
    grad_kv = total.astype(jnp.bfloat16)
    grad_key = grad_kv[:, :kv_width]
    grad_value = grad_kv[:, kv_width:]

    values = [grad_value]
    for steps in range(1, fsdp_count):
        values.append(rotated(grad_value, "fsdp", steps))
    stacked_inputs = jnp.concatenate(inputs, axis=0)
    stacked_values = jnp.concatenate(values, axis=0)
    shard = lax.dot_general(stacked_inputs, stacked_values, TN, preferred_element_type=jnp.float32)
    token_scale = float(fsdp_count * lax.axis_size(RING) * block_rows) ** (-0.5)
    scale_early = token_scale == 2.0 ** round(math.log2(token_scale))
    if scale_early:
        shard = shard * token_scale

    sub_count = lax.axis_size("sub")
    sub_at = lax.axis_index("sub")
    piece_rows = shard_rows // sub_count
    mine = lax.dynamic_slice_in_dim(shard, sub_at * piece_rows, piece_rows, axis=0)
    for steps in range(1, sub_count):
        target = (sub_at + steps) % sub_count
        outgoing = lax.dynamic_slice_in_dim(shard, target * piece_rows, piece_rows, axis=0)
        mine = mine + rotated(outgoing.astype(jnp.bfloat16), "sub", steps).astype(jnp.float32)
    reduced = ring_sum(mine, "ctx")
    if sub_count == 2:
        other = rotated(reduced.astype(jnp.bfloat16), "sub", 1).astype(jnp.float32)
        first = jnp.where(sub_at == 0, reduced, other)
        second = jnp.where(sub_at == 0, other, reduced)
        weight_v = jnp.concatenate([first, second], axis=0)
    else:
        weight_v = lax.all_gather(reduced, "sub", axis=0, tiled=True)
    if not scale_early:
        weight_v = weight_v * token_scale
    return (
        grad_q[None],
        grad_key[None],
        grad_value[None],
        weight_v,
    )


def solution(mesh):
    placed = (
        P(("groups", "fsdp"), ("ctx", "sub"), None),
        P(("groups", "fsdp"), ("ctx", "sub"), None),
        P(("groups", "fsdp"), ("ctx", "sub"), None),
        P(("groups", "fsdp"), ("ctx", "sub"), None),
        P(("groups", "fsdp"), ("ctx", "sub"), None),
        P(("groups", "fsdp"), None),
    )
    return jax.shard_map(
        body,
        mesh=mesh,
        in_specs=placed,
        out_specs=(
            P(("groups", "fsdp"), ("ctx", "sub"), None),
            P(("groups", "fsdp"), ("ctx", "sub"), None),
            P(("groups", "fsdp"), ("ctx", "sub"), None),
            P(("groups", "fsdp"), None),
        ),
        check_vma=False,
    )
```

```python
import functools
import math

import jax
import jax.numpy as jnp
from jax import lax
from jax.experimental import pallas as pl
from jax.experimental.pallas import tpu as pltpu
from jax.sharding import PartitionSpec as P

HEAD_DIM = 256
SPAN = 768
RING = ("ctx", "sub")
NT = (((1,), (1,)), ((), ()))
TN = (((0,), (0,)), ((), ()))


def passed_along(value, axis, steps):
    count = lax.axis_size(axis)
    first, last = (max(0, -steps), min(count, count - steps))
    return lax.ppermute(value, axis, [(source, source + steps) for source in range(first, last)])


def rotated(value, axis, steps):
    count = lax.axis_size(axis)
    return lax.ppermute(value, axis, [(source, (source + steps) % count) for source in range(count)])


def ring_sum(piece, axis):
    count = lax.axis_size(axis)
    at = lax.axis_index(axis)
    rows = piece.shape[0] // count
    total = lax.dynamic_slice_in_dim(piece, at * rows, rows, axis=0)
    for steps in range(1, count):
        outgoing = lax.dynamic_slice_in_dim(piece, ((at + steps) % count) * rows, rows, axis=0)
        total = total + rotated(outgoing.astype(jnp.bfloat16), axis, steps).astype(jnp.float32)
    low = total.astype(jnp.bfloat16)
    gathered = jnp.zeros(piece.shape, jnp.bfloat16)
    gathered = lax.dynamic_update_slice_in_dim(gathered, low, at * rows, axis=0)
    for steps in range(1, count):
        arrived = rotated(low, axis, steps)
        gathered = lax.dynamic_update_slice_in_dim(
            gathered, arrived, ((at - steps) % count) * rows, axis=0
        )
    return gathered


def doc_start_of(starts, positions):
    covered = starts[None, :] <= positions[:, None]
    return jnp.max(jnp.where(covered, starts[None, :], 0), axis=1)


def attention_kernel(*refs, heads, kv_heads, margin, slots, blocks, chip_outputs):
    flag_ref, lo_ref, q_ref, do_ref = refs[:4]
    block_refs = refs[4 : 4 + blocks]
    kv_ref, dkv_ref = refs[-2:]
    outs = refs[-3 - len(slots) : -2]
    dq_ref = outs[0]
    out_refs = outs[1:]
    block_rows = block_refs[0].shape[0]
    flag = flag_ref[0]
    for index, (when_low, when_high) in enumerate(slots):
        target = kv_ref.at[pl.ds(index * block_rows, block_rows), :]
        if when_low == when_high:
            target[...] = block_refs[when_low][...]
        else:

            @pl.when(flag == 0)
            def _():
                target[...] = block_refs[when_low][...]

            @pl.when(flag != 0)
            def _():
                target[...] = block_refs[when_high][...]

    rows = q_ref.shape[0]
    keys = kv_ref.shape[0]
    scale = HEAD_DIM ** (-0.5)
    kv_width = kv_heads * HEAD_DIM
    per_group = heads // kv_heads
    col = lax.broadcasted_iota(jnp.int32, (rows, keys), 1)
    row = lax.broadcasted_iota(jnp.int32, (rows, keys), 0)
    allowed = (col >= lo_ref[...]) & (col <= row + margin)
    for group in range(kv_heads):
        k_cols = pl.ds(group * HEAD_DIM, HEAD_DIM)
        v_cols = pl.ds(kv_width + group * HEAD_DIM, HEAD_DIM)
        key_g = kv_ref[:, k_cols]
        value_g = kv_ref[:, v_cols]
        grad_k = None
        grad_v = None
        for member in range(per_group):
            q_cols = pl.ds((group * per_group + member) * HEAD_DIM, HEAD_DIM)
            query_h = q_ref[:, q_cols]
            grad_h = do_ref[:, q_cols]
            scores = lax.dot_general(query_h, key_g, NT, preferred_element_type=jnp.float32) * scale
            scores = jnp.where(allowed, scores, -1e30)
            largest = jnp.max(scores, axis=1, keepdims=True)
            raised = jnp.exp(scores - largest)
            probs = raised * (1.0 / jnp.sum(raised, axis=1, keepdims=True))
            grad_probs = lax.dot_general(grad_h, value_g, NT, preferred_element_type=jnp.float32)
            row_dot = jnp.sum(probs * grad_probs, axis=1, keepdims=True)
            grad_scores = (probs * (grad_probs - row_dot) * scale).astype(jnp.bfloat16)
            probs_low = probs.astype(jnp.bfloat16)
            dq_ref[:, q_cols] = jnp.dot(
                grad_scores, key_g, preferred_element_type=jnp.float32
            ).astype(dq_ref.dtype)
            term_k = lax.dot_general(grad_scores, query_h, TN, preferred_element_type=jnp.float32)
            term_v = lax.dot_general(probs_low, grad_h, TN, preferred_element_type=jnp.float32)
            grad_k = term_k if grad_k is None else grad_k + term_k
            grad_v = term_v if grad_v is None else grad_v + term_v
        dkv_ref[:, k_cols] = grad_k
        dkv_ref[:, v_cols] = grad_v
    def slot_rows(index):
        return dkv_ref[pl.ds(index * block_rows, block_rows), :]

    if chip_outputs:
        mate_ref, other_ref, two_ref, own_ref = out_refs
        two_ref[...] = slot_rows(1)
        own_ref[...] = slot_rows(3)

        @pl.when(flag == 0)
        def _():
            mate_ref[...] = slot_rows(2).astype(mate_ref.dtype)
            other_ref[...] = slot_rows(0).astype(other_ref.dtype)

        @pl.when(flag != 0)
        def _():
            mate_ref[...] = slot_rows(0).astype(mate_ref.dtype)
            other_ref[...] = slot_rows(2).astype(other_ref.dtype)

    else:
        for index, out_ref in enumerate(out_refs):
            out_ref[...] = slot_rows(index)


def attention(
    flag, lo_rel, queries, grads, kv_blocks, slots, heads, kv_heads, margin, early, chip_outputs
):
    rows, width = queries.shape
    blocks = len(kv_blocks)
    block_rows, kv_cols = kv_blocks[0].shape
    keys = len(slots) * block_rows
    kernel = functools.partial(
        attention_kernel,
        heads=heads,
        kv_heads=kv_heads,
        margin=margin,
        slots=tuple(slots),
        blocks=blocks,
        chip_outputs=chip_outputs,
    )
    if chip_outputs:
        piece_types = [jnp.bfloat16, jnp.bfloat16, jnp.float32, jnp.float32]
    else:
        piece_types = [jnp.float32] * len(slots)
    vmem = pl.BlockSpec(memory_space=pltpu.VMEM)
    smem = pl.BlockSpec(memory_space=pltpu.SMEM)
    flops = 2 * 5 * heads * rows * keys * HEAD_DIM
    moved = 2 * (2 * rows * width + keys * kv_cols + rows * width) + 4 * keys * kv_cols
    return pl.pallas_call(
        kernel,
        out_shape=(jax.ShapeDtypeStruct((rows, width), jnp.bfloat16),)
        + tuple(jax.ShapeDtypeStruct((block_rows, kv_cols), kind) for kind in piece_types),
        in_specs=[smem] + [vmem] * (3 + blocks) + [pl.BlockSpec(memory_space=pl.ANY)] * len(early),
        out_specs=(vmem,) * (1 + len(slots)),
        scratch_shapes=[
            pltpu.VMEM((keys, kv_cols), kv_blocks[0].dtype),
            pltpu.VMEM((keys, kv_cols), jnp.float32),
        ],
        cost_estimate=pl.CostEstimate(
            flops=flops, transcendentals=heads * rows * keys, bytes_accessed=moved
        ),
    )(flag, lo_rel, queries, grads, *kv_blocks, *early)


def body(layer_input, query_heads, key_heads, value_heads, grad_out, doc_starts):
    block_rows = query_heads.shape[1]
    window = min(SPAN, lax.axis_size(RING) * block_rows // 2)
    reach = (window + block_rows - 2) // block_rows
    margin = reach * block_rows
    kv_width = key_heads.shape[2]
    heads = query_heads.shape[2] // HEAD_DIM
    kv_heads = kv_width // HEAD_DIM
    first_row = lax.axis_index(RING) * block_rows

    fsdp_count = lax.axis_size("fsdp")
    fsdp_at = lax.axis_index("fsdp")
    model_width = layer_input.shape[2]
    shard_rows = model_width // fsdp_count
    own_input = layer_input[0]
    inputs = [lax.dynamic_slice_in_dim(own_input, fsdp_at * shard_rows, shard_rows, axis=1)]
    for steps in range(1, fsdp_count):
        target = (fsdp_at + steps) % fsdp_count
        outgoing = lax.dynamic_slice_in_dim(own_input, target * shard_rows, shard_rows, axis=1)
        inputs.append(rotated(outgoing, "fsdp", steps))

    own_kv = jnp.concatenate([key_heads[0], value_heads[0]], axis=1)
    query_pos = first_row + jnp.arange(block_rows, dtype=jnp.int32)
    lowest = jnp.maximum(doc_start_of(doc_starts[0], query_pos), query_pos - window + 1)
    lo_rel = (lowest - first_row + margin).astype(jnp.int32)[:, None]
    sub_count = lax.axis_size("sub")
    sub_at = lax.axis_index("sub")
    flag = jnp.reshape(sub_at, (1,)).astype(jnp.int32)
    chip_route = sub_count == 2 and reach == 3
    if chip_route:
        ring_count = lax.axis_size(RING)
        across = [(2 * chip - 3, 2 * chip) for chip in range(2, ring_count // 2)]
        two_back = passed_along(own_kv, "ctx", 1)
        one_back_high = passed_along(own_kv, "sub", 1)
        three_back_low = lax.ppermute(own_kv, RING, across)
        swapped = rotated(two_back, "sub", 1)
        kv_blocks = [two_back, one_back_high, three_back_low, swapped, own_kv]
        slots = [(2, 3), (0, 0), (3, 1), (4, 4)]
    else:
        arrived = []
        moving = own_kv
        for _ in range(reach):
            moving = passed_along(moving, RING, 1)
            arrived.append(moving)
        kv_blocks = arrived[::-1] + [own_kv]
        slots = [(index, index) for index in range(reach + 1)]
    grad_q, *grad_pieces = attention(
        flag, lo_rel, query_heads[0], grad_out[0], kv_blocks, slots, heads, kv_heads, margin,
        inputs[1:],
        chip_route,
    )

    def low(value):
        return value.astype(jnp.bfloat16)

    if chip_route:
        back = [(target, source) for source, target in across]
        to_mate, to_other, g2, g0 = grad_pieces
        from_far = lax.ppermute(to_other, RING, back).astype(jnp.float32)
        from_mate = rotated(to_mate, "sub", 1).astype(jnp.float32)
        from_high = passed_along(to_other, "sub", -1).astype(jnp.float32)
        two_back_sum = g2 + from_mate
        from_next = passed_along(low(two_back_sum), "ctx", -1).astype(jnp.float32)
        total = g0 + from_high + from_far + from_next
    else:

        def own_piece(distance):
            return grad_pieces[reach - distance]

        total = own_piece(reach)
        for distance in range(reach - 1, -1, -1):
            moved = passed_along(low(total), RING, -1).astype(jnp.float32)
            total = moved + own_piece(distance)
    grad_kv = total.astype(jnp.bfloat16)
    grad_key = grad_kv[:, :kv_width]
    grad_value = grad_kv[:, kv_width:]

    values = [grad_value]
    for steps in range(1, fsdp_count):
        values.append(rotated(grad_value, "fsdp", steps))
    stacked_inputs = jnp.concatenate(inputs, axis=0)
    stacked_values = jnp.concatenate(values, axis=0)
    shard = lax.dot_general(stacked_inputs, stacked_values, TN, preferred_element_type=jnp.float32)
    token_scale = float(fsdp_count * lax.axis_size(RING) * block_rows) ** (-0.5)
    scale_early = token_scale == 2.0 ** round(math.log2(token_scale))
    if scale_early:
        shard = shard * token_scale

    sub_count = lax.axis_size("sub")
    sub_at = lax.axis_index("sub")
    piece_rows = shard_rows // sub_count
    mine = lax.dynamic_slice_in_dim(shard, sub_at * piece_rows, piece_rows, axis=0)
    for steps in range(1, sub_count):
        target = (sub_at + steps) % sub_count
        outgoing = lax.dynamic_slice_in_dim(shard, target * piece_rows, piece_rows, axis=0)
        mine = mine + rotated(outgoing.astype(jnp.bfloat16), "sub", steps).astype(jnp.float32)
    reduced = ring_sum(mine, "ctx")
    if sub_count == 2:
        other = rotated(reduced, "sub", 1)
        first = jnp.where(sub_at == 0, reduced, other)
        second = jnp.where(sub_at == 0, other, reduced)
        weight_v = jnp.concatenate([first, second], axis=0).astype(jnp.float32)
    else:
        weight_v = lax.all_gather(reduced, "sub", axis=0, tiled=True).astype(jnp.float32)
    if not scale_early:
        weight_v = weight_v * token_scale
    return (
        grad_q[None],
        grad_key[None],
        grad_value[None],
        weight_v,
    )


def solution(mesh):
    placed = (
        P(("groups", "fsdp"), ("ctx", "sub"), None),
        P(("groups", "fsdp"), ("ctx", "sub"), None),
        P(("groups", "fsdp"), ("ctx", "sub"), None),
        P(("groups", "fsdp"), ("ctx", "sub"), None),
        P(("groups", "fsdp"), ("ctx", "sub"), None),
        P(("groups", "fsdp"), None),
    )
    return jax.shard_map(
        body,
        mesh=mesh,
        in_specs=placed,
        out_specs=(
            P(("groups", "fsdp"), ("ctx", "sub"), None),
            P(("groups", "fsdp"), ("ctx", "sub"), None),
            P(("groups", "fsdp"), ("ctx", "sub"), None),
            P(("groups", "fsdp"), None),
        ),
        check_vma=False,
    )
```

```python
import functools
import math

import jax
import jax.numpy as jnp
from jax import lax
from jax.experimental import pallas as pl
from jax.experimental.pallas import tpu as pltpu
from jax.sharding import PartitionSpec as P

HEAD_DIM = 256
SPAN = 768
RING = ("ctx", "sub")
NT = (((1,), (1,)), ((), ()))
TN = (((0,), (0,)), ((), ()))


def passed_along(value, axis, steps):
    count = lax.axis_size(axis)
    first, last = (max(0, -steps), min(count, count - steps))
    return lax.ppermute(value, axis, [(source, source + steps) for source in range(first, last)])


def rotated(value, axis, steps):
    count = lax.axis_size(axis)
    return lax.ppermute(value, axis, [(source, (source + steps) % count) for source in range(count)])


def ring_sum(piece, axis):
    count = lax.axis_size(axis)
    at = lax.axis_index(axis)
    rows = piece.shape[0] // count
    total = lax.dynamic_slice_in_dim(piece, at * rows, rows, axis=0)
    for steps in range(1, count):
        outgoing = lax.dynamic_slice_in_dim(piece, ((at + steps) % count) * rows, rows, axis=0)
        total = total + rotated(outgoing.astype(jnp.bfloat16), axis, steps).astype(jnp.float32)
    low = total.astype(jnp.bfloat16)
    gathered = jnp.zeros(piece.shape, jnp.bfloat16)
    gathered = lax.dynamic_update_slice_in_dim(gathered, low, at * rows, axis=0)
    for steps in range(1, count):
        arrived = rotated(low, axis, steps)
        gathered = lax.dynamic_update_slice_in_dim(
            gathered, arrived, ((at - steps) % count) * rows, axis=0
        )
    return gathered


def doc_start_of(starts, positions):
    covered = starts[None, :] <= positions[:, None]
    return jnp.max(jnp.where(covered, starts[None, :], 0), axis=1)


def attention_kernel(*refs, heads, kv_heads, margin, slots, blocks, chip_outputs):
    flag_ref, lo_ref, q_ref, do_ref = refs[:4]
    block_refs = refs[4 : 4 + blocks]
    kv_ref, dkv_ref = refs[-2:]
    outs = refs[-3 - len(slots) : -2]
    dq_ref = outs[0]
    out_refs = outs[1:]
    block_rows = block_refs[0].shape[0]
    flag = flag_ref[0]
    for index, (when_low, when_high) in enumerate(slots):
        target = kv_ref.at[pl.ds(index * block_rows, block_rows), :]
        if when_low == when_high:
            target[...] = block_refs[when_low][...]
        else:

            @pl.when(flag == 0)
            def _():
                target[...] = block_refs[when_low][...]

            @pl.when(flag != 0)
            def _():
                target[...] = block_refs[when_high][...]

    rows = q_ref.shape[0]
    keys = kv_ref.shape[0]
    scale = HEAD_DIM ** (-0.5)
    kv_width = kv_heads * HEAD_DIM
    per_group = heads // kv_heads
    col = lax.broadcasted_iota(jnp.int32, (rows, keys), 1)
    row = lax.broadcasted_iota(jnp.int32, (rows, keys), 0)
    allowed = (col >= lo_ref[...]) & (col <= row + margin)
    for group in range(kv_heads):
        k_cols = pl.ds(group * HEAD_DIM, HEAD_DIM)
        v_cols = pl.ds(kv_width + group * HEAD_DIM, HEAD_DIM)
        key_g = kv_ref[:, k_cols]
        value_g = kv_ref[:, v_cols]
        grad_k = None
        grad_v = None
        for member in range(per_group):
            q_cols = pl.ds((group * per_group + member) * HEAD_DIM, HEAD_DIM)
            query_h = q_ref[:, q_cols]
            grad_h = do_ref[:, q_cols]
            query_scaled = query_h * jnp.asarray(scale, query_h.dtype)
            scores = lax.dot_general(query_scaled, key_g, NT, preferred_element_type=jnp.float32)
            scores = jnp.where(allowed, scores, -1e30)
            largest = jnp.max(scores, axis=1, keepdims=True)
            raised = jnp.exp(scores - largest)
            probs = raised * (1.0 / jnp.sum(raised, axis=1, keepdims=True))
            grad_probs = lax.dot_general(grad_h, value_g, NT, preferred_element_type=jnp.float32)
            row_dot = jnp.sum(probs * grad_probs, axis=1, keepdims=True)
            grad_scores = (probs * (grad_probs - row_dot) * scale).astype(jnp.bfloat16)
            probs_low = probs.astype(jnp.bfloat16)
            dq_ref[:, q_cols] = jnp.dot(
                grad_scores, key_g, preferred_element_type=jnp.float32
            ).astype(dq_ref.dtype)
            term_k = lax.dot_general(grad_scores, query_h, TN, preferred_element_type=jnp.float32)
            term_v = lax.dot_general(probs_low, grad_h, TN, preferred_element_type=jnp.float32)
            grad_k = term_k if grad_k is None else grad_k + term_k
            grad_v = term_v if grad_v is None else grad_v + term_v
        dkv_ref[:, k_cols] = grad_k
        dkv_ref[:, v_cols] = grad_v
    def slot_rows(index):
        return dkv_ref[pl.ds(index * block_rows, block_rows), :]

    if chip_outputs:
        mate_ref, other_ref, two_ref, own_ref = out_refs
        two_ref[...] = slot_rows(1)
        own_ref[...] = slot_rows(3)

        @pl.when(flag == 0)
        def _():
            mate_ref[...] = slot_rows(2).astype(mate_ref.dtype)
            other_ref[...] = slot_rows(0).astype(other_ref.dtype)

        @pl.when(flag != 0)
        def _():
            mate_ref[...] = slot_rows(0).astype(mate_ref.dtype)
            other_ref[...] = slot_rows(2).astype(other_ref.dtype)

    else:
        for index, out_ref in enumerate(out_refs):
            out_ref[...] = slot_rows(index)


def attention(
    flag, lo_rel, queries, grads, kv_blocks, slots, heads, kv_heads, margin, early, chip_outputs
):
    rows, width = queries.shape
    blocks = len(kv_blocks)
    block_rows, kv_cols = kv_blocks[0].shape
    keys = len(slots) * block_rows
    kernel = functools.partial(
        attention_kernel,
        heads=heads,
        kv_heads=kv_heads,
        margin=margin,
        slots=tuple(slots),
        blocks=blocks,
        chip_outputs=chip_outputs,
    )
    if chip_outputs:
        piece_types = [jnp.bfloat16, jnp.bfloat16, jnp.float32, jnp.float32]
    else:
        piece_types = [jnp.float32] * len(slots)
    vmem = pl.BlockSpec(memory_space=pltpu.VMEM)
    smem = pl.BlockSpec(memory_space=pltpu.SMEM)
    flops = 2 * 5 * heads * rows * keys * HEAD_DIM
    moved = 2 * (2 * rows * width + keys * kv_cols + rows * width) + 4 * keys * kv_cols
    return pl.pallas_call(
        kernel,
        out_shape=(jax.ShapeDtypeStruct((rows, width), jnp.bfloat16),)
        + tuple(jax.ShapeDtypeStruct((block_rows, kv_cols), kind) for kind in piece_types),
        in_specs=[smem] + [vmem] * (3 + blocks) + [pl.BlockSpec(memory_space=pl.ANY)] * len(early),
        out_specs=(vmem,) * (1 + len(slots)),
        scratch_shapes=[
            pltpu.VMEM((keys, kv_cols), kv_blocks[0].dtype),
            pltpu.VMEM((keys, kv_cols), jnp.float32),
        ],
        cost_estimate=pl.CostEstimate(
            flops=flops, transcendentals=heads * rows * keys, bytes_accessed=moved
        ),
    )(flag, lo_rel, queries, grads, *kv_blocks, *early)


def body(layer_input, query_heads, key_heads, value_heads, grad_out, doc_starts):
    block_rows = query_heads.shape[1]
    window = min(SPAN, lax.axis_size(RING) * block_rows // 2)
    reach = (window + block_rows - 2) // block_rows
    margin = reach * block_rows
    kv_width = key_heads.shape[2]
    heads = query_heads.shape[2] // HEAD_DIM
    kv_heads = kv_width // HEAD_DIM
    first_row = lax.axis_index(RING) * block_rows

    fsdp_count = lax.axis_size("fsdp")
    fsdp_at = lax.axis_index("fsdp")
    model_width = layer_input.shape[2]
    shard_rows = model_width // fsdp_count
    own_input = layer_input[0]
    inputs = [lax.dynamic_slice_in_dim(own_input, fsdp_at * shard_rows, shard_rows, axis=1)]
    for steps in range(1, fsdp_count):
        target = (fsdp_at + steps) % fsdp_count
        outgoing = lax.dynamic_slice_in_dim(own_input, target * shard_rows, shard_rows, axis=1)
        inputs.append(rotated(outgoing, "fsdp", steps))

    own_kv = jnp.concatenate([key_heads[0], value_heads[0]], axis=1)
    query_pos = first_row + jnp.arange(block_rows, dtype=jnp.int32)
    lowest = jnp.maximum(doc_start_of(doc_starts[0], query_pos), query_pos - window + 1)
    lo_rel = (lowest - first_row + margin).astype(jnp.int32)[:, None]
    sub_count = lax.axis_size("sub")
    sub_at = lax.axis_index("sub")
    flag = jnp.reshape(sub_at, (1,)).astype(jnp.int32)
    chip_route = sub_count == 2 and reach == 3
    if chip_route:
        ring_count = lax.axis_size(RING)
        across = [(2 * chip - 3, 2 * chip) for chip in range(2, ring_count // 2)]
        two_back = passed_along(own_kv, "ctx", 1)
        one_back_high = passed_along(own_kv, "sub", 1)
        three_back_low = lax.ppermute(own_kv, RING, across)
        swapped = rotated(two_back, "sub", 1)
        kv_blocks = [two_back, one_back_high, three_back_low, swapped, own_kv]
        slots = [(2, 3), (0, 0), (3, 1), (4, 4)]
    else:
        arrived = []
        moving = own_kv
        for _ in range(reach):
            moving = passed_along(moving, RING, 1)
            arrived.append(moving)
        kv_blocks = arrived[::-1] + [own_kv]
        slots = [(index, index) for index in range(reach + 1)]
    grad_q, *grad_pieces = attention(
        flag, lo_rel, query_heads[0], grad_out[0], kv_blocks, slots, heads, kv_heads, margin,
        inputs[1:],
        chip_route,
    )

    def low(value):
        return value.astype(jnp.bfloat16)

    if chip_route:
        back = [(target, source) for source, target in across]
        to_mate, to_other, g2, g0 = grad_pieces
        from_far = lax.ppermute(to_other, RING, back).astype(jnp.float32)
        from_mate = rotated(to_mate, "sub", 1).astype(jnp.float32)
        from_high = passed_along(to_other, "sub", -1).astype(jnp.float32)
        two_back_sum = g2 + from_mate
        from_next = passed_along(low(two_back_sum), "ctx", -1).astype(jnp.float32)
        total = g0 + from_high + from_far + from_next
    else:

        def own_piece(distance):
            return grad_pieces[reach - distance]

        total = own_piece(reach)
        for distance in range(reach - 1, -1, -1):
            moved = passed_along(low(total), RING, -1).astype(jnp.float32)
            total = moved + own_piece(distance)
    grad_kv = total.astype(jnp.bfloat16)
    grad_key = grad_kv[:, :kv_width]
    grad_value = grad_kv[:, kv_width:]

    values = [grad_value]
    for steps in range(1, fsdp_count):
        values.append(rotated(grad_value, "fsdp", steps))
    stacked_inputs = jnp.concatenate(inputs, axis=0)
    stacked_values = jnp.concatenate(values, axis=0)
    shard = lax.dot_general(stacked_inputs, stacked_values, TN, preferred_element_type=jnp.float32)
    token_scale = float(fsdp_count * lax.axis_size(RING) * block_rows) ** (-0.5)
    scale_early = token_scale == 2.0 ** round(math.log2(token_scale))
    if scale_early:
        shard = shard * token_scale

    sub_count = lax.axis_size("sub")
    sub_at = lax.axis_index("sub")
    piece_rows = shard_rows // sub_count
    mine = lax.dynamic_slice_in_dim(shard, sub_at * piece_rows, piece_rows, axis=0)
    for steps in range(1, sub_count):
        target = (sub_at + steps) % sub_count
        outgoing = lax.dynamic_slice_in_dim(shard, target * piece_rows, piece_rows, axis=0)
        mine = mine + rotated(outgoing.astype(jnp.bfloat16), "sub", steps).astype(jnp.float32)
    reduced = ring_sum(mine, "ctx")
    if sub_count == 2:
        other = rotated(reduced, "sub", 1)
        first = jnp.where(sub_at == 0, reduced, other)
        second = jnp.where(sub_at == 0, other, reduced)
        weight_v = jnp.concatenate([first, second], axis=0).astype(jnp.float32)
    else:
        weight_v = lax.all_gather(reduced, "sub", axis=0, tiled=True).astype(jnp.float32)
    if not scale_early:
        weight_v = weight_v * token_scale
    return (
        grad_q[None],
        grad_key[None],
        grad_value[None],
        weight_v,
    )


def solution(mesh):
    placed = (
        P(("groups", "fsdp"), ("ctx", "sub"), None),
        P(("groups", "fsdp"), ("ctx", "sub"), None),
        P(("groups", "fsdp"), ("ctx", "sub"), None),
        P(("groups", "fsdp"), ("ctx", "sub"), None),
        P(("groups", "fsdp"), ("ctx", "sub"), None),
        P(("groups", "fsdp"), None),
    )
    return jax.shard_map(
        body,
        mesh=mesh,
        in_specs=placed,
        out_specs=(
            P(("groups", "fsdp"), ("ctx", "sub"), None),
            P(("groups", "fsdp"), ("ctx", "sub"), None),
            P(("groups", "fsdp"), ("ctx", "sub"), None),
            P(("groups", "fsdp"), None),
        ),
        check_vma=False,
    )
```

```python
import functools
import math

import jax
import jax.numpy as jnp
from jax import lax
from jax.experimental import pallas as pl
from jax.experimental.pallas import tpu as pltpu
from jax.sharding import PartitionSpec as P

HEAD_DIM = 256
SPAN = 768
RING = ("ctx", "sub")
NT = (((1,), (1,)), ((), ()))
TN = (((0,), (0,)), ((), ()))


def passed_along(value, axis, steps):
    count = lax.axis_size(axis)
    first, last = (max(0, -steps), min(count, count - steps))
    return lax.ppermute(value, axis, [(source, source + steps) for source in range(first, last)])


def rotated(value, axis, steps):
    count = lax.axis_size(axis)
    return lax.ppermute(value, axis, [(source, (source + steps) % count) for source in range(count)])


def ring_sum(piece, axis):
    count = lax.axis_size(axis)
    at = lax.axis_index(axis)
    rows = piece.shape[0] // count
    total = lax.dynamic_slice_in_dim(piece, at * rows, rows, axis=0)
    for steps in range(1, count):
        outgoing = lax.dynamic_slice_in_dim(piece, ((at + steps) % count) * rows, rows, axis=0)
        total = total + rotated(outgoing.astype(jnp.bfloat16), axis, steps).astype(jnp.float32)
    low = total.astype(jnp.bfloat16)
    gathered = jnp.zeros(piece.shape, jnp.bfloat16)
    gathered = lax.dynamic_update_slice_in_dim(gathered, low, at * rows, axis=0)
    for steps in range(1, count):
        arrived = rotated(low, axis, steps)
        gathered = lax.dynamic_update_slice_in_dim(
            gathered, arrived, ((at - steps) % count) * rows, axis=0
        )
    return gathered


def doc_start_of(starts, positions):
    covered = starts[None, :] <= positions[:, None]
    return jnp.max(jnp.where(covered, starts[None, :], 0), axis=1)


def attention_kernel(*refs, heads, kv_heads, margin, slots, blocks, chip_outputs):
    flag_ref, lo_ref, q_ref, do_ref = refs[:4]
    block_refs = refs[4 : 4 + blocks]
    kv_ref, dkv_ref = refs[-2:]
    outs = refs[-3 - len(slots) : -2]
    dq_ref = outs[0]
    out_refs = outs[1:]
    block_rows = block_refs[0].shape[0]
    flag = flag_ref[0]
    for index, (when_low, when_high) in enumerate(slots):
        target = kv_ref.at[pl.ds(index * block_rows, block_rows), :]
        if when_low == when_high:
            target[...] = block_refs[when_low][...]
        else:

            @pl.when(flag == 0)
            def _():
                target[...] = block_refs[when_low][...]

            @pl.when(flag != 0)
            def _():
                target[...] = block_refs[when_high][...]

    rows = q_ref.shape[0]
    keys = kv_ref.shape[0]
    scale = HEAD_DIM ** (-0.5)
    kv_width = kv_heads * HEAD_DIM
    per_group = heads // kv_heads
    col = lax.broadcasted_iota(jnp.int32, (rows, keys), 1)
    row = lax.broadcasted_iota(jnp.int32, (rows, keys), 0)
    allowed = (col >= lo_ref[...]) & (col <= row + margin)
    for group in range(kv_heads):
        k_cols = pl.ds(group * HEAD_DIM, HEAD_DIM)
        v_cols = pl.ds(kv_width + group * HEAD_DIM, HEAD_DIM)
        key_g = kv_ref[:, k_cols]
        value_g = kv_ref[:, v_cols]
        grad_k = None
        grad_v = None
        for member in range(per_group):
            q_cols = pl.ds((group * per_group + member) * HEAD_DIM, HEAD_DIM)
            query_h = q_ref[:, q_cols]
            grad_h = do_ref[:, q_cols]
            query_scaled = query_h * jnp.asarray(scale, query_h.dtype)
            scores = lax.dot_general(query_scaled, key_g, NT, preferred_element_type=jnp.float32)
            scores = jnp.where(allowed, scores, -1e30)
            largest = jnp.max(scores, axis=1, keepdims=True)
            raised = jnp.exp(scores - largest)
            probs = raised * (1.0 / jnp.sum(raised, axis=1, keepdims=True))
            grad_scaled = grad_h * jnp.asarray(scale, grad_h.dtype)
            grad_probs = lax.dot_general(grad_scaled, value_g, NT, preferred_element_type=jnp.float32)
            row_dot = jnp.sum(probs * grad_probs, axis=1, keepdims=True)
            grad_scores = (probs * (grad_probs - row_dot)).astype(jnp.bfloat16)
            probs_low = probs.astype(jnp.bfloat16)
            dq_ref[:, q_cols] = jnp.dot(
                grad_scores, key_g, preferred_element_type=jnp.float32
            ).astype(dq_ref.dtype)
            term_k = lax.dot_general(grad_scores, query_h, TN, preferred_element_type=jnp.float32)
            term_v = lax.dot_general(probs_low, grad_h, TN, preferred_element_type=jnp.float32)
            grad_k = term_k if grad_k is None else grad_k + term_k
            grad_v = term_v if grad_v is None else grad_v + term_v
        dkv_ref[:, k_cols] = grad_k
        dkv_ref[:, v_cols] = grad_v
    def slot_rows(index):
        return dkv_ref[pl.ds(index * block_rows, block_rows), :]

    if chip_outputs:
        mate_ref, other_ref, two_ref, own_ref = out_refs
        two_ref[...] = slot_rows(1)
        own_ref[...] = slot_rows(3)

        @pl.when(flag == 0)
        def _():
            mate_ref[...] = slot_rows(2).astype(mate_ref.dtype)
            other_ref[...] = slot_rows(0).astype(other_ref.dtype)

        @pl.when(flag != 0)
        def _():
            mate_ref[...] = slot_rows(0).astype(mate_ref.dtype)
            other_ref[...] = slot_rows(2).astype(other_ref.dtype)

    else:
        for index, out_ref in enumerate(out_refs):
            out_ref[...] = slot_rows(index)


def attention(
    flag, lo_rel, queries, grads, kv_blocks, slots, heads, kv_heads, margin, early, chip_outputs
):
    rows, width = queries.shape
    blocks = len(kv_blocks)
    block_rows, kv_cols = kv_blocks[0].shape
    keys = len(slots) * block_rows
    kernel = functools.partial(
        attention_kernel,
        heads=heads,
        kv_heads=kv_heads,
        margin=margin,
        slots=tuple(slots),
        blocks=blocks,
        chip_outputs=chip_outputs,
    )
    if chip_outputs:
        piece_types = [jnp.bfloat16, jnp.bfloat16, jnp.float32, jnp.float32]
    else:
        piece_types = [jnp.float32] * len(slots)
    vmem = pl.BlockSpec(memory_space=pltpu.VMEM)
    smem = pl.BlockSpec(memory_space=pltpu.SMEM)
    flops = 2 * 5 * heads * rows * keys * HEAD_DIM
    moved = 2 * (2 * rows * width + keys * kv_cols + rows * width) + 4 * keys * kv_cols
    return pl.pallas_call(
        kernel,
        out_shape=(jax.ShapeDtypeStruct((rows, width), jnp.bfloat16),)
        + tuple(jax.ShapeDtypeStruct((block_rows, kv_cols), kind) for kind in piece_types),
        in_specs=[smem] + [vmem] * (3 + blocks) + [pl.BlockSpec(memory_space=pl.ANY)] * len(early),
        out_specs=(vmem,) * (1 + len(slots)),
        scratch_shapes=[
            pltpu.VMEM((keys, kv_cols), kv_blocks[0].dtype),
            pltpu.VMEM((keys, kv_cols), jnp.float32),
        ],
        cost_estimate=pl.CostEstimate(
            flops=flops, transcendentals=heads * rows * keys, bytes_accessed=moved
        ),
    )(flag, lo_rel, queries, grads, *kv_blocks, *early)


def body(layer_input, query_heads, key_heads, value_heads, grad_out, doc_starts):
    block_rows = query_heads.shape[1]
    window = min(SPAN, lax.axis_size(RING) * block_rows // 2)
    reach = (window + block_rows - 2) // block_rows
    margin = reach * block_rows
    kv_width = key_heads.shape[2]
    heads = query_heads.shape[2] // HEAD_DIM
    kv_heads = kv_width // HEAD_DIM
    first_row = lax.axis_index(RING) * block_rows

    fsdp_count = lax.axis_size("fsdp")
    fsdp_at = lax.axis_index("fsdp")
    model_width = layer_input.shape[2]
    shard_rows = model_width // fsdp_count
    own_input = layer_input[0]
    inputs = [lax.dynamic_slice_in_dim(own_input, fsdp_at * shard_rows, shard_rows, axis=1)]
    for steps in range(1, fsdp_count):
        target = (fsdp_at + steps) % fsdp_count
        outgoing = lax.dynamic_slice_in_dim(own_input, target * shard_rows, shard_rows, axis=1)
        inputs.append(rotated(outgoing, "fsdp", steps))

    own_kv = jnp.concatenate([key_heads[0], value_heads[0]], axis=1)
    query_pos = first_row + jnp.arange(block_rows, dtype=jnp.int32)
    lowest = jnp.maximum(doc_start_of(doc_starts[0], query_pos), query_pos - window + 1)
    lo_rel = (lowest - first_row + margin).astype(jnp.int32)[:, None]
    sub_count = lax.axis_size("sub")
    sub_at = lax.axis_index("sub")
    flag = jnp.reshape(sub_at, (1,)).astype(jnp.int32)
    chip_route = sub_count == 2 and reach == 3
    if chip_route:
        ring_count = lax.axis_size(RING)
        across = [(2 * chip - 3, 2 * chip) for chip in range(2, ring_count // 2)]
        two_back = passed_along(own_kv, "ctx", 1)
        one_back_high = passed_along(own_kv, "sub", 1)
        three_back_low = lax.ppermute(own_kv, RING, across)
        swapped = rotated(two_back, "sub", 1)
        kv_blocks = [two_back, one_back_high, three_back_low, swapped, own_kv]
        slots = [(2, 3), (0, 0), (3, 1), (4, 4)]
    else:
        arrived = []
        moving = own_kv
        for _ in range(reach):
            moving = passed_along(moving, RING, 1)
            arrived.append(moving)
        kv_blocks = arrived[::-1] + [own_kv]
        slots = [(index, index) for index in range(reach + 1)]
    grad_q, *grad_pieces = attention(
        flag, lo_rel, query_heads[0], grad_out[0], kv_blocks, slots, heads, kv_heads, margin,
        inputs[1:],
        chip_route,
    )

    def low(value):
        return value.astype(jnp.bfloat16)

    if chip_route:
        back = [(target, source) for source, target in across]
        to_mate, to_other, g2, g0 = grad_pieces
        from_far = lax.ppermute(to_other, RING, back).astype(jnp.float32)
        from_mate = rotated(to_mate, "sub", 1).astype(jnp.float32)
        from_high = passed_along(to_other, "sub", -1).astype(jnp.float32)
        two_back_sum = g2 + from_mate
        from_next = passed_along(low(two_back_sum), "ctx", -1).astype(jnp.float32)
        total = g0 + from_high + from_far + from_next
    else:

        def own_piece(distance):
            return grad_pieces[reach - distance]

        total = own_piece(reach)
        for distance in range(reach - 1, -1, -1):
            moved = passed_along(low(total), RING, -1).astype(jnp.float32)
            total = moved + own_piece(distance)
    grad_kv = total.astype(jnp.bfloat16)
    grad_key = grad_kv[:, :kv_width]
    grad_value = grad_kv[:, kv_width:]

    values = [grad_value]
    for steps in range(1, fsdp_count):
        values.append(rotated(grad_value, "fsdp", steps))
    stacked_inputs = jnp.concatenate(inputs, axis=0)
    stacked_values = jnp.concatenate(values, axis=0)
    shard = lax.dot_general(stacked_inputs, stacked_values, TN, preferred_element_type=jnp.float32)
    token_scale = float(fsdp_count * lax.axis_size(RING) * block_rows) ** (-0.5)
    scale_early = token_scale == 2.0 ** round(math.log2(token_scale))
    if scale_early:
        shard = shard * token_scale

    sub_count = lax.axis_size("sub")
    sub_at = lax.axis_index("sub")
    piece_rows = shard_rows // sub_count
    mine = lax.dynamic_slice_in_dim(shard, sub_at * piece_rows, piece_rows, axis=0)
    for steps in range(1, sub_count):
        target = (sub_at + steps) % sub_count
        outgoing = lax.dynamic_slice_in_dim(shard, target * piece_rows, piece_rows, axis=0)
        mine = mine + rotated(outgoing.astype(jnp.bfloat16), "sub", steps).astype(jnp.float32)
    reduced = ring_sum(mine, "ctx")
    if sub_count == 2:
        other = rotated(reduced, "sub", 1)
        first = jnp.where(sub_at == 0, reduced, other)
        second = jnp.where(sub_at == 0, other, reduced)
        weight_v = jnp.concatenate([first, second], axis=0).astype(jnp.float32)
    else:
        weight_v = lax.all_gather(reduced, "sub", axis=0, tiled=True).astype(jnp.float32)
    if not scale_early:
        weight_v = weight_v * token_scale
    return (
        grad_q[None],
        grad_key[None],
        grad_value[None],
        weight_v,
    )


def solution(mesh):
    placed = (
        P(("groups", "fsdp"), ("ctx", "sub"), None),
        P(("groups", "fsdp"), ("ctx", "sub"), None),
        P(("groups", "fsdp"), ("ctx", "sub"), None),
        P(("groups", "fsdp"), ("ctx", "sub"), None),
        P(("groups", "fsdp"), ("ctx", "sub"), None),
        P(("groups", "fsdp"), None),
    )
    return jax.shard_map(
        body,
        mesh=mesh,
        in_specs=placed,
        out_specs=(
            P(("groups", "fsdp"), ("ctx", "sub"), None),
            P(("groups", "fsdp"), ("ctx", "sub"), None),
            P(("groups", "fsdp"), ("ctx", "sub"), None),
            P(("groups", "fsdp"), None),
        ),
        check_vma=False,
    )
```
